256 devices in a mesh: dom: 128 (over x, z, y), head: 2 (over core).
Axes of the slice: x: 4, y: 4, z: 8, core: 2. Of those that a mesh axis runs over, the one named last changes fastest.
Arguments:
- query_rows: bfloat16 [32768, 512], P('dom', 'head'), may hold values from -70 to 70
- key_rows: bfloat16 [32768, 512], P('dom', 'head'), may hold values from -4 to 4
- value_rows: bfloat16 [32768, 512], P('dom', 'head'), may hold values from -6 to 6
- out_weight: bfloat16 [512, 512], P('head'), may hold values from -0.25 to 0.25
- out_grad: bfloat16 [32768, 512], P('dom', 'head'), may hold values from -24 to 24
- far_bias: float32 [8], P('head'), may hold values from 4 to 7
- tile_list: int32 [256, 4], P('dom'), may hold values from 0 to 255, as said below
- tile_count: int32 [256], P('dom'), may hold values from 1 to 4, as said below
- send_rows: int32 [128, 128, 8], P('dom'), may hold values from 0 to 255
- expander_slot: int32 [32768, 3], P('dom'), may hold values from 0 to 1023, as said below
Outputs:
- layer_out: bfloat16 [32768, 512], P('dom', 'head')
- query_grad: bfloat16 [32768, 512], P('dom', 'head')
- key_grad: bfloat16 [32768, 512], P('dom', 'head')
- value_grad: bfloat16 [32768, 512], P('dom', 'head')
- out_weight_grad: float32 [512, 512], P('dom', 'head')
The draws below stay inside these ranges and needn't reach their ends.
Inputs may be any that keep to these rules, and one draw needn't show every extreme that they name: `tile_list`: row t begins with t itself; its first tile_count[t] entries are distinct tiles from the 2 last tiles of the previous partition, the 2 tiles of t's own partition and the 2 first tiles of the next partition (partition = block of 2 tiles); later entries equal t. `tile_count`: every partition of 2 tiles has a tile with 4. `expander_slot`: A value names source partition value // 8 and slot value % 8 of send_rows[source, partition of the node].
All inputs are finite; a program needn't handle non-finite values.
Results may differ from the reference program's by a relative error of at most 0.011.
Values may be sent and summed in bfloat16 or wider, within the bound.
No kernel may reach another device: no remote copies, remote signals or barrier semaphores. Data moves between devices by JAX's collectives and lax.ppermute only.
A program may use at most 64 MiB of HBM per device.

```python
import jax
import jax.numpy as jnp
from jax import lax

D = 512
HEADS = 8
TILE = 128
NODE_DEV = 256
KT = 4
HALO = 2
DEG = 3
NODES = 32768
TILES = 256
TPD = 2
CAP = 8
N_DOM = 128


def query_key_pair(seed_key):
    base_key = jax.random.fold_in(seed_key, 7)
    query_key, keys_key = jax.random.split(base_key, 2)
    shape_pair = (NODES, D)
    query_draw = jnp.clip(jax.random.normal(query_key, shape_pair, jnp.float32), -4.0, 4.0)
    key_draw = jnp.clip(jax.random.normal(keys_key, shape_pair, jnp.float32), -4.0, 4.0)
    return (query_draw, key_draw)


def draw_query_rows(key, part):
    return query_key_pair(key)[0].astype(jnp.bfloat16)


def draw_key_rows(key, part):
    return query_key_pair(key)[1].astype(jnp.bfloat16)


def tile_plan(seed_key):
    base_key = jax.random.fold_in(seed_key, 3)
    pick_key, low_key, spread_key, force_key = jax.random.split(base_key, 4)
    cand_width = TPD + 2 * HALO
    tile_index = jnp.arange(TILES, dtype=jnp.int32)
    owner = tile_index // TPD
    offsets = jnp.arange(cand_width, dtype=jnp.int32)
    candidate = owner[:, None] * TPD - HALO + offsets[None, :]
    usable = (candidate >= 0) & (candidate < TILES)
    scores = jax.random.randint(pick_key, (TILES, cand_width), 0, 2 ** 16) * 64 + offsets[None, :]
    scores = jnp.where(candidate == tile_index[:, None], 2 ** 30, jnp.where(usable, scores, -1))
    top_scores, picked = lax.top_k(scores, KT)
    chosen = jnp.take_along_axis(candidate, picked, axis=1)
    lowest = jax.random.randint(low_key, (N_DOM,), 1, KT + 1)[owner]
    extra = jax.random.randint(spread_key, (TILES,), 0, 2 ** 20) % (KT + 1 - lowest)
    counts = lowest + extra
    forced = jax.random.randint(force_key, (N_DOM,), 0, TPD)[owner]
    counts = jnp.where(tile_index % TPD == forced, KT, counts)
    slot_index = jnp.arange(KT, dtype=jnp.int32)
    lists = jnp.where(slot_index[None, :] < counts[:, None], chosen, tile_index[:, None])
    return (lists.astype(jnp.int32), counts.astype(jnp.int32))


def draw_tile_list(key, part):
    return tile_plan(key)[0]


def draw_tile_count(key, part):
    return tile_plan(key)[1]


def far_plan(seed_key):
    base_key = jax.random.fold_in(seed_key, 5)
    count_key, perm_key, row_key, source_key, place_key = jax.random.split(base_key, 5)
    lowest = max(1, CAP // 4)
    counts = jax.random.randint(count_key, (N_DOM, N_DOM), lowest, CAP + 1)
    order = jax.random.permutation(perm_key, N_DOM)
    targets = jnp.arange(N_DOM, dtype=jnp.int32)
    counts = counts.at[order, targets].set(CAP)
    sending = jax.random.randint(row_key, (N_DOM, N_DOM, CAP), 0, NODE_DEV)
    sending = sending.at[0, 0, 0].set(NODE_DEV - 1).at[0, 0, 1].set(0)
    node_index = jnp.arange(NODES, dtype=jnp.int32)
    dest_part = node_index // NODE_DEV
    sources = jax.random.randint(source_key, (NODES, DEG), 0, N_DOM)
    places = jax.random.randint(place_key, (NODES, DEG), 0, 2 ** 20) % counts[sources, dest_part[:, None]]
    slots = sources * CAP + places
    leading = (node_index % NODE_DEV == 0)[:, None]
    edge_index = jnp.arange(DEG, dtype=jnp.int32)[None, :]
    anchor = (order[dest_part] * CAP)[:, None]
    slots = jnp.where(leading & (edge_index == 0), anchor + CAP - 1, slots)
    slots = jnp.where(leading & (edge_index == 1), anchor, slots)
    return (sending.astype(jnp.int32), slots.astype(jnp.int32))


def draw_send_rows(key, part):
    return far_plan(key)[0]


def draw_expander_slot(key, part):
    return far_plan(key)[1]


def spiked(drawn, key, source, target, shards_of, factor):
    def block_of(position):
        return (jnp.arange(drawn.shape[position]) // (drawn.shape[position] // shards_of)).reshape((-1,) + (1,) * (drawn.ndim - 1 - position))

    first = jax.random.permutation(key, shards_of)[block_of(target)]
    other_side = (block_of(target) + shards_of // 2) % shards_of
    return jnp.where((block_of(source) == first) | (block_of(source) == other_side), factor * drawn, drawn)


def level_of(own_key, extent, cuts, smallest, high):
    factor_of = 1.0
    for axis_at, shards_of in cuts:
        draws = jax.random.uniform(jax.random.fold_in(jax.random.fold_in(own_key, 6), axis_at), (shards_of,), jnp.float32, smallest / len(cuts), high / len(cuts))
        factor_of = factor_of * jnp.repeat(jnp.exp(draws), extent[axis_at] // shards_of).reshape((-1,) + (1,) * (len(extent) - 1 - axis_at))
    return factor_of


def noise(stream_key, shape, scale, reach, cuts=(), held_as=jnp.bfloat16):
    result = scale * jax.random.normal(stream_key, shape, jnp.float32)
    if cuts:
        result = result * level_of(stream_key, shape, cuts, -0.22, 0.18)
    return jnp.clip(result, -reach, reach).astype(held_as)


def noise_with(key, extent, scale, reach, pieces, heavy, held_as=jnp.bfloat16):
    values = scale * jax.random.normal(key, extent, jnp.float32)
    if pieces:
        values = values * level_of(key, extent, pieces, -0.22, 0.18)
    return jnp.clip(spiked(values, jax.random.fold_in(key, 3), *heavy), -reach, reach).astype(held_as)


def setup_inputs(seed: int = 0) -> dict:
    splits = jax.random.split(jax.random.key(seed), 11)
    query_rows = draw_query_rows(jax.random.fold_in(splits[10], 71), 0)
    key_rows = draw_key_rows(jax.random.fold_in(splits[10], 71), 0)
    value_rows = noise(splits[2], (NODES, D), 1.0, 6.0, ((0, 128), (1, 2)))
    out_weight = noise(splits[3], (D, D), D ** -0.5, 0.25, ((0, 2),))
    out_grad = noise_with(splits[4], (NODES, D), 1.0, 24.0, ((0, 128), (1, 2)), (0, 1, 128, 5.5))
    far_bias = jnp.clip(4.0 + 3.0 * jax.random.uniform(splits[5], (HEADS,), jnp.float32) ** level_of(splits[5], (HEADS,), ((0, 2),), -0.2, 0.2), 4.0, 7.0)
    tile_list = draw_tile_list(jax.random.fold_in(splits[10], 71), 0)
    tile_count = draw_tile_count(jax.random.fold_in(splits[10], 71), 0)
    send_rows = draw_send_rows(jax.random.fold_in(splits[10], 71), 0)
    expander_slot = draw_expander_slot(jax.random.fold_in(splits[10], 71), 0)
    return dict(query_rows=query_rows, key_rows=key_rows, value_rows=value_rows, out_weight=out_weight, out_grad=out_grad, far_bias=far_bias, tile_list=tile_list, tile_count=tile_count, send_rows=send_rows, expander_slot=expander_slot)


def rounded(values):
    return lax.optimization_barrier(values.astype(jnp.bfloat16)).astype(jnp.float32)


def reference(query_rows, key_rows, value_rows, out_weight, out_grad, far_bias, tile_list, tile_count, send_rows, expander_slot):
    head_size = D // HEADS
    score_scale = head_size ** -0.5
    node_index = jnp.arange(NODES, dtype=jnp.int32)
    dest_part = node_index // NODE_DEV
    source_part = (expander_slot // CAP).astype(jnp.int32)
    far_index = source_part * NODE_DEV + send_rows[source_part, dest_part[:, None], expander_slot % CAP]
    attn_grad = jnp.dot(out_grad, out_weight.T, preferred_element_type=jnp.float32).astype(jnp.bfloat16)
    tile_lanes = jnp.arange(TILE, dtype=jnp.int32)
    slot_index = jnp.arange(KT, dtype=jnp.int32)

    def advance(accum, tile):
        key_acc, value_acc = accum
        first_row = (tile * TILE).astype(jnp.int32)
        queries = lax.dynamic_slice_in_dim(query_rows, first_row, TILE, 0).astype(jnp.float32).reshape(TILE, HEADS, head_size)
        upstream = lax.dynamic_slice_in_dim(attn_grad, first_row, TILE, 0).astype(jnp.float32).reshape(TILE, HEADS, head_size)
        near_rows = (tile_list[tile][:, None] * TILE + tile_lanes[None, :]).reshape(-1).astype(jnp.int32)
        live_keys = jnp.repeat(slot_index < tile_count[tile], TILE)
        near_keys = key_rows[near_rows].astype(jnp.float32).reshape(-1, HEADS, head_size)
        near_values = value_rows[near_rows].astype(jnp.float32).reshape(-1, HEADS, head_size)
        far_rows = lax.dynamic_slice_in_dim(far_index, first_row, TILE, 0).astype(jnp.int32)
        far_keys = key_rows[far_rows].astype(jnp.float32).reshape(TILE, DEG, HEADS, head_size)
        far_values = value_rows[far_rows].astype(jnp.float32).reshape(TILE, DEG, HEADS, head_size)
        near_score = jnp.einsum("qhd,khd->hqk", queries, near_keys) * score_scale
        far_score = jnp.einsum("qhd,qehd->hqe", queries, far_keys) * score_scale + far_bias[:, None, None]
        row_max = jnp.maximum(jnp.max(jnp.where(live_keys, near_score, -jnp.inf), axis=2), jnp.max(far_score, axis=2))
        near_exp = jnp.where(live_keys, jnp.exp(near_score - row_max[:, :, None]), 0.0)
        far_exp = jnp.exp(far_score - row_max[:, :, None])
        row_sum = jnp.sum(near_exp, axis=2) + jnp.sum(far_exp, axis=2)
        mixed = jnp.einsum("hqk,khd->qhd", rounded(near_exp), near_values) + jnp.einsum("hqe,qehd->qhd", rounded(far_exp), far_values)
        attention = rounded(mixed / row_sum.T[:, :, None])
        delta_term = jnp.sum(upstream * attention, axis=2).T
        near_dprob = jnp.einsum("qhd,khd->hqk", upstream, near_values)
        far_dprob = jnp.einsum("qhd,qehd->hqe", upstream, far_values)
        near_prob = near_exp / row_sum[:, :, None]
        far_prob = far_exp / row_sum[:, :, None]
        near_dscore = rounded(near_prob * (near_dprob - delta_term[:, :, None]))
        far_dscore = rounded(far_prob * (far_dprob - delta_term[:, :, None]))
        query_grad = (jnp.einsum("hqk,khd->qhd", near_dscore, near_keys) + jnp.einsum("hqe,qehd->qhd", far_dscore, far_keys)) * score_scale
        near_kgrad = jnp.einsum("hqk,qhd->khd", near_dscore, queries) * score_scale
        near_vgrad = jnp.einsum("hqk,qhd->khd", rounded(near_prob), upstream)
        far_kgrad = jnp.einsum("hqe,qhd->qehd", far_dscore, queries) * score_scale
        far_vgrad = jnp.einsum("hqe,qhd->qehd", rounded(far_prob), upstream)
        flat_far = far_rows.reshape(-1)
        key_acc = key_acc.at[near_rows].add(near_kgrad.reshape(-1, D)).at[flat_far].add(far_kgrad.reshape(-1, D))
        value_acc = value_acc.at[near_rows].add(near_vgrad.reshape(-1, D)).at[flat_far].add(far_vgrad.reshape(-1, D))
        return (key_acc, value_acc), (attention.astype(jnp.bfloat16).reshape(TILE, D), query_grad.astype(jnp.bfloat16).reshape(TILE, D))

    zero_rows = jnp.zeros((NODES, D), jnp.float32)
    (key_acc, value_acc), (attn_tiles, qgrad_tiles) = lax.scan(advance, (zero_rows, zero_rows), jnp.arange(TILES, dtype=jnp.int32))
    attention_all = attn_tiles.reshape(NODES, D)
    layer_out = jnp.dot(attention_all, out_weight, preferred_element_type=jnp.float32).astype(jnp.bfloat16)
    out_weight_grad = jnp.dot(out_grad.T, attention_all, preferred_element_type=jnp.float32)
    return (layer_out, qgrad_tiles.reshape(NODES, D), key_acc.astype(jnp.bfloat16), value_acc.astype(jnp.bfloat16), out_weight_grad)
```

```python
import math

import jax
import jax.numpy as jnp
from jax import lax
from jax.sharding import PartitionSpec as P

TILE = 128
HALO = 2
DEG = 3


def extended_2(value, sides, width):
    for axis, dim in sides:
        peers, length = (lax.axis_size(axis), value.shape[dim])
        up = [(i, (i + 1) % peers) for i in range(peers - 1)]
        down = [(j, i) for i, j in up]
        last = lax.slice_in_dim(value, length - width, length, axis=dim)
        leading = lax.slice_in_dim(value, 0, width, axis=dim)
        before = lax.ppermute(last, axis, up)
        after = lax.ppermute(leading, axis, down)
        value = jnp.concatenate([before, value, after], axis=dim)
    return value


def from_behind(value, axis, steps):
    count = lax.axis_size(axis)
    leading, last = (max(0, -steps), min(count, count - steps))
    return lax.ppermute(value, axis, [(source, source + steps) for source in range(leading, last)])


def rounded(values):
    return lax.optimization_barrier(values.astype(jnp.bfloat16)).astype(jnp.float32)


def tile_work(query_tile, grad_tile, tile_ids, live_count, far_tile, ext_tiles, bias, base_tile):
    col_width = query_tile.shape[1]
    heads_here = bias.shape[0]
    head_size = col_width // heads_here
    score_scale = head_size ** (-0.5)
    key_block = ext_tiles[tile_ids - base_tile].reshape(-1, 2 * col_width)
    near_keys = key_block[:, :col_width].reshape(-1, heads_here, head_size)
    near_values = key_block[:, col_width:].reshape(-1, heads_here, head_size)
    far_keys = far_tile[:, :, :col_width].reshape(TILE, -1, heads_here, head_size)
    far_values = far_tile[:, :, col_width:].reshape(TILE, -1, heads_here, head_size)
    queries = query_tile.reshape(TILE, heads_here, head_size)
    upstream = grad_tile.reshape(TILE, heads_here, head_size)
    live_keys = jnp.repeat(jnp.arange(tile_ids.shape[0]) < live_count, TILE)
    near_score = (
        jnp.einsum("qhd,khd->hqk", queries, near_keys, preferred_element_type=jnp.float32)
        * score_scale
    )
    far_score = (
        jnp.einsum("qhd,qehd->hqe", queries, far_keys, preferred_element_type=jnp.float32)
        * score_scale
        + bias[:, None, None]
    )
    row_max = jnp.maximum(
        jnp.max(jnp.where(live_keys, near_score, -jnp.inf), axis=2), jnp.max(far_score, axis=2)
    )
    near_exp = jnp.where(live_keys, jnp.exp(near_score - row_max[:, :, None]), 0.0)
    far_exp = jnp.exp(far_score - row_max[:, :, None])
    row_sum = jnp.sum(near_exp, axis=2) + jnp.sum(far_exp, axis=2)
    mixed = jnp.einsum(
        "hqk,khd->qhd",
        near_exp.astype(jnp.bfloat16),
        near_values,
        preferred_element_type=jnp.float32,
    )
    mixed = mixed + jnp.einsum(
        "hqe,qehd->qhd",
        far_exp.astype(jnp.bfloat16),
        far_values,
        preferred_element_type=jnp.float32,
    )
    attention = (mixed / row_sum.T[:, :, None]).astype(jnp.bfloat16)
    delta_term = jnp.sum(
        upstream.astype(jnp.float32) * rounded(mixed / row_sum.T[:, :, None]), axis=2
    ).T
    near_dprob = jnp.einsum(
        "qhd,khd->hqk", upstream, near_values, preferred_element_type=jnp.float32
    )
    far_dprob = jnp.einsum(
        "qhd,qehd->hqe", upstream, far_values, preferred_element_type=jnp.float32
    )
    near_prob = near_exp / row_sum[:, :, None]
    far_prob = far_exp / row_sum[:, :, None]
    near_dscore = (near_prob * (near_dprob - delta_term[:, :, None])).astype(jnp.bfloat16)
    far_dscore = (far_prob * (far_dprob - delta_term[:, :, None])).astype(jnp.bfloat16)
    query_grad = jnp.einsum(
        "hqk,khd->qhd", near_dscore, near_keys, preferred_element_type=jnp.float32
    )
    query_grad = (
        query_grad
        + jnp.einsum("hqe,qehd->qhd", far_dscore, far_keys, preferred_element_type=jnp.float32)
    ) * score_scale
    near_kgrad = (
        jnp.einsum("hqk,qhd->khd", near_dscore, queries, preferred_element_type=jnp.float32)
        * score_scale
    )
    near_vgrad = jnp.einsum(
        "hqk,qhd->khd", near_prob.astype(jnp.bfloat16), upstream, preferred_element_type=jnp.float32
    )
    far_kgrad = (
        jnp.einsum("hqe,qhd->qehd", far_dscore, queries, preferred_element_type=jnp.float32)
        * score_scale
    )
    far_vgrad = jnp.einsum(
        "hqe,qhd->qehd", far_prob.astype(jnp.bfloat16), upstream, preferred_element_type=jnp.float32
    )
    near_grad = jnp.concatenate(
        [near_kgrad.reshape(-1, col_width), near_vgrad.reshape(-1, col_width)], axis=1
    )
    far_grad = jnp.concatenate(
        [far_kgrad.reshape(TILE, -1, col_width), far_vgrad.reshape(TILE, -1, col_width)], axis=2
    )
    return (
        attention.reshape(TILE, col_width),
        query_grad.astype(jnp.bfloat16).reshape(TILE, col_width),
        near_grad,
        far_grad,
    )


def shards(
    query_rows,
    key_rows,
    value_rows,
    out_weight,
    out_grad,
    far_bias,
    tile_list,
    tile_count,
    send_rows,
    expander_slot,
):
    col_width = query_rows.shape[1]
    node_count = query_rows.shape[0]
    per_part = node_count // TILE
    dom_index = lax.axis_index("dom")
    full_grad = lax.all_gather(out_grad, "head", axis=1, tiled=True)
    attn_grad = lax.dot_general(
        full_grad, out_weight, (((1,), (1,)), ((), ())), preferred_element_type=jnp.float32
    ).astype(jnp.bfloat16)
    stacked = jnp.concatenate([key_rows, value_rows], axis=1)
    rim_rows = HALO * TILE
    extended = extended_2(stacked, (("dom", 0),), rim_rows)
    ext_tiles = extended.reshape(-1, TILE, 2 * col_width)
    outgoing = stacked[send_rows[0]]
    received = lax.all_to_all(outgoing, "dom", split_axis=0, concat_axis=0, tiled=True)
    far_all = received.reshape(-1, 2 * col_width)[expander_slot]
    group = math.gcd(4, per_part)
    rounds = per_part // group
    base_tile = dom_index * per_part - HALO
    tile_lanes = jnp.arange(TILE, dtype=jnp.int32)
    batched = jax.vmap(tile_work, in_axes=(0, 0, 0, 0, 0, None, None, None))

    def advance(accum, inputs):
        query_group, grad_group, list_group, count_group, far_group = inputs
        attn_group, qgrad_group, near_group, fgrad_group = batched(
            query_group,
            grad_group,
            list_group,
            count_group,
            far_group,
            ext_tiles,
            far_bias,
            base_tile,
        )
        targets = ((list_group - base_tile)[:, :, None] * TILE + tile_lanes).reshape(-1)
        accum = accum.at[targets].add(near_group.reshape(-1, 2 * col_width))
        return (accum, (attn_group, qgrad_group, fgrad_group))

    inputs = (
        query_rows.reshape(rounds, group, TILE, col_width),
        attn_grad.reshape(rounds, group, TILE, col_width),
        tile_list.reshape(rounds, group, -1),
        tile_count.reshape(rounds, group),
        far_all.reshape(rounds, group, TILE, DEG, 2 * col_width),
    )
    start_grad = jnp.zeros((extended.shape[0], 2 * col_width), jnp.float32)
    ext_grad, (attn_all, qgrad_all, far_grad) = lax.scan(advance, start_grad, inputs)
    attn_mine = attn_all.reshape(node_count, col_width)
    low_part = ext_grad[:rim_rows]
    high_part = ext_grad[rim_rows + node_count :]
    own_grad = ext_grad[rim_rows : rim_rows + node_count]
    from_next = from_behind(low_part.astype(jnp.bfloat16), "dom", -1).astype(low_part.dtype)
    from_prev = from_behind(high_part.astype(jnp.bfloat16), "dom", 1).astype(high_part.dtype)
    own_grad = own_grad.at[:rim_rows].add(from_prev).at[node_count - rim_rows :].add(from_next)
    slot_grad = jnp.zeros((received.shape[0] * received.shape[1], 2 * col_width), jnp.float32)
    slot_grad = slot_grad.at[expander_slot.reshape(-1)].add(far_grad.reshape(-1, 2 * col_width))
    n_dom = received.shape[0]
    weight_part = lax.dot_general(
        full_grad, attn_mine, (((0,), (0,)), ((), ())), preferred_element_type=jnp.float32
    ).reshape(n_dom, -1, 2 * col_width)
    weight_rows = weight_part.shape[1]
    both = jnp.concatenate(
        [slot_grad.reshape(n_dom, received.shape[1], -1), weight_part], axis=1
    )
    both_back = lax.all_to_all(both, "dom", split_axis=0, concat_axis=0, tiled=True)
    returned = both_back[:, : received.shape[1]]
    weight_sum = jnp.sum(both_back[:, received.shape[1] :], axis=0)
    own_grad = own_grad.at[send_rows[0].reshape(-1)].add(returned.reshape(-1, 2 * col_width))
    key_grad = own_grad[:, :col_width].astype(jnp.bfloat16)
    value_grad = own_grad[:, col_width:].astype(jnp.bfloat16)
    partial_out = jnp.dot(attn_mine, out_weight, preferred_element_type=jnp.float32)
    layer_out = lax.psum_scatter(partial_out, "head", scatter_dimension=1, tiled=True).astype(
        jnp.bfloat16
    )
    out_weight_grad = weight_sum.reshape(-1, col_width)
    return (
        layer_out,
        qgrad_all.reshape(node_count, col_width),
        key_grad,
        value_grad,
        out_weight_grad,
    )


def solution(mesh):
    in_specs = (
        P("dom", "head"),
        P("dom", "head"),
        P("dom", "head"),
        P("head", None),
        P("dom", "head"),
        P("head"),
        P("dom", None),
        P("dom"),
        P("dom", None, None),
        P("dom", None),
    )
    out_specs = (
        P("dom", "head"),
        P("dom", "head"),
        P("dom", "head"),
        P("dom", "head"),
        P("dom", "head"),
    )
    return jax.shard_map(shards, mesh=mesh, in_specs=in_specs, out_specs=out_specs, check_vma=False)
```

```python
import math

import jax
import jax.numpy as jnp
from jax import lax
from jax.sharding import PartitionSpec as P

TILE = 128
HALO = 2
DEG = 3


def extended_2(value, sides, width):
    for axis, dim in sides:
        peers, length = (lax.axis_size(axis), value.shape[dim])
        up = [(i, (i + 1) % peers) for i in range(peers - 1)]
        down = [(j, i) for i, j in up]
        last = lax.slice_in_dim(value, length - width, length, axis=dim)
        leading = lax.slice_in_dim(value, 0, width, axis=dim)
        before = lax.ppermute(last, axis, up)
        after = lax.ppermute(leading, axis, down)
        value = jnp.concatenate([before, value, after], axis=dim)
    return value


def from_behind(value, axis, steps):
    count = lax.axis_size(axis)
    leading, last = (max(0, -steps), min(count, count - steps))
    return lax.ppermute(value, axis, [(source, source + steps) for source in range(leading, last)])


def rounded(values):
    return lax.optimization_barrier(values.astype(jnp.bfloat16)).astype(jnp.float32)


def tile_work(query_tile, grad_tile, tile_ids, live_count, far_tile, ext_tiles, bias, base_tile):
    col_width = query_tile.shape[1]
    heads_here = bias.shape[0]
    head_size = col_width // heads_here
    score_scale = head_size ** (-0.5)
    key_block = ext_tiles[tile_ids - base_tile].reshape(-1, 2 * col_width)
    near_keys = key_block[:, :col_width].reshape(-1, heads_here, head_size)
    near_values = key_block[:, col_width:].reshape(-1, heads_here, head_size)
    far_keys = far_tile[:, :, :col_width].reshape(TILE, -1, heads_here, head_size)
    far_values = far_tile[:, :, col_width:].reshape(TILE, -1, heads_here, head_size)
    queries = query_tile.reshape(TILE, heads_here, head_size)
    upstream = grad_tile.reshape(TILE, heads_here, head_size)
    live_keys = jnp.repeat(jnp.arange(tile_ids.shape[0]) < live_count, TILE)
    near_score = (
        jnp.einsum("qhd,khd->hqk", queries, near_keys, preferred_element_type=jnp.float32)
        * score_scale
    )
    far_score = (
        jnp.einsum("qhd,qehd->hqe", queries, far_keys, preferred_element_type=jnp.float32)
        * score_scale
        + bias[:, None, None]
    )
    row_max = jnp.maximum(
        jnp.max(jnp.where(live_keys, near_score, -jnp.inf), axis=2), jnp.max(far_score, axis=2)
    )
    near_exp = jnp.where(live_keys, jnp.exp(near_score - row_max[:, :, None]), 0.0)
    far_exp = jnp.exp(far_score - row_max[:, :, None])
    row_sum = jnp.sum(near_exp, axis=2) + jnp.sum(far_exp, axis=2)
    mixed = jnp.einsum(
        "hqk,khd->qhd",
        near_exp.astype(jnp.bfloat16),
        near_values,
        preferred_element_type=jnp.float32,
    )
    mixed = mixed + jnp.einsum(
        "hqe,qehd->qhd",
        far_exp.astype(jnp.bfloat16),
        far_values,
        preferred_element_type=jnp.float32,
    )
    attention = (mixed / row_sum.T[:, :, None]).astype(jnp.bfloat16)
    delta_term = jnp.sum(
        upstream.astype(jnp.float32) * rounded(mixed / row_sum.T[:, :, None]), axis=2
    ).T
    near_dprob = jnp.einsum(
        "qhd,khd->hqk", upstream, near_values, preferred_element_type=jnp.float32
    )
    far_dprob = jnp.einsum(
        "qhd,qehd->hqe", upstream, far_values, preferred_element_type=jnp.float32
    )
    near_prob = near_exp / row_sum[:, :, None]
    far_prob = far_exp / row_sum[:, :, None]
    near_dscore = (near_prob * (near_dprob - delta_term[:, :, None])).astype(jnp.bfloat16)
    far_dscore = (far_prob * (far_dprob - delta_term[:, :, None])).astype(jnp.bfloat16)
    query_grad = jnp.einsum(
        "hqk,khd->qhd", near_dscore, near_keys, preferred_element_type=jnp.float32
    )
    query_grad = (
        query_grad
        + jnp.einsum("hqe,qehd->qhd", far_dscore, far_keys, preferred_element_type=jnp.float32)
    ) * score_scale
    near_kgrad = (
        jnp.einsum("hqk,qhd->khd", near_dscore, queries, preferred_element_type=jnp.float32)
        * score_scale
    )
    near_vgrad = jnp.einsum(
        "hqk,qhd->khd", near_prob.astype(jnp.bfloat16), upstream, preferred_element_type=jnp.float32
    )
    far_kgrad = (
        jnp.einsum("hqe,qhd->qehd", far_dscore, queries, preferred_element_type=jnp.float32)
        * score_scale
    )
    far_vgrad = jnp.einsum(
        "hqe,qhd->qehd", far_prob.astype(jnp.bfloat16), upstream, preferred_element_type=jnp.float32
    )
    near_grad = jnp.concatenate(
        [near_kgrad.reshape(-1, col_width), near_vgrad.reshape(-1, col_width)], axis=1
    )
    far_grad = jnp.concatenate(
        [far_kgrad.reshape(TILE, -1, col_width), far_vgrad.reshape(TILE, -1, col_width)], axis=2
    )
    return (
        attention.reshape(TILE, col_width),
        query_grad.astype(jnp.bfloat16).reshape(TILE, col_width),
        near_grad,
        far_grad,
    )


def shards(
    query_rows,
    key_rows,
    value_rows,
    out_weight,
    out_grad,
    far_bias,
    tile_list,
    tile_count,
    send_rows,
    expander_slot,
):
    col_width = query_rows.shape[1]
    node_count = query_rows.shape[0]
    per_part = node_count // TILE
    dom_index = lax.axis_index("dom")
    full_grad = lax.all_gather(out_grad, "head", axis=1, tiled=True)
    attn_grad = lax.dot_general(
        full_grad, out_weight, (((1,), (1,)), ((), ())), preferred_element_type=jnp.float32
    ).astype(jnp.bfloat16)
    stacked = jnp.concatenate([key_rows, value_rows], axis=1)
    rim_rows = HALO * TILE
    extended = extended_2(stacked, (("dom", 0),), rim_rows)
    ext_tiles = extended.reshape(-1, TILE, 2 * col_width)
    outgoing = stacked[send_rows[0]]
    received = lax.all_to_all(outgoing, "dom", split_axis=0, concat_axis=0, tiled=True)
    far_all = received.reshape(-1, 2 * col_width)[expander_slot]
    base_tile = dom_index * per_part - HALO
    batched = jax.vmap(tile_work, in_axes=(0, 0, 0, 0, 0, None, None, None))
    attn_all, qgrad_all, near_all, far_grad = batched(
        query_rows.reshape(per_part, TILE, col_width),
        attn_grad.reshape(per_part, TILE, col_width),
        tile_list,
        tile_count,
        far_all.reshape(per_part, TILE, DEG, 2 * col_width),
        ext_tiles,
        far_bias,
        base_tile,
    )
    n_ext = ext_tiles.shape[0]
    hit = (tile_list - base_tile)[:, :, None] == jnp.arange(n_ext)[None, None, :]
    near_tiles = near_all.reshape(per_part, tile_list.shape[1], 1, TILE, 2 * col_width)
    ext_grad = jnp.sum(
        jnp.where(hit[:, :, :, None, None], near_tiles, 0.0), axis=(0, 1)
    ).reshape(-1, 2 * col_width)
    attn_mine = attn_all.reshape(node_count, col_width)
    low_part = ext_grad[:rim_rows]
    high_part = ext_grad[rim_rows + node_count :]
    own_grad = ext_grad[rim_rows : rim_rows + node_count]
    from_next = from_behind(low_part.astype(jnp.bfloat16), "dom", -1).astype(low_part.dtype)
    from_prev = from_behind(high_part.astype(jnp.bfloat16), "dom", 1).astype(high_part.dtype)
    own_grad = own_grad.at[:rim_rows].add(from_prev).at[node_count - rim_rows :].add(from_next)
    n_dom, cap = received.shape[0], received.shape[1]
    pair_grad = far_grad.reshape(-1, 2 * col_width)
    pair_hi = lax.reduce_precision(pair_grad, exponent_bits=8, mantissa_bits=7)
    pair_lo = (pair_grad - pair_hi).astype(jnp.bfloat16)
    slot_hit = (
        expander_slot.reshape(1, -1) == jnp.arange(n_dom * cap, dtype=jnp.int32)[:, None]
    ).astype(jnp.bfloat16)
    slot_grad = jnp.dot(
        slot_hit, pair_hi.astype(jnp.bfloat16), preferred_element_type=jnp.float32
    ) + jnp.dot(slot_hit, pair_lo, preferred_element_type=jnp.float32)
    weight_part = lax.dot_general(
        full_grad, attn_mine, (((0,), (0,)), ((), ())), preferred_element_type=jnp.float32
    ).reshape(n_dom, -1, 2 * col_width)
    both = jnp.concatenate(
        [slot_grad.reshape(n_dom, cap, -1), weight_part], axis=1
    ).astype(jnp.bfloat16)
    both_back = lax.all_to_all(both, "dom", split_axis=0, concat_axis=0, tiled=True)
    returned = both_back[:, :cap].reshape(-1, 2 * col_width)
    weight_sum = jnp.sum(both_back[:, cap:].astype(jnp.float32), axis=0)
    row_hit = (
        send_rows[0].reshape(1, -1) == jnp.arange(node_count, dtype=jnp.int32)[:, None]
    ).astype(jnp.bfloat16)
    own_grad = own_grad + jnp.dot(row_hit, returned, preferred_element_type=jnp.float32)
    key_grad = own_grad[:, :col_width].astype(jnp.bfloat16)
    value_grad = own_grad[:, col_width:].astype(jnp.bfloat16)
    partial_out = jnp.dot(attn_mine, out_weight, preferred_element_type=jnp.float32)
    layer_out = lax.psum_scatter(partial_out, "head", scatter_dimension=1, tiled=True).astype(
        jnp.bfloat16
    )
    out_weight_grad = weight_sum.reshape(-1, col_width)
    return (
        layer_out,
        qgrad_all.reshape(node_count, col_width),
        key_grad,
        value_grad,
        out_weight_grad,
    )


def solution(mesh):
    in_specs = (
        P("dom", "head"),
        P("dom", "head"),
        P("dom", "head"),
        P("head", None),
        P("dom", "head"),
        P("head"),
        P("dom", None),
        P("dom"),
        P("dom", None, None),
        P("dom", None),
    )
    out_specs = (
        P("dom", "head"),
        P("dom", "head"),
        P("dom", "head"),
        P("dom", "head"),
        P("dom", "head"),
    )
    return jax.shard_map(shards, mesh=mesh, in_specs=in_specs, out_specs=out_specs, check_vma=False)
```

```python
import functools
import math

import jax
import jax.numpy as jnp
from jax import lax
from jax.experimental import pallas as pl
from jax.experimental.pallas import tpu as pltpu
from jax.sharding import PartitionSpec as P

TILE = 128
HALO = 2
DEG = 3


def extended_2(value, sides, width):
    for axis, dim in sides:
        peers, length = (lax.axis_size(axis), value.shape[dim])
        up = [(i, (i + 1) % peers) for i in range(peers - 1)]
        down = [(j, i) for i, j in up]
        last = lax.slice_in_dim(value, length - width, length, axis=dim)
        leading = lax.slice_in_dim(value, 0, width, axis=dim)
        before = lax.ppermute(last, axis, up)
        after = lax.ppermute(leading, axis, down)
        value = jnp.concatenate([before, value, after], axis=dim)
    return value


def from_behind(value, axis, steps):
    count = lax.axis_size(axis)
    leading, last = (max(0, -steps), min(count, count - steps))
    return lax.ppermute(value, axis, [(source, source + steps) for source in range(leading, last)])


def rounded(values):
    return lax.optimization_barrier(values.astype(jnp.bfloat16)).astype(jnp.float32)


def tile_work(query_tile, grad_tile, tile_ids, live_count, far_tile, ext_tiles, bias, base_tile):
    col_width = query_tile.shape[1]
    heads_here = bias.shape[0]
    head_size = col_width // heads_here
    score_scale = head_size ** (-0.5)
    key_block = ext_tiles[tile_ids - base_tile].reshape(-1, 2 * col_width)
    near_keys = key_block[:, :col_width].reshape(-1, heads_here, head_size)
    near_values = key_block[:, col_width:].reshape(-1, heads_here, head_size)
    far_keys = far_tile[:, :, :col_width].reshape(TILE, -1, heads_here, head_size)
    far_values = far_tile[:, :, col_width:].reshape(TILE, -1, heads_here, head_size)
    queries = query_tile.reshape(TILE, heads_here, head_size)
    upstream = grad_tile.reshape(TILE, heads_here, head_size)
    live_keys = jnp.repeat(jnp.arange(tile_ids.shape[0]) < live_count, TILE)
    near_score = (
        jnp.einsum("qhd,khd->hqk", queries, near_keys, preferred_element_type=jnp.float32)
        * score_scale
    )
    far_score = (
        jnp.einsum("qhd,qehd->hqe", queries, far_keys, preferred_element_type=jnp.float32)
        * score_scale
        + bias[:, None, None]
    )
    row_max = jnp.maximum(
        jnp.max(jnp.where(live_keys, near_score, -jnp.inf), axis=2), jnp.max(far_score, axis=2)
    )
    near_exp = jnp.where(live_keys, jnp.exp(near_score - row_max[:, :, None]), 0.0)
    far_exp = jnp.exp(far_score - row_max[:, :, None])
    row_sum = jnp.sum(near_exp, axis=2) + jnp.sum(far_exp, axis=2)
    mixed = jnp.einsum(
        "hqk,khd->qhd",
        near_exp.astype(jnp.bfloat16),
        near_values,
        preferred_element_type=jnp.float32,
    )
    mixed = mixed + jnp.einsum(
        "hqe,qehd->qhd",
        far_exp.astype(jnp.bfloat16),
        far_values,
        preferred_element_type=jnp.float32,
    )
    attention = (mixed / row_sum.T[:, :, None]).astype(jnp.bfloat16)
    delta_term = jnp.sum(
        upstream.astype(jnp.float32) * rounded(mixed / row_sum.T[:, :, None]), axis=2
    ).T
    near_dprob = jnp.einsum(
        "qhd,khd->hqk", upstream, near_values, preferred_element_type=jnp.float32
    )
    far_dprob = jnp.einsum(
        "qhd,qehd->hqe", upstream, far_values, preferred_element_type=jnp.float32
    )
    near_prob = near_exp / row_sum[:, :, None]
    far_prob = far_exp / row_sum[:, :, None]
    near_dscore = (near_prob * (near_dprob - delta_term[:, :, None])).astype(jnp.bfloat16)
    far_dscore = (far_prob * (far_dprob - delta_term[:, :, None])).astype(jnp.bfloat16)
    query_grad = jnp.einsum(
        "hqk,khd->qhd", near_dscore, near_keys, preferred_element_type=jnp.float32
    )
    query_grad = (
        query_grad
        + jnp.einsum("hqe,qehd->qhd", far_dscore, far_keys, preferred_element_type=jnp.float32)
    ) * score_scale
    near_kgrad = (
        jnp.einsum("hqk,qhd->khd", near_dscore, queries, preferred_element_type=jnp.float32)
        * score_scale
    )
    near_vgrad = jnp.einsum(
        "hqk,qhd->khd", near_prob.astype(jnp.bfloat16), upstream, preferred_element_type=jnp.float32
    )
    far_kgrad = (
        jnp.einsum("hqe,qhd->qehd", far_dscore, queries, preferred_element_type=jnp.float32)
        * score_scale
    )
    far_vgrad = jnp.einsum(
        "hqe,qhd->qehd", far_prob.astype(jnp.bfloat16), upstream, preferred_element_type=jnp.float32
    )
    near_grad = jnp.concatenate(
        [near_kgrad.reshape(-1, col_width), near_vgrad.reshape(-1, col_width)], axis=1
    )
    far_grad = jnp.concatenate(
        [far_kgrad.reshape(TILE, -1, col_width), far_vgrad.reshape(TILE, -1, col_width)], axis=2
    )
    return (
        attention.reshape(TILE, col_width),
        query_grad.astype(jnp.bfloat16).reshape(TILE, col_width),
        near_grad,
        far_grad,
    )


def _attn_kernel(heads, kt, pos_ref, cnt_ref, bias_ref, q_ref, do_ref, ext_ref, far_ref,
                 attn_ref, qg_ref, eg_ref, fg_ref, attn_acc, qg_acc):
    cols = q_ref.shape[1]
    hs = cols // heads
    scale = hs ** (-0.5)
    n_tiles = q_ref.shape[0] // TILE
    f32, bf16 = jnp.float32, jnp.bfloat16
    eg_ref[...] = jnp.zeros(eg_ref.shape, f32)
    fg_ref[...] = jnp.zeros(fg_ref.shape, f32)
    attn_acc[...] = jnp.zeros(attn_acc.shape, f32)
    qg_acc[...] = jnp.zeros(qg_acc.shape, f32)
    lane = lax.broadcasted_iota(jnp.int32, (TILE, cols), 1)
    nt = (((1,), (1,)), ((), ()))
    tn = (((0,), (0,)), ((), ()))
    for t in range(n_tiles):
        rows = pl.ds(t * TILE, TILE)
        count = cnt_ref[t]
        pos = [pos_ref[t * kt + j] for j in range(kt)]

        def head_body(h, carry):
            mask = (lane >= h * hs) & (lane < (h + 1) * hs)
            q = q_ref[rows, :]
            do = do_ref[rows, :]
            qf = q.astype(f32)
            dof = do.astype(f32)
            qh = jnp.where(mask, q, jnp.zeros_like(q))
            doh = jnp.where(mask, do, jnp.zeros_like(do))
            keys = [ext_ref[pos[j], :, :cols] for j in range(kt)]
            vals = [ext_ref[pos[j], :, cols:] for j in range(kt)]
            live = [j < count for j in range(kt)]
            s = [lax.dot_general(qh, keys[j], nt, preferred_element_type=f32) * scale for j in range(kt)]
            fk = [far_ref[e, rows, :cols].astype(f32) for e in range(DEG)]
            fv = [far_ref[e, rows, cols:].astype(f32) for e in range(DEG)]
            bias = bias_ref[h]
            fs = [jnp.sum(jnp.where(mask, qf * fk[e], 0.0), axis=1, keepdims=True) * scale + bias
                  for e in range(DEG)]
            m = fs[0]
            for e in range(1, DEG):
                m = jnp.maximum(m, fs[e])
            for j in range(kt):
                m = jnp.maximum(m, jnp.where(live[j], jnp.max(s[j], axis=1, keepdims=True), -jnp.inf))
            ne = [jnp.where(live[j], jnp.exp(s[j] - m), 0.0) for j in range(kt)]
            fe = [jnp.exp(fs[e] - m) for e in range(DEG)]
            row_sum = fe[0] + fe[1] + fe[2]
            row_sum = jnp.sum(ne[0], axis=1, keepdims=True) + row_sum
            for j in range(1, kt):
                row_sum = row_sum + jnp.sum(ne[j], axis=1, keepdims=True)
            mixed = jnp.dot(ne[0].astype(bf16), vals[0], preferred_element_type=f32)
            for j in range(1, kt):
                mixed = mixed + jnp.dot(ne[j].astype(bf16), vals[j], preferred_element_type=f32)
            for e in range(DEG):
                mixed = mixed + fe[e].astype(bf16).astype(f32) * fv[e]
            attn = (mixed / row_sum).astype(bf16).astype(f32)
            attn_acc[rows, :] += jnp.where(mask, attn, 0.0)
            delta = jnp.sum(jnp.where(mask, dof * attn, 0.0), axis=1, keepdims=True)
            qg = None
            for j in range(kt):
                ndp = lax.dot_general(doh, vals[j], nt, preferred_element_type=f32)
                npr = ne[j] / row_sum
                nds = (npr * (ndp - delta)).astype(bf16)
                part = jnp.dot(nds, keys[j], preferred_element_type=f32)
                qg = part if qg is None else qg + part
                kg = lax.dot_general(nds, qh, tn, preferred_element_type=f32) * scale
                vg = lax.dot_general(npr.astype(bf16), doh, tn, preferred_element_type=f32)
                eg_ref[pos[j], :, :cols] += kg
                eg_ref[pos[j], :, cols:] += vg
            for e in range(DEG):
                fdp = jnp.sum(jnp.where(mask, dof * fv[e], 0.0), axis=1, keepdims=True)
                fpr = fe[e] / row_sum
                fds = (fpr * (fdp - delta)).astype(bf16).astype(f32)
                qg = qg + fds * fk[e]
                fg_ref[e, rows, :cols] += jnp.where(mask, fds * qf * scale, 0.0)
                fg_ref[e, rows, cols:] += jnp.where(mask, fpr.astype(bf16).astype(f32) * dof, 0.0)
            qg_acc[rows, :] += jnp.where(mask, qg * scale, 0.0)
            return carry

        lax.fori_loop(0, heads, head_body, 0)
        attn_ref[rows, :] = attn_acc[rows, :].astype(attn_ref.dtype)
        qg_ref[rows, :] = qg_acc[rows, :].astype(qg_ref.dtype)


def attention_tiles(pos, cnt, bias, q, do, ext, far):
    heads = bias.shape[0]
    kt = pos.shape[0] // cnt.shape[0]
    n, cols = q.shape
    smem = pl.BlockSpec(memory_space=pltpu.SMEM)
    vmem = pl.BlockSpec(memory_space=pltpu.VMEM)
    return pl.pallas_call(
        functools.partial(_attn_kernel, heads, kt),
        out_shape=(
            jax.ShapeDtypeStruct((n, cols), jnp.bfloat16),
            jax.ShapeDtypeStruct((n, cols), jnp.bfloat16),
            jax.ShapeDtypeStruct(ext.shape, jnp.float32),
            jax.ShapeDtypeStruct(far.shape, jnp.float32),
        ),
        in_specs=[smem, smem, smem, vmem, vmem, vmem, vmem],
        out_specs=(vmem, vmem, vmem, vmem),
        scratch_shapes=[pltpu.VMEM((n, cols), jnp.float32), pltpu.VMEM((n, cols), jnp.float32)],
        cost_estimate=pl.CostEstimate(flops=int(2 * n * kt * TILE * cols * 6), bytes_accessed=int(8 * 1024 * 1024), transcendentals=int(n * heads * (kt * TILE + DEG))),
    )(pos, cnt, bias, q, do, ext, far)


def shards(
    query_rows,
    key_rows,
    value_rows,
    out_weight,
    out_grad,
    far_bias,
    tile_list,
    tile_count,
    send_rows,
    expander_slot,
):
    col_width = query_rows.shape[1]
    node_count = query_rows.shape[0]
    per_part = node_count // TILE
    dom_index = lax.axis_index("dom")
    full_grad = lax.all_gather(out_grad, "head", axis=1, tiled=True)
    attn_grad = lax.dot_general(
        full_grad, out_weight, (((1,), (1,)), ((), ())), preferred_element_type=jnp.float32
    ).astype(jnp.bfloat16)
    stacked = jnp.concatenate([key_rows, value_rows], axis=1)
    rim_rows = HALO * TILE
    extended = extended_2(stacked, (("dom", 0),), rim_rows)
    ext_tiles = extended.reshape(-1, TILE, 2 * col_width)
    send_hit = (
        send_rows[0].reshape(-1, 1) == jnp.arange(node_count, dtype=jnp.int32)[None, :]
    ).astype(jnp.bfloat16)
    outgoing = (
        jnp.dot(send_hit, stacked, preferred_element_type=jnp.float32)
        .astype(jnp.bfloat16)
        .reshape(send_rows.shape[1], send_rows.shape[2], -1)
    )
    received = lax.all_to_all(outgoing, "dom", split_axis=0, concat_axis=0, tiled=True)
    edge_slots = expander_slot.T.reshape(-1)
    n_recv = received.shape[0] * received.shape[1]
    far_hit = (
        edge_slots[:, None] == jnp.arange(n_recv, dtype=jnp.int32)[None, :]
    ).astype(jnp.bfloat16)
    far_all = (
        jnp.dot(far_hit, received.reshape(n_recv, -1), preferred_element_type=jnp.float32)
        .astype(jnp.bfloat16)
        .reshape(DEG, node_count, -1)
    )
    base_tile = dom_index * per_part - HALO
    attn_all, qgrad_all, ext_grad, far_grad = attention_tiles(
        (tile_list - base_tile).reshape(-1),
        tile_count,
        far_bias,
        query_rows,
        attn_grad,
        ext_tiles,
        far_all,
    )
    ext_grad = ext_grad.reshape(-1, 2 * col_width)
    attn_mine = attn_all.reshape(node_count, col_width)
    low_part = ext_grad[:rim_rows]
    high_part = ext_grad[rim_rows + node_count :]
    own_grad = ext_grad[rim_rows : rim_rows + node_count]
    from_next = from_behind(low_part.astype(jnp.bfloat16), "dom", -1).astype(low_part.dtype)
    from_prev = from_behind(high_part.astype(jnp.bfloat16), "dom", 1).astype(high_part.dtype)
    own_grad = own_grad.at[:rim_rows].add(from_prev).at[node_count - rim_rows :].add(from_next)
    n_dom, cap = received.shape[0], received.shape[1]
    pair_grad = far_grad.reshape(-1, 2 * col_width)
    pair_hi = lax.reduce_precision(pair_grad, exponent_bits=8, mantissa_bits=7)
    pair_lo = (pair_grad - pair_hi).astype(jnp.bfloat16)
    slot_hit = (
        edge_slots.reshape(1, -1) == jnp.arange(n_dom * cap, dtype=jnp.int32)[:, None]
    ).astype(jnp.bfloat16)
    slot_grad = jnp.dot(
        slot_hit, pair_hi.astype(jnp.bfloat16), preferred_element_type=jnp.float32
    ) + jnp.dot(slot_hit, pair_lo, preferred_element_type=jnp.float32)
    weight_part = lax.dot_general(
        full_grad, attn_mine, (((0,), (0,)), ((), ())), preferred_element_type=jnp.float32
    ).reshape(n_dom, -1, 2 * col_width)
    both = jnp.concatenate(
        [slot_grad.reshape(n_dom, cap, -1), weight_part], axis=1
    ).astype(jnp.bfloat16)
    both_back = lax.all_to_all(both, "dom", split_axis=0, concat_axis=0, tiled=True)
    returned = both_back[:, :cap].reshape(-1, 2 * col_width)
    weight_sum = jnp.sum(both_back[:, cap:].astype(jnp.float32), axis=0)
    row_hit = (
        send_rows[0].reshape(1, -1) == jnp.arange(node_count, dtype=jnp.int32)[:, None]
    ).astype(jnp.bfloat16)
    own_grad = own_grad + jnp.dot(row_hit, returned, preferred_element_type=jnp.float32)
    key_grad = own_grad[:, :col_width].astype(jnp.bfloat16)
    value_grad = own_grad[:, col_width:].astype(jnp.bfloat16)
    partial_out = jnp.dot(attn_mine, out_weight, preferred_element_type=jnp.float32)
    layer_out = lax.psum_scatter(partial_out, "head", scatter_dimension=1, tiled=True).astype(
        jnp.bfloat16
    )
    out_weight_grad = weight_sum.reshape(-1, col_width)
    return (
        layer_out,
        qgrad_all.reshape(node_count, col_width),
        key_grad,
        value_grad,
        out_weight_grad,
    )


def solution(mesh):
    in_specs = (
        P("dom", "head"),
        P("dom", "head"),
        P("dom", "head"),
        P("head", None),
        P("dom", "head"),
        P("head"),
        P("dom", None),
        P("dom"),
        P("dom", None, None),
        P("dom", None),
    )
    out_specs = (
        P("dom", "head"),
        P("dom", "head"),
        P("dom", "head"),
        P("dom", "head"),
        P("dom", "head"),
    )
    return jax.shard_map(shards, mesh=mesh, in_specs=in_specs, out_specs=out_specs, check_vma=False)
```

```python
import functools
import math

import jax
import jax.numpy as jnp
from jax import lax
from jax.experimental import pallas as pl
from jax.experimental.pallas import tpu as pltpu
from jax.sharding import PartitionSpec as P

TILE = 128
HALO = 2
DEG = 3


def extended_2(value, sides, width):
    for axis, dim in sides:
        peers, length = (lax.axis_size(axis), value.shape[dim])
        up = [(i, (i + 1) % peers) for i in range(peers - 1)]
        down = [(j, i) for i, j in up]
        last = lax.slice_in_dim(value, length - width, length, axis=dim)
        leading = lax.slice_in_dim(value, 0, width, axis=dim)
        before = lax.ppermute(last, axis, up)
        after = lax.ppermute(leading, axis, down)
        value = jnp.concatenate([before, value, after], axis=dim)
    return value


def from_behind(value, axis, steps):
    count = lax.axis_size(axis)
    leading, last = (max(0, -steps), min(count, count - steps))
    return lax.ppermute(value, axis, [(source, source + steps) for source in range(leading, last)])


def rounded(values):
    return lax.optimization_barrier(values.astype(jnp.bfloat16)).astype(jnp.float32)


def tile_work(query_tile, grad_tile, tile_ids, live_count, far_tile, ext_tiles, bias, base_tile):
    col_width = query_tile.shape[1]
    heads_here = bias.shape[0]
    head_size = col_width // heads_here
    score_scale = head_size ** (-0.5)
    key_block = ext_tiles[tile_ids - base_tile].reshape(-1, 2 * col_width)
    near_keys = key_block[:, :col_width].reshape(-1, heads_here, head_size)
    near_values = key_block[:, col_width:].reshape(-1, heads_here, head_size)
    far_keys = far_tile[:, :, :col_width].reshape(TILE, -1, heads_here, head_size)
    far_values = far_tile[:, :, col_width:].reshape(TILE, -1, heads_here, head_size)
    queries = query_tile.reshape(TILE, heads_here, head_size)
    upstream = grad_tile.reshape(TILE, heads_here, head_size)
    live_keys = jnp.repeat(jnp.arange(tile_ids.shape[0]) < live_count, TILE)
    near_score = (
        jnp.einsum("qhd,khd->hqk", queries, near_keys, preferred_element_type=jnp.float32)
        * score_scale
    )
    far_score = (
        jnp.einsum("qhd,qehd->hqe", queries, far_keys, preferred_element_type=jnp.float32)
        * score_scale
        + bias[:, None, None]
    )
    row_max = jnp.maximum(
        jnp.max(jnp.where(live_keys, near_score, -jnp.inf), axis=2), jnp.max(far_score, axis=2)
    )
    near_exp = jnp.where(live_keys, jnp.exp(near_score - row_max[:, :, None]), 0.0)
    far_exp = jnp.exp(far_score - row_max[:, :, None])
    row_sum = jnp.sum(near_exp, axis=2) + jnp.sum(far_exp, axis=2)
    mixed = jnp.einsum(
        "hqk,khd->qhd",
        near_exp.astype(jnp.bfloat16),
        near_values,
        preferred_element_type=jnp.float32,
    )
    mixed = mixed + jnp.einsum(
        "hqe,qehd->qhd",
        far_exp.astype(jnp.bfloat16),
        far_values,
        preferred_element_type=jnp.float32,
    )
    attention = (mixed / row_sum.T[:, :, None]).astype(jnp.bfloat16)
    delta_term = jnp.sum(
        upstream.astype(jnp.float32) * rounded(mixed / row_sum.T[:, :, None]), axis=2
    ).T
    near_dprob = jnp.einsum(
        "qhd,khd->hqk", upstream, near_values, preferred_element_type=jnp.float32
    )
    far_dprob = jnp.einsum(
        "qhd,qehd->hqe", upstream, far_values, preferred_element_type=jnp.float32
    )
    near_prob = near_exp / row_sum[:, :, None]
    far_prob = far_exp / row_sum[:, :, None]
    near_dscore = (near_prob * (near_dprob - delta_term[:, :, None])).astype(jnp.bfloat16)
    far_dscore = (far_prob * (far_dprob - delta_term[:, :, None])).astype(jnp.bfloat16)
    query_grad = jnp.einsum(
        "hqk,khd->qhd", near_dscore, near_keys, preferred_element_type=jnp.float32
    )
    query_grad = (
        query_grad
        + jnp.einsum("hqe,qehd->qhd", far_dscore, far_keys, preferred_element_type=jnp.float32)
    ) * score_scale
    near_kgrad = (
        jnp.einsum("hqk,qhd->khd", near_dscore, queries, preferred_element_type=jnp.float32)
        * score_scale
    )
    near_vgrad = jnp.einsum(
        "hqk,qhd->khd", near_prob.astype(jnp.bfloat16), upstream, preferred_element_type=jnp.float32
    )
    far_kgrad = (
        jnp.einsum("hqe,qhd->qehd", far_dscore, queries, preferred_element_type=jnp.float32)
        * score_scale
    )
    far_vgrad = jnp.einsum(
        "hqe,qhd->qehd", far_prob.astype(jnp.bfloat16), upstream, preferred_element_type=jnp.float32
    )
    near_grad = jnp.concatenate(
        [near_kgrad.reshape(-1, col_width), near_vgrad.reshape(-1, col_width)], axis=1
    )
    far_grad = jnp.concatenate(
        [far_kgrad.reshape(TILE, -1, col_width), far_vgrad.reshape(TILE, -1, col_width)], axis=2
    )
    return (
        attention.reshape(TILE, col_width),
        query_grad.astype(jnp.bfloat16).reshape(TILE, col_width),
        near_grad,
        far_grad,
    )


def _attn_kernel(heads, kt, near_out, pos_ref, cnt_ref, bias_ref, q_ref, do_ref, ext_ref, far_ref, *refs):
    if near_out:
        qg_ref, eg_ref, acc = refs
    else:
        attn_ref, fg_ref, acc = refs
    cols = q_ref.shape[1]
    hs = cols // heads
    scale = hs ** (-0.5)
    n_tiles = q_ref.shape[0] // TILE
    f32, bf16 = jnp.float32, jnp.bfloat16
    if near_out:
        eg_ref[...] = jnp.zeros(eg_ref.shape, f32)
    else:
        fg_ref[...] = jnp.zeros(fg_ref.shape, f32)
    acc[...] = jnp.zeros(acc.shape, f32)
    lane = lax.broadcasted_iota(jnp.int32, (TILE, cols), 1)
    nt = (((1,), (1,)), ((), ()))
    tn = (((0,), (0,)), ((), ()))
    for t in range(n_tiles):
        rows = pl.ds(t * TILE, TILE)
        count = cnt_ref[t]
        pos = [pos_ref[t * kt + j] for j in range(kt)]

        def head_body(h, carry):
            mask = (lane >= h * hs) & (lane < (h + 1) * hs)
            q = q_ref[rows, :]
            do = do_ref[rows, :]
            qf = q.astype(f32)
            dof = do.astype(f32)
            qh = jnp.where(mask, q, jnp.zeros_like(q))
            doh = jnp.where(mask, do, jnp.zeros_like(do))
            keys = [ext_ref[pos[j], :, :cols] for j in range(kt)]
            vals = [ext_ref[pos[j], :, cols:] for j in range(kt)]
            live = [j < count for j in range(kt)]
            s = [lax.dot_general(qh, keys[j], nt, preferred_element_type=f32) * scale for j in range(kt)]
            fk = [far_ref[e, rows, :cols].astype(f32) for e in range(DEG)]
            fv = [far_ref[e, rows, cols:].astype(f32) for e in range(DEG)]
            bias = bias_ref[h]
            fs = [jnp.sum(jnp.where(mask, qf * fk[e], 0.0), axis=1, keepdims=True) * scale + bias
                  for e in range(DEG)]
            m = fs[0]
            for e in range(1, DEG):
                m = jnp.maximum(m, fs[e])
            for j in range(kt):
                m = jnp.maximum(m, jnp.where(live[j], jnp.max(s[j], axis=1, keepdims=True), -jnp.inf))
            ne = [jnp.where(live[j], jnp.exp(s[j] - m), 0.0) for j in range(kt)]
            fe = [jnp.exp(fs[e] - m) for e in range(DEG)]
            row_sum = fe[0] + fe[1] + fe[2]
            row_sum = jnp.sum(ne[0], axis=1, keepdims=True) + row_sum
            for j in range(1, kt):
                row_sum = row_sum + jnp.sum(ne[j], axis=1, keepdims=True)
            mixed = jnp.dot(ne[0].astype(bf16), vals[0], preferred_element_type=f32)
            for j in range(1, kt):
                mixed = mixed + jnp.dot(ne[j].astype(bf16), vals[j], preferred_element_type=f32)
            for e in range(DEG):
                mixed = mixed + fe[e].astype(bf16).astype(f32) * fv[e]
            attn = (mixed / row_sum).astype(bf16).astype(f32)
            delta = jnp.sum(jnp.where(mask, dof * attn, 0.0), axis=1, keepdims=True)
            if not near_out:
                acc[rows, :] += jnp.where(mask, attn, 0.0)
                for e in range(DEG):
                    fdp = jnp.sum(jnp.where(mask, dof * fv[e], 0.0), axis=1, keepdims=True)
                    fpr = fe[e] / row_sum
                    fds = (fpr * (fdp - delta)).astype(bf16).astype(f32)
                    fg_ref[e, rows, :cols] += jnp.where(mask, fds * qf * scale, 0.0)
                    fg_ref[e, rows, cols:] += jnp.where(mask, fpr.astype(bf16).astype(f32) * dof, 0.0)
                return carry
            qg = None
            for j in range(kt):
                ndp = lax.dot_general(doh, vals[j], nt, preferred_element_type=f32)
                npr = ne[j] / row_sum
                nds = (npr * (ndp - delta)).astype(bf16)
                part = jnp.dot(nds, keys[j], preferred_element_type=f32)
                qg = part if qg is None else qg + part
                kg = lax.dot_general(nds, qh, tn, preferred_element_type=f32) * scale
                vg = lax.dot_general(npr.astype(bf16), doh, tn, preferred_element_type=f32)
                eg_ref[pos[j], :, :cols] += kg
                eg_ref[pos[j], :, cols:] += vg
            for e in range(DEG):
                fdp = jnp.sum(jnp.where(mask, dof * fv[e], 0.0), axis=1, keepdims=True)
                fpr = fe[e] / row_sum
                fds = (fpr * (fdp - delta)).astype(bf16).astype(f32)
                qg = qg + fds * fk[e]
            acc[rows, :] += jnp.where(mask, qg * scale, 0.0)
            return carry

        lax.fori_loop(0, heads, head_body, 0)
        out_ref = qg_ref if near_out else attn_ref
        out_ref[rows, :] = acc[rows, :].astype(out_ref.dtype)


def attention_tiles(near_out, pos, cnt, bias, q, do, ext, far):
    heads = bias.shape[0]
    kt = pos.shape[0] // cnt.shape[0]
    n, cols = q.shape
    smem = pl.BlockSpec(memory_space=pltpu.SMEM)
    vmem = pl.BlockSpec(memory_space=pltpu.VMEM)
    grads = jax.ShapeDtypeStruct(ext.shape if near_out else far.shape, jnp.float32)
    return pl.pallas_call(
        functools.partial(_attn_kernel, heads, kt, near_out),
        out_shape=(jax.ShapeDtypeStruct((n, cols), jnp.bfloat16), grads),
        in_specs=[smem, smem, smem, vmem, vmem, vmem, vmem],
        out_specs=(vmem, vmem),
        scratch_shapes=[pltpu.VMEM((n, cols), jnp.float32)],
        cost_estimate=pl.CostEstimate(
            flops=int(2 * n * kt * TILE * cols * (6 if near_out else 3) * heads),
            bytes_accessed=int(4 * 1024 * 1024),
            transcendentals=int(n * heads * (kt * TILE + DEG)),
        ),
    )(pos, cnt, bias, q, do, ext, far)


def shards(
    query_rows,
    key_rows,
    value_rows,
    out_weight,
    out_grad,
    far_bias,
    tile_list,
    tile_count,
    send_rows,
    expander_slot,
):
    col_width = query_rows.shape[1]
    node_count = query_rows.shape[0]
    per_part = node_count // TILE
    dom_index = lax.axis_index("dom")
    full_grad = lax.all_gather(out_grad, "head", axis=1, tiled=True)
    attn_grad = lax.dot_general(
        full_grad, out_weight, (((1,), (1,)), ((), ())), preferred_element_type=jnp.float32
    ).astype(jnp.bfloat16)
    stacked = jnp.concatenate([key_rows, value_rows], axis=1)
    rim_rows = HALO * TILE
    extended = extended_2(stacked, (("dom", 0),), rim_rows)
    ext_tiles = extended.reshape(-1, TILE, 2 * col_width)
    send_hit = (
        send_rows[0].reshape(-1, 1) == jnp.arange(node_count, dtype=jnp.int32)[None, :]
    ).astype(jnp.bfloat16)
    outgoing = (
        jnp.dot(send_hit, stacked, preferred_element_type=jnp.float32)
        .astype(jnp.bfloat16)
        .reshape(send_rows.shape[1], send_rows.shape[2], -1)
    )
    received = lax.all_to_all(outgoing, "dom", split_axis=0, concat_axis=0, tiled=True)
    edge_slots = expander_slot.T.reshape(-1)
    n_recv = received.shape[0] * received.shape[1]
    far_hit = (
        edge_slots[:, None] == jnp.arange(n_recv, dtype=jnp.int32)[None, :]
    ).astype(jnp.bfloat16)
    far_all = (
        jnp.dot(far_hit, received.reshape(n_recv, -1), preferred_element_type=jnp.float32)
        .astype(jnp.bfloat16)
        .reshape(DEG, node_count, -1)
    )
    base_tile = dom_index * per_part - HALO
    kernel_args = (
        (tile_list - base_tile).reshape(-1),
        tile_count,
        far_bias,
        query_rows,
        attn_grad,
        ext_tiles,
        far_all,
    )
    attn_all, far_grad = attention_tiles(False, *kernel_args)
    qgrad_all, ext_grad = attention_tiles(True, *kernel_args)
    ext_grad = ext_grad.reshape(-1, 2 * col_width)
    attn_mine = attn_all.reshape(node_count, col_width)
    low_part = ext_grad[:rim_rows]
    high_part = ext_grad[rim_rows + node_count :]
    own_grad = ext_grad[rim_rows : rim_rows + node_count]
    from_next = from_behind(low_part.astype(jnp.bfloat16), "dom", -1).astype(low_part.dtype)
    from_prev = from_behind(high_part.astype(jnp.bfloat16), "dom", 1).astype(high_part.dtype)
    own_grad = own_grad.at[:rim_rows].add(from_prev).at[node_count - rim_rows :].add(from_next)
    n_dom, cap = received.shape[0], received.shape[1]
    pair_grad = far_grad.reshape(-1, 2 * col_width)
    pair_hi = lax.reduce_precision(pair_grad, exponent_bits=8, mantissa_bits=7)
    pair_lo = (pair_grad - pair_hi).astype(jnp.bfloat16)
    slot_hit = (
        edge_slots.reshape(1, -1) == jnp.arange(n_dom * cap, dtype=jnp.int32)[:, None]
    ).astype(jnp.bfloat16)
    slot_grad = jnp.dot(
        slot_hit, pair_hi.astype(jnp.bfloat16), preferred_element_type=jnp.float32
    ) + jnp.dot(slot_hit, pair_lo, preferred_element_type=jnp.float32)
    weight_part = lax.dot_general(
        full_grad, attn_mine, (((0,), (0,)), ((), ())), preferred_element_type=jnp.float32
    ).reshape(n_dom, -1, 2 * col_width)
    both = jnp.concatenate(
        [slot_grad.reshape(n_dom, cap, -1), weight_part], axis=1
    ).astype(jnp.bfloat16)
    both_back = lax.all_to_all(both, "dom", split_axis=0, concat_axis=0, tiled=True)
    returned = both_back[:, :cap].reshape(-1, 2 * col_width)
    weight_sum = jnp.sum(both_back[:, cap:].astype(jnp.float32), axis=0)
    row_hit = (
        send_rows[0].reshape(1, -1) == jnp.arange(node_count, dtype=jnp.int32)[:, None]
    ).astype(jnp.bfloat16)
    own_grad = own_grad + jnp.dot(row_hit, returned, preferred_element_type=jnp.float32)
    key_grad = own_grad[:, :col_width].astype(jnp.bfloat16)
    value_grad = own_grad[:, col_width:].astype(jnp.bfloat16)
    partial_out = jnp.dot(attn_mine, out_weight, preferred_element_type=jnp.float32)
    layer_out = lax.psum_scatter(partial_out, "head", scatter_dimension=1, tiled=True).astype(
        jnp.bfloat16
    )
    out_weight_grad = weight_sum.reshape(-1, col_width)
    return (
        layer_out,
        qgrad_all.reshape(node_count, col_width),
        key_grad,
        value_grad,
        out_weight_grad,
    )


def solution(mesh):
    in_specs = (
        P("dom", "head"),
        P("dom", "head"),
        P("dom", "head"),
        P("head", None),
        P("dom", "head"),
        P("head"),
        P("dom", None),
        P("dom"),
        P("dom", None, None),
        P("dom", None),
    )
    out_specs = (
        P("dom", "head"),
        P("dom", "head"),
        P("dom", "head"),
        P("dom", "head"),
        P("dom", "head"),
    )
    return jax.shard_map(shards, mesh=mesh, in_specs=in_specs, out_specs=out_specs, check_vma=False)
```

```python
import functools
import math

import jax
import jax.numpy as jnp
from jax import lax
from jax.experimental import pallas as pl
from jax.experimental.pallas import tpu as pltpu
from jax.sharding import PartitionSpec as P

TILE = 128
HALO = 2
DEG = 3


def extended_2(value, sides, width):
    for axis, dim in sides:
        peers, length = (lax.axis_size(axis), value.shape[dim])
        up = [(i, (i + 1) % peers) for i in range(peers - 1)]
        down = [(j, i) for i, j in up]
        last = lax.slice_in_dim(value, length - width, length, axis=dim)
        leading = lax.slice_in_dim(value, 0, width, axis=dim)
        before = lax.ppermute(last, axis, up)
        after = lax.ppermute(leading, axis, down)
        value = jnp.concatenate([before, value, after], axis=dim)
    return value


def from_behind(value, axis, steps):
    count = lax.axis_size(axis)
    leading, last = (max(0, -steps), min(count, count - steps))
    return lax.ppermute(value, axis, [(source, source + steps) for source in range(leading, last)])


def rounded(values):
    return lax.optimization_barrier(values.astype(jnp.bfloat16)).astype(jnp.float32)


def tile_work(query_tile, grad_tile, tile_ids, live_count, far_tile, ext_tiles, bias, base_tile):
    col_width = query_tile.shape[1]
    heads_here = bias.shape[0]
    head_size = col_width // heads_here
    score_scale = head_size ** (-0.5)
    key_block = ext_tiles[tile_ids - base_tile].reshape(-1, 2 * col_width)
    near_keys = key_block[:, :col_width].reshape(-1, heads_here, head_size)
    near_values = key_block[:, col_width:].reshape(-1, heads_here, head_size)
    far_keys = far_tile[:, :, :col_width].reshape(TILE, -1, heads_here, head_size)
    far_values = far_tile[:, :, col_width:].reshape(TILE, -1, heads_here, head_size)
    queries = query_tile.reshape(TILE, heads_here, head_size)
    upstream = grad_tile.reshape(TILE, heads_here, head_size)
    live_keys = jnp.repeat(jnp.arange(tile_ids.shape[0]) < live_count, TILE)
    near_score = (
        jnp.einsum("qhd,khd->hqk", queries, near_keys, preferred_element_type=jnp.float32)
        * score_scale
    )
    far_score = (
        jnp.einsum("qhd,qehd->hqe", queries, far_keys, preferred_element_type=jnp.float32)
        * score_scale
        + bias[:, None, None]
    )
    row_max = jnp.maximum(
        jnp.max(jnp.where(live_keys, near_score, -jnp.inf), axis=2), jnp.max(far_score, axis=2)
    )
    near_exp = jnp.where(live_keys, jnp.exp(near_score - row_max[:, :, None]), 0.0)
    far_exp = jnp.exp(far_score - row_max[:, :, None])
    row_sum = jnp.sum(near_exp, axis=2) + jnp.sum(far_exp, axis=2)
    mixed = jnp.einsum(
        "hqk,khd->qhd",
        near_exp.astype(jnp.bfloat16),
        near_values,
        preferred_element_type=jnp.float32,
    )
    mixed = mixed + jnp.einsum(
        "hqe,qehd->qhd",
        far_exp.astype(jnp.bfloat16),
        far_values,
        preferred_element_type=jnp.float32,
    )
    attention = (mixed / row_sum.T[:, :, None]).astype(jnp.bfloat16)
    delta_term = jnp.sum(
        upstream.astype(jnp.float32) * rounded(mixed / row_sum.T[:, :, None]), axis=2
    ).T
    near_dprob = jnp.einsum(
        "qhd,khd->hqk", upstream, near_values, preferred_element_type=jnp.float32
    )
    far_dprob = jnp.einsum(
        "qhd,qehd->hqe", upstream, far_values, preferred_element_type=jnp.float32
    )
    near_prob = near_exp / row_sum[:, :, None]
    far_prob = far_exp / row_sum[:, :, None]
    near_dscore = (near_prob * (near_dprob - delta_term[:, :, None])).astype(jnp.bfloat16)
    far_dscore = (far_prob * (far_dprob - delta_term[:, :, None])).astype(jnp.bfloat16)
    query_grad = jnp.einsum(
        "hqk,khd->qhd", near_dscore, near_keys, preferred_element_type=jnp.float32
    )
    query_grad = (
        query_grad
        + jnp.einsum("hqe,qehd->qhd", far_dscore, far_keys, preferred_element_type=jnp.float32)
    ) * score_scale
    near_kgrad = (
        jnp.einsum("hqk,qhd->khd", near_dscore, queries, preferred_element_type=jnp.float32)
        * score_scale
    )
    near_vgrad = jnp.einsum(
        "hqk,qhd->khd", near_prob.astype(jnp.bfloat16), upstream, preferred_element_type=jnp.float32
    )
    far_kgrad = (
        jnp.einsum("hqe,qhd->qehd", far_dscore, queries, preferred_element_type=jnp.float32)
        * score_scale
    )
    far_vgrad = jnp.einsum(
        "hqe,qhd->qehd", far_prob.astype(jnp.bfloat16), upstream, preferred_element_type=jnp.float32
    )
    near_grad = jnp.concatenate(
        [near_kgrad.reshape(-1, col_width), near_vgrad.reshape(-1, col_width)], axis=1
    )
    far_grad = jnp.concatenate(
        [far_kgrad.reshape(TILE, -1, col_width), far_vgrad.reshape(TILE, -1, col_width)], axis=2
    )
    return (
        attention.reshape(TILE, col_width),
        query_grad.astype(jnp.bfloat16).reshape(TILE, col_width),
        near_grad,
        far_grad,
    )


def _attn_kernel(heads, kt, near_out, pos_ref, cnt_ref, bias_ref, q_ref, do_ref, ext_ref, far_ref, *refs):
    if near_out:
        qg_ref, eg_ref, acc = refs
    else:
        attn_ref, fg_ref, acc = refs
    cols = q_ref.shape[1]
    hs = cols // heads
    scale = hs ** (-0.5)
    n_tiles = q_ref.shape[0] // TILE
    f32, bf16 = jnp.float32, jnp.bfloat16
    if near_out:
        eg_ref[...] = jnp.zeros(eg_ref.shape, f32)
    else:
        fg_ref[...] = jnp.zeros(fg_ref.shape, f32)
    acc[...] = jnp.zeros(acc.shape, f32)
    lane = lax.broadcasted_iota(jnp.int32, (TILE, cols), 1)
    nt = (((1,), (1,)), ((), ()))
    tn = (((0,), (0,)), ((), ()))
    for t in range(n_tiles):
        rows = pl.ds(t * TILE, TILE)
        count = cnt_ref[t]
        pos = [pos_ref[t * kt + j] for j in range(kt)]

        def head_body(h, carry):
            mask = (lane >= h * hs) & (lane < (h + 1) * hs)
            q = q_ref[rows, :]
            do = do_ref[rows, :]
            qf = q.astype(f32)
            dof = do.astype(f32)
            qh = jnp.where(mask, q, jnp.zeros_like(q))
            doh = jnp.where(mask, do, jnp.zeros_like(do))
            keys = [ext_ref[pos[j], :, :cols] for j in range(kt)]
            vals = [ext_ref[pos[j], :, cols:] for j in range(kt)]
            live = [j < count for j in range(kt)]
            s = [lax.dot_general(qh, keys[j], nt, preferred_element_type=f32) * scale for j in range(kt)]
            fk = [far_ref[e, rows, :cols].astype(f32) for e in range(DEG)]
            fv = [far_ref[e, rows, cols:].astype(f32) for e in range(DEG)]
            bias = bias_ref[h]
            fs = [jnp.sum(jnp.where(mask, qf * fk[e], 0.0), axis=1, keepdims=True) * scale + bias
                  for e in range(DEG)]
            m = fs[0]
            for e in range(1, DEG):
                m = jnp.maximum(m, fs[e])
            for j in range(kt):
                m = jnp.maximum(m, jnp.where(live[j], jnp.max(s[j], axis=1, keepdims=True), -jnp.inf))
            ne = [jnp.where(live[j], jnp.exp(s[j] - m), 0.0) for j in range(kt)]
            fe = [jnp.exp(fs[e] - m) for e in range(DEG)]
            row_sum = fe[0] + fe[1] + fe[2]
            row_sum = jnp.sum(ne[0], axis=1, keepdims=True) + row_sum
            for j in range(1, kt):
                row_sum = row_sum + jnp.sum(ne[j], axis=1, keepdims=True)
            mixed = jnp.dot(ne[0].astype(bf16), vals[0], preferred_element_type=f32)
            for j in range(1, kt):
                mixed = mixed + jnp.dot(ne[j].astype(bf16), vals[j], preferred_element_type=f32)
            for e in range(DEG):
                mixed = mixed + fe[e].astype(bf16).astype(f32) * fv[e]
            attn = (mixed / row_sum).astype(bf16).astype(f32)
            delta = jnp.sum(jnp.where(mask, dof * attn, 0.0), axis=1, keepdims=True)
            if not near_out:
                acc[rows, :] += jnp.where(mask, attn, 0.0)
                for e in range(DEG):
                    fdp = jnp.sum(jnp.where(mask, dof * fv[e], 0.0), axis=1, keepdims=True)
                    fpr = fe[e] / row_sum
                    fds = (fpr * (fdp - delta)).astype(bf16).astype(f32)
                    fg_ref[e, rows, :cols] += jnp.where(mask, fds * qf * scale, 0.0)
                    fg_ref[e, rows, cols:] += jnp.where(mask, fpr.astype(bf16).astype(f32) * dof, 0.0)
                return carry
            qg = None
            for j in range(kt):
                ndp = lax.dot_general(doh, vals[j], nt, preferred_element_type=f32)
                npr = ne[j] / row_sum
                nds = (npr * (ndp - delta)).astype(bf16)
                part = jnp.dot(nds, keys[j], preferred_element_type=f32)
                qg = part if qg is None else qg + part
                kg = lax.dot_general(nds, qh, tn, preferred_element_type=f32) * scale
                vg = lax.dot_general(npr.astype(bf16), doh, tn, preferred_element_type=f32)
                eg_ref[pos[j], :, :cols] += kg
                eg_ref[pos[j], :, cols:] += vg
            for e in range(DEG):
                fdp = jnp.sum(jnp.where(mask, dof * fv[e], 0.0), axis=1, keepdims=True)
                fpr = fe[e] / row_sum
                fds = (fpr * (fdp - delta)).astype(bf16).astype(f32)
                qg = qg + fds * fk[e]
            acc[rows, :] += jnp.where(mask, qg * scale, 0.0)
            return carry

        lax.fori_loop(0, heads, head_body, 0)
        out_ref = qg_ref if near_out else attn_ref
        out_ref[rows, :] = acc[rows, :].astype(out_ref.dtype)


def attention_tiles(near_out, pos, cnt, bias, q, do, ext, far):
    heads = bias.shape[0]
    kt = pos.shape[0] // cnt.shape[0]
    n, cols = q.shape
    smem = pl.BlockSpec(memory_space=pltpu.SMEM)
    vmem = pl.BlockSpec(memory_space=pltpu.VMEM)
    grads = jax.ShapeDtypeStruct(ext.shape if near_out else far.shape, jnp.float32)
    return pl.pallas_call(
        functools.partial(_attn_kernel, heads, kt, near_out),
        out_shape=(jax.ShapeDtypeStruct((n, cols), jnp.bfloat16), grads),
        in_specs=[smem, smem, smem, vmem, vmem, vmem, vmem],
        out_specs=(vmem, vmem),
        scratch_shapes=[pltpu.VMEM((n, cols), jnp.float32)],
        cost_estimate=pl.CostEstimate(
            flops=int(2 * n * kt * TILE * cols * (6 if near_out else 3) * heads),
            bytes_accessed=int(4 * 1024 * 1024),
            transcendentals=int(n * heads * (kt * TILE + DEG)),
        ),
    )(pos, cnt, bias, q, do, ext, far)


def shards(
    query_rows,
    key_rows,
    value_rows,
    out_weight,
    out_grad,
    far_bias,
    tile_list,
    tile_count,
    send_rows,
    expander_slot,
):
    col_width = query_rows.shape[1]
    node_count = query_rows.shape[0]
    per_part = node_count // TILE
    dom_index = lax.axis_index("dom")
    full_grad = lax.all_gather(out_grad, "head", axis=1, tiled=True)
    attn_grad = lax.dot_general(
        full_grad, out_weight, (((1,), (1,)), ((), ())), preferred_element_type=jnp.float32
    ).astype(jnp.bfloat16)
    stacked = jnp.concatenate([key_rows, value_rows], axis=1)
    rim_rows = HALO * TILE
    extended = extended_2(stacked, (("dom", 0),), rim_rows)
    ext_tiles = extended.reshape(-1, TILE, 2 * col_width)
    send_hit = (
        send_rows[0].reshape(-1, 1) == jnp.arange(node_count, dtype=jnp.int32)[None, :]
    ).astype(jnp.bfloat16)
    outgoing = (
        jnp.dot(send_hit, stacked, preferred_element_type=jnp.float32)
        .astype(jnp.bfloat16)
        .reshape(send_rows.shape[1], send_rows.shape[2], -1)
    )
    received = lax.all_to_all(outgoing, "dom", split_axis=0, concat_axis=0, tiled=True)
    edge_slots = expander_slot.T.reshape(-1)
    n_recv = received.shape[0] * received.shape[1]
    far_hit = (
        edge_slots[:, None] == jnp.arange(n_recv, dtype=jnp.int32)[None, :]
    ).astype(jnp.bfloat16)
    far_all = (
        jnp.dot(far_hit, received.reshape(n_recv, -1), preferred_element_type=jnp.float32)
        .astype(jnp.bfloat16)
        .reshape(DEG, node_count, -1)
    )
    base_tile = dom_index * per_part - HALO
    kernel_args = (
        (tile_list - base_tile).reshape(-1),
        tile_count,
        far_bias,
        query_rows,
        attn_grad,
        ext_tiles,
        far_all,
    )
    attn_all, far_grad = attention_tiles(False, *kernel_args)
    qgrad_all, ext_grad = attention_tiles(True, *kernel_args)
    ext_grad = ext_grad.reshape(-1, 2 * col_width)
    attn_mine = attn_all.reshape(node_count, col_width)
    low_part = ext_grad[:rim_rows]
    high_part = ext_grad[rim_rows + node_count :]
    own_grad = ext_grad[rim_rows : rim_rows + node_count]
    from_next = from_behind(low_part.astype(jnp.bfloat16), "dom", -1).astype(low_part.dtype)
    from_prev = from_behind(high_part.astype(jnp.bfloat16), "dom", 1).astype(high_part.dtype)
    own_grad = own_grad.at[:rim_rows].add(from_prev).at[node_count - rim_rows :].add(from_next)
    n_dom, cap = received.shape[0], received.shape[1]
    pair_grad = far_grad.reshape(-1, 2 * col_width)
    pair_hi = lax.reduce_precision(pair_grad, exponent_bits=8, mantissa_bits=7)
    pair_lo = (pair_grad - pair_hi).astype(jnp.bfloat16)
    slot_hit = (
        edge_slots.reshape(1, -1) == jnp.arange(n_dom * cap, dtype=jnp.int32)[:, None]
    ).astype(jnp.bfloat16)
    slot_grad = jnp.dot(
        slot_hit, pair_hi.astype(jnp.bfloat16), preferred_element_type=jnp.float32
    ) + jnp.dot(slot_hit, pair_lo, preferred_element_type=jnp.float32)
    weight_part = lax.dot_general(
        full_grad, attn_mine, (((0,), (0,)), ((), ())), preferred_element_type=jnp.float32
    ).reshape(n_dom, -1, 2 * col_width)
    both = jnp.concatenate(
        [slot_grad.reshape(n_dom, cap, -1), weight_part], axis=1
    ).astype(jnp.bfloat16)
    both_back = lax.all_to_all(both, "dom", split_axis=0, concat_axis=0, tiled=True)
    returned = both_back[:, :cap].reshape(-1, 2 * col_width)
    weight_sum = jnp.sum(both_back[:, cap:].astype(jnp.float32), axis=0)
    row_hit = (
        send_rows[0].reshape(1, -1) == jnp.arange(node_count, dtype=jnp.int32)[:, None]
    ).astype(jnp.bfloat16)
    own_grad = own_grad + jnp.dot(row_hit, returned, preferred_element_type=jnp.float32)
    key_grad = own_grad[:, :col_width].astype(jnp.bfloat16)
    value_grad = own_grad[:, col_width:].astype(jnp.bfloat16)
    partial_out = jnp.dot(attn_mine, out_weight, preferred_element_type=jnp.float32)
    head_index = lax.axis_index("head")
    other_cols = lax.dynamic_slice_in_dim(partial_out, (1 - head_index) * col_width, col_width, 1)
    own_cols = lax.dynamic_slice_in_dim(partial_out, head_index * col_width, col_width, 1)
    swapped = lax.ppermute(other_cols, "head", [(0, 1), (1, 0)])
    layer_out = (own_cols + swapped).astype(jnp.bfloat16)
    out_weight_grad = weight_sum.reshape(-1, col_width)
    return (
        layer_out,
        qgrad_all.reshape(node_count, col_width),
        key_grad,
        value_grad,
        out_weight_grad,
    )


def solution(mesh):
    in_specs = (
        P("dom", "head"),
        P("dom", "head"),
        P("dom", "head"),
        P("head", None),
        P("dom", "head"),
        P("head"),
        P("dom", None),
        P("dom"),
        P("dom", None, None),
        P("dom", None),
    )
    out_specs = (
        P("dom", "head"),
        P("dom", "head"),
        P("dom", "head"),
        P("dom", "head"),
        P("dom", "head"),
    )
    return jax.shard_map(shards, mesh=mesh, in_specs=in_specs, out_specs=out_specs, check_vma=False)
```

```python
import functools
import math

import jax
import jax.numpy as jnp
from jax import lax
from jax.experimental import pallas as pl
from jax.experimental.pallas import tpu as pltpu
from jax.sharding import PartitionSpec as P

TILE = 128
HALO = 2
DEG = 3


def extended_2(value, sides, width):
    for axis, dim in sides:
        peers, length = (lax.axis_size(axis), value.shape[dim])
        up = [(i, (i + 1) % peers) for i in range(peers - 1)]
        down = [(j, i) for i, j in up]
        last = lax.slice_in_dim(value, length - width, length, axis=dim)
        leading = lax.slice_in_dim(value, 0, width, axis=dim)
        before = lax.ppermute(last, axis, up)
        after = lax.ppermute(leading, axis, down)
        value = jnp.concatenate([before, value, after], axis=dim)
    return value


def from_behind(value, axis, steps):
    count = lax.axis_size(axis)
    leading, last = (max(0, -steps), min(count, count - steps))
    return lax.ppermute(value, axis, [(source, source + steps) for source in range(leading, last)])


def rounded(values):
    return lax.optimization_barrier(values.astype(jnp.bfloat16)).astype(jnp.float32)


def tile_work(query_tile, grad_tile, tile_ids, live_count, far_tile, ext_tiles, bias, base_tile):
    col_width = query_tile.shape[1]
    heads_here = bias.shape[0]
    head_size = col_width // heads_here
    score_scale = head_size ** (-0.5)
    key_block = ext_tiles[tile_ids - base_tile].reshape(-1, 2 * col_width)
    near_keys = key_block[:, :col_width].reshape(-1, heads_here, head_size)
    near_values = key_block[:, col_width:].reshape(-1, heads_here, head_size)
    far_keys = far_tile[:, :, :col_width].reshape(TILE, -1, heads_here, head_size)
    far_values = far_tile[:, :, col_width:].reshape(TILE, -1, heads_here, head_size)
    queries = query_tile.reshape(TILE, heads_here, head_size)
    upstream = grad_tile.reshape(TILE, heads_here, head_size)
    live_keys = jnp.repeat(jnp.arange(tile_ids.shape[0]) < live_count, TILE)
    near_score = (
        jnp.einsum("qhd,khd->hqk", queries, near_keys, preferred_element_type=jnp.float32)
        * score_scale
    )
    far_score = (
        jnp.einsum("qhd,qehd->hqe", queries, far_keys, preferred_element_type=jnp.float32)
        * score_scale
        + bias[:, None, None]
    )
    row_max = jnp.maximum(
        jnp.max(jnp.where(live_keys, near_score, -jnp.inf), axis=2), jnp.max(far_score, axis=2)
    )
    near_exp = jnp.where(live_keys, jnp.exp(near_score - row_max[:, :, None]), 0.0)
    far_exp = jnp.exp(far_score - row_max[:, :, None])
    row_sum = jnp.sum(near_exp, axis=2) + jnp.sum(far_exp, axis=2)
    mixed = jnp.einsum(
        "hqk,khd->qhd",
        near_exp.astype(jnp.bfloat16),
        near_values,
        preferred_element_type=jnp.float32,
    )
    mixed = mixed + jnp.einsum(
        "hqe,qehd->qhd",
        far_exp.astype(jnp.bfloat16),
        far_values,
        preferred_element_type=jnp.float32,
    )
    attention = (mixed / row_sum.T[:, :, None]).astype(jnp.bfloat16)
    delta_term = jnp.sum(
        upstream.astype(jnp.float32) * rounded(mixed / row_sum.T[:, :, None]), axis=2
    ).T
    near_dprob = jnp.einsum(
        "qhd,khd->hqk", upstream, near_values, preferred_element_type=jnp.float32
    )
    far_dprob = jnp.einsum(
        "qhd,qehd->hqe", upstream, far_values, preferred_element_type=jnp.float32
    )
    near_prob = near_exp / row_sum[:, :, None]
    far_prob = far_exp / row_sum[:, :, None]
    near_dscore = (near_prob * (near_dprob - delta_term[:, :, None])).astype(jnp.bfloat16)
    far_dscore = (far_prob * (far_dprob - delta_term[:, :, None])).astype(jnp.bfloat16)
    query_grad = jnp.einsum(
        "hqk,khd->qhd", near_dscore, near_keys, preferred_element_type=jnp.float32
    )
    query_grad = (
        query_grad
        + jnp.einsum("hqe,qehd->qhd", far_dscore, far_keys, preferred_element_type=jnp.float32)
    ) * score_scale
    near_kgrad = (
        jnp.einsum("hqk,qhd->khd", near_dscore, queries, preferred_element_type=jnp.float32)
        * score_scale
    )
    near_vgrad = jnp.einsum(
        "hqk,qhd->khd", near_prob.astype(jnp.bfloat16), upstream, preferred_element_type=jnp.float32
    )
    far_kgrad = (
        jnp.einsum("hqe,qhd->qehd", far_dscore, queries, preferred_element_type=jnp.float32)
        * score_scale
    )
    far_vgrad = jnp.einsum(
        "hqe,qhd->qehd", far_prob.astype(jnp.bfloat16), upstream, preferred_element_type=jnp.float32
    )
    near_grad = jnp.concatenate(
        [near_kgrad.reshape(-1, col_width), near_vgrad.reshape(-1, col_width)], axis=1
    )
    far_grad = jnp.concatenate(
        [far_kgrad.reshape(TILE, -1, col_width), far_vgrad.reshape(TILE, -1, col_width)], axis=2
    )
    return (
        attention.reshape(TILE, col_width),
        query_grad.astype(jnp.bfloat16).reshape(TILE, col_width),
        near_grad,
        far_grad,
    )


def _attn_kernel(heads, kt, near_out, pos_ref, cnt_ref, bias_ref, q_ref, do_ref, ext_ref, far_ref, *refs):
    if near_out:
        qg_ref, eg_ref, acc = refs
    else:
        attn_ref, fg_ref, acc = refs
    cols = q_ref.shape[1]
    hs = cols // heads
    scale = hs ** (-0.5)
    n_tiles = q_ref.shape[0] // TILE
    f32, bf16 = jnp.float32, jnp.bfloat16
    if near_out:
        eg_ref[...] = jnp.zeros(eg_ref.shape, f32)
    else:
        fg_ref[...] = jnp.zeros(fg_ref.shape, f32)
    acc[...] = jnp.zeros(acc.shape, f32)
    lane = lax.broadcasted_iota(jnp.int32, (TILE, cols), 1)
    nt = (((1,), (1,)), ((), ()))
    tn = (((0,), (0,)), ((), ()))
    for t in range(n_tiles):
        rows = pl.ds(t * TILE, TILE)
        count = cnt_ref[t]
        pos = [pos_ref[t * kt + j] for j in range(kt)]

        def head_body(h, carry):
            mask = (lane >= h * hs) & (lane < (h + 1) * hs)
            q = q_ref[rows, :]
            do = do_ref[rows, :]
            qf = q.astype(f32)
            dof = do.astype(f32)
            qh = jnp.where(mask, q, jnp.zeros_like(q))
            doh = jnp.where(mask, do, jnp.zeros_like(do))
            keys = [ext_ref[pos[j], :, :cols] for j in range(kt)]
            vals = [ext_ref[pos[j], :, cols:] for j in range(kt)]
            live = [j < count for j in range(kt)]
            s = [lax.dot_general(qh, keys[j], nt, preferred_element_type=f32) * scale for j in range(kt)]
            fk = [far_ref[e, rows, :cols].astype(f32) for e in range(DEG)]
            fv = [far_ref[e, rows, cols:].astype(f32) for e in range(DEG)]
            bias = bias_ref[h]
            fs = [jnp.sum(jnp.where(mask, qf * fk[e], 0.0), axis=1, keepdims=True) * scale + bias
                  for e in range(DEG)]
            m = fs[0]
            for e in range(1, DEG):
                m = jnp.maximum(m, fs[e])
            for j in range(kt):
                m = jnp.maximum(m, jnp.where(live[j], jnp.max(s[j], axis=1, keepdims=True), -jnp.inf))
            ne = [jnp.where(live[j], jnp.exp(s[j] - m), 0.0) for j in range(kt)]
            fe = [jnp.exp(fs[e] - m) for e in range(DEG)]
            row_sum = fe[0] + fe[1] + fe[2]
            row_sum = jnp.sum(ne[0], axis=1, keepdims=True) + row_sum
            for j in range(1, kt):
                row_sum = row_sum + jnp.sum(ne[j], axis=1, keepdims=True)
            mixed = jnp.dot(ne[0].astype(bf16), vals[0], preferred_element_type=f32)
            for j in range(1, kt):
                mixed = mixed + jnp.dot(ne[j].astype(bf16), vals[j], preferred_element_type=f32)
            for e in range(DEG):
                mixed = mixed + fe[e].astype(bf16).astype(f32) * fv[e]
            attn = (mixed / row_sum).astype(bf16).astype(f32)
            delta = jnp.sum(jnp.where(mask, dof * attn, 0.0), axis=1, keepdims=True)
            if not near_out:
                acc[rows, :] += jnp.where(mask, attn, 0.0)
                for e in range(DEG):
                    fdp = jnp.sum(jnp.where(mask, dof * fv[e], 0.0), axis=1, keepdims=True)
                    fpr = fe[e] / row_sum
                    fds = (fpr * (fdp - delta)).astype(bf16).astype(f32)
                    fg_ref[e, rows, :cols] += jnp.where(mask, fds * qf * scale, 0.0)
                    fg_ref[e, rows, cols:] += jnp.where(mask, fpr.astype(bf16).astype(f32) * dof, 0.0)
                return carry
            qg = None
            for j in range(kt):
                ndp = lax.dot_general(doh, vals[j], nt, preferred_element_type=f32)
                npr = ne[j] / row_sum
                nds = (npr * (ndp - delta)).astype(bf16)
                part = jnp.dot(nds, keys[j], preferred_element_type=f32)
                qg = part if qg is None else qg + part
                kg = lax.dot_general(nds, qh, tn, preferred_element_type=f32) * scale
                vg = lax.dot_general(npr.astype(bf16), doh, tn, preferred_element_type=f32)
                eg_ref[pos[j], :, :cols] += kg
                eg_ref[pos[j], :, cols:] += vg
            for e in range(DEG):
                fdp = jnp.sum(jnp.where(mask, dof * fv[e], 0.0), axis=1, keepdims=True)
                fpr = fe[e] / row_sum
                fds = (fpr * (fdp - delta)).astype(bf16).astype(f32)
                qg = qg + fds * fk[e]
            acc[rows, :] += jnp.where(mask, qg * scale, 0.0)
            return carry

        lax.fori_loop(0, heads, head_body, 0)
        out_ref = qg_ref if near_out else attn_ref
        out_ref[rows, :] = acc[rows, :].astype(out_ref.dtype)


def attention_tiles(near_out, pos, cnt, bias, q, do, ext, far):
    heads = bias.shape[0]
    kt = pos.shape[0] // cnt.shape[0]
    n, cols = q.shape
    smem = pl.BlockSpec(memory_space=pltpu.SMEM)
    vmem = pl.BlockSpec(memory_space=pltpu.VMEM)
    grads = jax.ShapeDtypeStruct(ext.shape if near_out else far.shape, jnp.float32)
    return pl.pallas_call(
        functools.partial(_attn_kernel, heads, kt, near_out),
        out_shape=(jax.ShapeDtypeStruct((n, cols), jnp.bfloat16), grads),
        in_specs=[smem, smem, smem, vmem, vmem, vmem, vmem],
        out_specs=(vmem, vmem),
        scratch_shapes=[pltpu.VMEM((n, cols), jnp.float32)],
        cost_estimate=pl.CostEstimate(
            flops=int(2 * n * kt * TILE * cols * (6 if near_out else 3) * heads),
            bytes_accessed=int(4 * 1024 * 1024),
            transcendentals=int(n * heads * (kt * TILE + DEG)),
        ),
    )(pos, cnt, bias, q, do, ext, far)


def _fwd_kernel(heads, kt, pos_ref, cnt_ref, bias_ref, q_ref, do_ref, ext_ref, hit_ref, recv_ref,
                attn_ref, fg_ref, far_ref):
    cols = q_ref.shape[1]
    hs = cols // heads
    scale = hs ** (-0.5)
    n = q_ref.shape[0]
    n_tiles = n // TILE
    f32, bf16 = jnp.float32, jnp.bfloat16
    recv = recv_ref[...]
    for e in range(DEG):
        far_ref[e] = jnp.dot(
            hit_ref[pl.ds(e * n, n), :], recv, preferred_element_type=f32
        ).astype(bf16)
    seg = (
        lax.broadcasted_iota(jnp.int32, (cols, TILE), 0) // hs
        == lax.broadcasted_iota(jnp.int32, (cols, TILE), 1)
    ).astype(bf16)
    spread = (
        lax.broadcasted_iota(jnp.int32, (TILE, cols), 0)
        == lax.broadcasted_iota(jnp.int32, (TILE, cols), 1) // hs
    ).astype(bf16)
    lane = lax.broadcasted_iota(jnp.int32, (TILE, cols), 1)
    col = lax.broadcasted_iota(jnp.int32, (TILE, TILE), 1)
    bias_row = jnp.zeros((TILE, TILE), f32)
    for h in range(heads):
        bias_row = jnp.where(col == h, bias_ref[h], bias_row)
    nt = (((1,), (1,)), ((), ()))

    def seg_sum(x):
        hi = x.astype(bf16)
        lo = (x - hi.astype(f32)).astype(bf16)
        return jnp.dot(hi, seg, preferred_element_type=f32) + jnp.dot(lo, seg, preferred_element_type=f32)

    for t in range(n_tiles):
        rows = pl.ds(t * TILE, TILE)
        count = cnt_ref[t]
        pos = [pos_ref[t * kt + j] for j in range(kt)]
        q = q_ref[rows, :]
        do = do_ref[rows, :]
        qf = q.astype(f32)
        dof = do.astype(f32)
        fk = [far_ref[e, rows, :cols].astype(f32) for e in range(DEG)]
        fv = [far_ref[e, rows, cols:].astype(f32) for e in range(DEG)]
        fs_all = [seg_sum(qf * fk[e]) * scale + bias_row for e in range(DEG)]
        fdp_all = [seg_sum(dof * fv[e]) for e in range(DEG)]
        live = [j < count for j in range(kt)]
        attn_acc = jnp.zeros((TILE, cols), f32)
        fds_cols = [jnp.zeros((TILE, TILE), f32) for e in range(DEG)]
        fpr_cols = [jnp.zeros((TILE, TILE), f32) for e in range(DEG)]
        for h in range(heads):
            mask = (lane >= h * hs) & (lane < (h + 1) * hs)
            qh = jnp.where(mask, q, jnp.zeros_like(q))
            keys = [ext_ref[pos[j], :, :cols] for j in range(kt)]
            vals = [ext_ref[pos[j], :, cols:] for j in range(kt)]
            s = [lax.dot_general(qh, keys[j], nt, preferred_element_type=f32) * scale for j in range(kt)]
            fs = [fs_all[e][:, h:h + 1] for e in range(DEG)]
            m = fs[0]
            for e in range(1, DEG):
                m = jnp.maximum(m, fs[e])
            for j in range(kt):
                m = jnp.maximum(m, jnp.where(live[j], jnp.max(s[j], axis=1, keepdims=True), -jnp.inf))
            ne = [jnp.where(live[j], jnp.exp(s[j] - m), 0.0) for j in range(kt)]
            fe = [jnp.exp(fs[e] - m) for e in range(DEG)]
            row_sum = fe[0] + fe[1] + fe[2]
            row_sum = jnp.sum(ne[0], axis=1, keepdims=True) + row_sum
            for j in range(1, kt):
                row_sum = row_sum + jnp.sum(ne[j], axis=1, keepdims=True)
            mixed = jnp.dot(ne[0].astype(bf16), vals[0], preferred_element_type=f32)
            for j in range(1, kt):
                mixed = mixed + jnp.dot(ne[j].astype(bf16), vals[j], preferred_element_type=f32)
            for e in range(DEG):
                mixed = mixed + fe[e].astype(bf16).astype(f32) * fv[e]
            attn = (mixed / row_sum).astype(bf16).astype(f32)
            attn_acc = jnp.where(mask, attn, attn_acc)
            delta = jnp.sum(jnp.where(mask, dof * attn, 0.0), axis=1, keepdims=True)
            for e in range(DEG):
                fpr = fe[e] / row_sum
                fds = (fpr * (fdp_all[e][:, h:h + 1] - delta)).astype(bf16).astype(f32)
                fds_cols[e] = jnp.where(col == h, fds, fds_cols[e])
                fpr_cols[e] = jnp.where(col == h, fpr.astype(bf16).astype(f32), fpr_cols[e])
        attn_ref[rows, :] = attn_acc.astype(attn_ref.dtype)
        for e in range(DEG):
            fds_wide = jnp.dot(fds_cols[e].astype(bf16), spread, preferred_element_type=f32)
            fpr_wide = jnp.dot(fpr_cols[e].astype(bf16), spread, preferred_element_type=f32)
            fg_ref[e, rows, :cols] = fds_wide * qf * scale
            fg_ref[e, rows, cols:] = fpr_wide * dof


def forward_tiles(pos, cnt, bias, q, do, ext, hit, recv):
    heads = bias.shape[0]
    kt = pos.shape[0] // cnt.shape[0]
    n, cols = q.shape
    smem = pl.BlockSpec(memory_space=pltpu.SMEM)
    vmem = pl.BlockSpec(memory_space=pltpu.VMEM)
    return pl.pallas_call(
        functools.partial(_fwd_kernel, heads, kt),
        out_shape=(
            jax.ShapeDtypeStruct((n, cols), jnp.bfloat16),
            jax.ShapeDtypeStruct((DEG, n, 2 * cols), jnp.float32),
            jax.ShapeDtypeStruct((DEG, n, 2 * cols), jnp.bfloat16),
        ),
        in_specs=[smem, smem, smem, vmem, vmem, vmem, vmem, vmem],
        out_specs=(vmem, vmem, vmem),
        cost_estimate=pl.CostEstimate(
            flops=int(2 * n * kt * TILE * cols * 3 * heads + 2 * hit.shape[0] * hit.shape[1] * recv.shape[1]),
            bytes_accessed=int(8 * 1024 * 1024),
            transcendentals=int(n * heads * (kt * TILE + DEG)),
        ),
    )(pos, cnt, bias, q, do, ext, hit, recv)


def shards(
    query_rows,
    key_rows,
    value_rows,
    out_weight,
    out_grad,
    far_bias,
    tile_list,
    tile_count,
    send_rows,
    expander_slot,
):
    col_width = query_rows.shape[1]
    node_count = query_rows.shape[0]
    per_part = node_count // TILE
    dom_index = lax.axis_index("dom")
    full_grad = lax.all_gather(out_grad, "head", axis=1, tiled=True)
    attn_grad = lax.dot_general(
        full_grad, out_weight, (((1,), (1,)), ((), ())), preferred_element_type=jnp.float32
    ).astype(jnp.bfloat16)
    stacked = jnp.concatenate([key_rows, value_rows], axis=1)
    rim_rows = HALO * TILE
    extended = extended_2(stacked, (("dom", 0),), rim_rows)
    ext_tiles = extended.reshape(-1, TILE, 2 * col_width)
    send_hit = (
        send_rows[0].reshape(-1, 1) == jnp.arange(node_count, dtype=jnp.int32)[None, :]
    ).astype(jnp.bfloat16)
    outgoing = (
        jnp.dot(send_hit, stacked, preferred_element_type=jnp.float32)
        .astype(jnp.bfloat16)
        .reshape(send_rows.shape[1], send_rows.shape[2], -1)
    )
    received = lax.all_to_all(outgoing, "dom", split_axis=0, concat_axis=0, tiled=True)
    edge_slots = expander_slot.T.reshape(-1)
    n_recv = received.shape[0] * received.shape[1]
    far_hit = (
        edge_slots[:, None] == jnp.arange(n_recv, dtype=jnp.int32)[None, :]
    ).astype(jnp.bfloat16)
    base_tile = dom_index * per_part - HALO
    tile_pos = (tile_list - base_tile).reshape(-1)
    attn_all, far_grad, far_all = forward_tiles(
        tile_pos,
        tile_count,
        far_bias,
        query_rows,
        attn_grad,
        ext_tiles,
        far_hit,
        received.reshape(n_recv, -1),
    )
    qgrad_all, ext_grad = attention_tiles(
        True, tile_pos, tile_count, far_bias, query_rows, attn_grad, ext_tiles, far_all
    )
    ext_grad = ext_grad.reshape(-1, 2 * col_width)
    attn_mine = attn_all.reshape(node_count, col_width)
    low_part = ext_grad[:rim_rows]
    high_part = ext_grad[rim_rows + node_count :]
    own_grad = ext_grad[rim_rows : rim_rows + node_count]
    from_next = from_behind(low_part.astype(jnp.bfloat16), "dom", -1).astype(low_part.dtype)
    from_prev = from_behind(high_part.astype(jnp.bfloat16), "dom", 1).astype(high_part.dtype)
    own_grad = own_grad.at[:rim_rows].add(from_prev).at[node_count - rim_rows :].add(from_next)
    n_dom, cap = received.shape[0], received.shape[1]
    pair_grad = far_grad.reshape(-1, 2 * col_width)
    pair_hi = lax.reduce_precision(pair_grad, exponent_bits=8, mantissa_bits=7)
    pair_lo = (pair_grad - pair_hi).astype(jnp.bfloat16)
    slot_hit = (
        edge_slots.reshape(1, -1) == jnp.arange(n_dom * cap, dtype=jnp.int32)[:, None]
    ).astype(jnp.bfloat16)
    slot_grad = jnp.dot(
        slot_hit, pair_hi.astype(jnp.bfloat16), preferred_element_type=jnp.float32
    ) + jnp.dot(slot_hit, pair_lo, preferred_element_type=jnp.float32)
    weight_part = lax.dot_general(
        full_grad, attn_mine, (((0,), (0,)), ((), ())), preferred_element_type=jnp.float32
    ).reshape(n_dom, -1, 2 * col_width)
    both = jnp.concatenate(
        [slot_grad.reshape(n_dom, cap, -1), weight_part], axis=1
    ).astype(jnp.bfloat16)
    both_back = lax.all_to_all(both, "dom", split_axis=0, concat_axis=0, tiled=True)
    returned = both_back[:, :cap].reshape(-1, 2 * col_width)
    weight_sum = jnp.sum(both_back[:, cap:].astype(jnp.float32), axis=0)
    row_hit = (
        send_rows[0].reshape(1, -1) == jnp.arange(node_count, dtype=jnp.int32)[:, None]
    ).astype(jnp.bfloat16)
    own_grad = own_grad + jnp.dot(row_hit, returned, preferred_element_type=jnp.float32)
    key_grad = own_grad[:, :col_width].astype(jnp.bfloat16)
    value_grad = own_grad[:, col_width:].astype(jnp.bfloat16)
    partial_out = jnp.dot(attn_mine, out_weight, preferred_element_type=jnp.float32)
    head_index = lax.axis_index("head")
    other_cols = lax.dynamic_slice_in_dim(partial_out, (1 - head_index) * col_width, col_width, 1)
    own_cols = lax.dynamic_slice_in_dim(partial_out, head_index * col_width, col_width, 1)
    swapped = lax.ppermute(other_cols, "head", [(0, 1), (1, 0)])
    layer_out = (own_cols + swapped).astype(jnp.bfloat16)
    out_weight_grad = weight_sum.reshape(-1, col_width)
    return (
        layer_out,
        qgrad_all.reshape(node_count, col_width),
        key_grad,
        value_grad,
        out_weight_grad,
    )


def solution(mesh):
    in_specs = (
        P("dom", "head"),
        P("dom", "head"),
        P("dom", "head"),
        P("head", None),
        P("dom", "head"),
        P("head"),
        P("dom", None),
        P("dom"),
        P("dom", None, None),
        P("dom", None),
    )
    out_specs = (
        P("dom", "head"),
        P("dom", "head"),
        P("dom", "head"),
        P("dom", "head"),
        P("dom", "head"),
    )
    return jax.shard_map(shards, mesh=mesh, in_specs=in_specs, out_specs=out_specs, check_vma=False)
```

```python
import functools
import math

import jax
import jax.numpy as jnp
from jax import lax
from jax.experimental import pallas as pl
from jax.experimental.pallas import tpu as pltpu
from jax.sharding import PartitionSpec as P

TILE = 128
HALO = 2
DEG = 3


def extended_2(value, sides, width):
    for axis, dim in sides:
        peers, length = (lax.axis_size(axis), value.shape[dim])
        up = [(i, (i + 1) % peers) for i in range(peers - 1)]
        down = [(j, i) for i, j in up]
        last = lax.slice_in_dim(value, length - width, length, axis=dim)
        leading = lax.slice_in_dim(value, 0, width, axis=dim)
        before = lax.ppermute(last, axis, up)
        after = lax.ppermute(leading, axis, down)
        value = jnp.concatenate([before, value, after], axis=dim)
    return value


def from_behind(value, axis, steps):
    count = lax.axis_size(axis)
    leading, last = (max(0, -steps), min(count, count - steps))
    return lax.ppermute(value, axis, [(source, source + steps) for source in range(leading, last)])


def rounded(values):
    return lax.optimization_barrier(values.astype(jnp.bfloat16)).astype(jnp.float32)


def tile_work(query_tile, grad_tile, tile_ids, live_count, far_tile, ext_tiles, bias, base_tile):
    col_width = query_tile.shape[1]
    heads_here = bias.shape[0]
    head_size = col_width // heads_here
    score_scale = head_size ** (-0.5)
    key_block = ext_tiles[tile_ids - base_tile].reshape(-1, 2 * col_width)
    near_keys = key_block[:, :col_width].reshape(-1, heads_here, head_size)
    near_values = key_block[:, col_width:].reshape(-1, heads_here, head_size)
    far_keys = far_tile[:, :, :col_width].reshape(TILE, -1, heads_here, head_size)
    far_values = far_tile[:, :, col_width:].reshape(TILE, -1, heads_here, head_size)
    queries = query_tile.reshape(TILE, heads_here, head_size)
    upstream = grad_tile.reshape(TILE, heads_here, head_size)
    live_keys = jnp.repeat(jnp.arange(tile_ids.shape[0]) < live_count, TILE)
    near_score = (
        jnp.einsum("qhd,khd->hqk", queries, near_keys, preferred_element_type=jnp.float32)
        * score_scale
    )
    far_score = (
        jnp.einsum("qhd,qehd->hqe", queries, far_keys, preferred_element_type=jnp.float32)
        * score_scale
        + bias[:, None, None]
    )
    row_max = jnp.maximum(
        jnp.max(jnp.where(live_keys, near_score, -jnp.inf), axis=2), jnp.max(far_score, axis=2)
    )
    near_exp = jnp.where(live_keys, jnp.exp(near_score - row_max[:, :, None]), 0.0)
    far_exp = jnp.exp(far_score - row_max[:, :, None])
    row_sum = jnp.sum(near_exp, axis=2) + jnp.sum(far_exp, axis=2)
    mixed = jnp.einsum(
        "hqk,khd->qhd",
        near_exp.astype(jnp.bfloat16),
        near_values,
        preferred_element_type=jnp.float32,
    )
    mixed = mixed + jnp.einsum(
        "hqe,qehd->qhd",
        far_exp.astype(jnp.bfloat16),
        far_values,
        preferred_element_type=jnp.float32,
    )
    attention = (mixed / row_sum.T[:, :, None]).astype(jnp.bfloat16)
    delta_term = jnp.sum(
        upstream.astype(jnp.float32) * rounded(mixed / row_sum.T[:, :, None]), axis=2
    ).T
    near_dprob = jnp.einsum(
        "qhd,khd->hqk", upstream, near_values, preferred_element_type=jnp.float32
    )
    far_dprob = jnp.einsum(
        "qhd,qehd->hqe", upstream, far_values, preferred_element_type=jnp.float32
    )
    near_prob = near_exp / row_sum[:, :, None]
    far_prob = far_exp / row_sum[:, :, None]
    near_dscore = (near_prob * (near_dprob - delta_term[:, :, None])).astype(jnp.bfloat16)
    far_dscore = (far_prob * (far_dprob - delta_term[:, :, None])).astype(jnp.bfloat16)
    query_grad = jnp.einsum(
        "hqk,khd->qhd", near_dscore, near_keys, preferred_element_type=jnp.float32
    )
    query_grad = (
        query_grad
        + jnp.einsum("hqe,qehd->qhd", far_dscore, far_keys, preferred_element_type=jnp.float32)
    ) * score_scale
    near_kgrad = (
        jnp.einsum("hqk,qhd->khd", near_dscore, queries, preferred_element_type=jnp.float32)
        * score_scale
    )
    near_vgrad = jnp.einsum(
        "hqk,qhd->khd", near_prob.astype(jnp.bfloat16), upstream, preferred_element_type=jnp.float32
    )
    far_kgrad = (
        jnp.einsum("hqe,qhd->qehd", far_dscore, queries, preferred_element_type=jnp.float32)
        * score_scale
    )
    far_vgrad = jnp.einsum(
        "hqe,qhd->qehd", far_prob.astype(jnp.bfloat16), upstream, preferred_element_type=jnp.float32
    )
    near_grad = jnp.concatenate(
        [near_kgrad.reshape(-1, col_width), near_vgrad.reshape(-1, col_width)], axis=1
    )
    far_grad = jnp.concatenate(
        [far_kgrad.reshape(TILE, -1, col_width), far_vgrad.reshape(TILE, -1, col_width)], axis=2
    )
    return (
        attention.reshape(TILE, col_width),
        query_grad.astype(jnp.bfloat16).reshape(TILE, col_width),
        near_grad,
        far_grad,
    )


def _attn_kernel(heads, kt, near_out, pos_ref, cnt_ref, bias_ref, q_ref, do_ref, ext_ref, far_ref, *refs):
    if near_out:
        qg_ref, eg_ref, acc = refs
    else:
        fge_ref, fgo_ref, attn_ref, fg_ref, acc = refs
    cols = q_ref.shape[1]
    hs = cols // heads
    scale = hs ** (-0.5)
    n_tiles = q_ref.shape[0] // TILE
    f32, bf16 = jnp.float32, jnp.bfloat16
    if near_out:
        eg_ref[...] = jnp.zeros(eg_ref.shape, f32)
    else:
        fg_ref[...] = jnp.zeros(fg_ref.shape, f32)
    acc[...] = jnp.zeros(acc.shape, f32)
    lane = lax.broadcasted_iota(jnp.int32, (TILE, cols), 1)
    nt = (((1,), (1,)), ((), ()))
    tn = (((0,), (0,)), ((), ()))
    for t in range(n_tiles):
        rows = pl.ds(t * TILE, TILE)
        count = cnt_ref[t]
        pos = [pos_ref[t * kt + j] for j in range(kt)]

        def head_body(h, carry):
            mask = (lane >= h * hs) & (lane < (h + 1) * hs)
            q = q_ref[rows, :]
            do = do_ref[rows, :]
            qf = q.astype(f32)
            dof = do.astype(f32)
            qh = jnp.where(mask, q, jnp.zeros_like(q))
            doh = jnp.where(mask, do, jnp.zeros_like(do))
            keys = [ext_ref[pos[j], :, :cols] for j in range(kt)]
            vals = [ext_ref[pos[j], :, cols:] for j in range(kt)]
            live = [j < count for j in range(kt)]
            s = [lax.dot_general(qh, keys[j], nt, preferred_element_type=f32) * scale for j in range(kt)]
            fk = [far_ref[e, rows, :cols].astype(f32) for e in range(DEG)]
            fv = [far_ref[e, rows, cols:].astype(f32) for e in range(DEG)]
            bias = bias_ref[h]
            fs = [jnp.sum(jnp.where(mask, qf * fk[e], 0.0), axis=1, keepdims=True) * scale + bias
                  for e in range(DEG)]
            m = fs[0]
            for e in range(1, DEG):
                m = jnp.maximum(m, fs[e])
            for j in range(kt):
                m = jnp.maximum(m, jnp.where(live[j], jnp.max(s[j], axis=1, keepdims=True), -jnp.inf))
            ne = [jnp.where(live[j], jnp.exp(s[j] - m), 0.0) for j in range(kt)]
            fe = [jnp.exp(fs[e] - m) for e in range(DEG)]
            row_sum = fe[0] + fe[1] + fe[2]
            row_sum = jnp.sum(ne[0], axis=1, keepdims=True) + row_sum
            for j in range(1, kt):
                row_sum = row_sum + jnp.sum(ne[j], axis=1, keepdims=True)
            mixed = jnp.dot(ne[0].astype(bf16), vals[0], preferred_element_type=f32)
            for j in range(1, kt):
                mixed = mixed + jnp.dot(ne[j].astype(bf16), vals[j], preferred_element_type=f32)
            for e in range(DEG):
                mixed = mixed + fe[e].astype(bf16).astype(f32) * fv[e]
            attn = (mixed / row_sum).astype(bf16).astype(f32)
            delta = jnp.sum(jnp.where(mask, dof * attn, 0.0), axis=1, keepdims=True)
            if not near_out:
                acc[rows, :] += jnp.where(mask, attn, 0.0)
                for e in range(DEG):
                    fdp = jnp.sum(jnp.where(mask, dof * fv[e], 0.0), axis=1, keepdims=True)
                    fpr = fe[e] / row_sum
                    fds = (fpr * (fdp - delta)).astype(bf16).astype(f32)
                    pair_rows = pl.ds(e * q_ref.shape[0] + t * TILE, TILE)
                    fg_ref[pair_rows, :cols] += jnp.where(mask, fds * qf * scale, 0.0)
                    fg_ref[pair_rows, cols:] += jnp.where(mask, fpr.astype(bf16).astype(f32) * dof, 0.0)
                return carry
            qg = None
            for j in range(kt):
                ndp = lax.dot_general(doh, vals[j], nt, preferred_element_type=f32)
                npr = ne[j] / row_sum
                nds = (npr * (ndp - delta)).astype(bf16)
                part = jnp.dot(nds, keys[j], preferred_element_type=f32)
                qg = part if qg is None else qg + part
                kg = lax.dot_general(nds, qh, tn, preferred_element_type=f32) * scale
                vg = lax.dot_general(npr.astype(bf16), doh, tn, preferred_element_type=f32)
                eg_ref[pos[j], :, :cols] += kg
                eg_ref[pos[j], :, cols:] += vg
            for e in range(DEG):
                fdp = jnp.sum(jnp.where(mask, dof * fv[e], 0.0), axis=1, keepdims=True)
                fpr = fe[e] / row_sum
                fds = (fpr * (fdp - delta)).astype(bf16).astype(f32)
                qg = qg + fds * fk[e]
            acc[rows, :] += jnp.where(mask, qg * scale, 0.0)
            return carry

        lax.fori_loop(0, heads, head_body, 0)
        out_ref = qg_ref if near_out else attn_ref
        out_ref[rows, :] = acc[rows, :].astype(out_ref.dtype)
    if not near_out:
        w_rows = pl.ds(DEG * q_ref.shape[0], fge_ref.shape[1])
        attn_all = attn_ref[...]
        fg_ref[w_rows, :cols] = lax.dot_general(fge_ref[...], attn_all, tn, preferred_element_type=f32)
        fg_ref[w_rows, cols:] = lax.dot_general(fgo_ref[...], attn_all, tn, preferred_element_type=f32)


def attention_tiles(near_out, pos, cnt, bias, q, do, ext, far, *model_cols):
    heads = bias.shape[0]
    kt = pos.shape[0] // cnt.shape[0]
    n, cols = q.shape
    smem = pl.BlockSpec(memory_space=pltpu.SMEM)
    vmem = pl.BlockSpec(memory_space=pltpu.VMEM)
    if near_out:
        grads = jax.ShapeDtypeStruct(ext.shape, jnp.float32)
    else:
        grads = jax.ShapeDtypeStruct(
            (DEG * n + model_cols[0].shape[1], far.shape[2]), jnp.float32
        )
    return pl.pallas_call(
        functools.partial(_attn_kernel, heads, kt, near_out),
        out_shape=(jax.ShapeDtypeStruct((n, cols), jnp.bfloat16), grads),
        in_specs=[smem, smem, smem] + [vmem] * (4 + len(model_cols)),
        out_specs=(vmem, vmem),
        scratch_shapes=[pltpu.VMEM((n, cols), jnp.float32)],
        cost_estimate=pl.CostEstimate(
            flops=int(2 * n * kt * TILE * cols * (6 if near_out else 3) * heads),
            bytes_accessed=int(4 * 1024 * 1024),
            transcendentals=int(n * heads * (kt * TILE + DEG)),
        ),
    )(pos, cnt, bias, q, do, ext, far, *model_cols)


def shards(
    query_rows,
    key_rows,
    value_rows,
    out_weight,
    out_grad,
    far_bias,
    tile_list,
    tile_count,
    send_rows,
    expander_slot,
):
    col_width = query_rows.shape[1]
    node_count = query_rows.shape[0]
    per_part = node_count // TILE
    dom_index = lax.axis_index("dom")
    full_grad = lax.all_gather(out_grad, "head", axis=1, tiled=True)
    attn_grad = lax.dot_general(
        full_grad, out_weight, (((1,), (1,)), ((), ())), preferred_element_type=jnp.float32
    ).astype(jnp.bfloat16)
    stacked = jnp.concatenate([key_rows, value_rows], axis=1)
    rim_rows = HALO * TILE
    extended = extended_2(stacked, (("dom", 0),), rim_rows)
    ext_tiles = extended.reshape(-1, TILE, 2 * col_width)
    send_hit = (
        send_rows[0].reshape(-1, 1) == jnp.arange(node_count, dtype=jnp.int32)[None, :]
    ).astype(jnp.bfloat16)
    outgoing = (
        jnp.dot(send_hit, stacked, preferred_element_type=jnp.float32)
        .astype(jnp.bfloat16)
        .reshape(send_rows.shape[1], send_rows.shape[2], -1)
    )
    received = lax.all_to_all(outgoing, "dom", split_axis=0, concat_axis=0, tiled=True)
    edge_slots = expander_slot.T.reshape(-1)
    n_recv = received.shape[0] * received.shape[1]
    far_hit = (
        edge_slots[:, None] == jnp.arange(n_recv, dtype=jnp.int32)[None, :]
    ).astype(jnp.bfloat16)
    far_all = (
        jnp.dot(far_hit, received.reshape(n_recv, -1), preferred_element_type=jnp.float32)
        .astype(jnp.bfloat16)
        .reshape(DEG, node_count, -1)
    )
    base_tile = dom_index * per_part - HALO
    kernel_args = (
        (tile_list - base_tile).reshape(-1),
        tile_count,
        far_bias,
        query_rows,
        attn_grad,
        ext_tiles,
        far_all,
    )
    attn_all, far_grad = attention_tiles(
        False, *kernel_args, full_grad[:, 0::2], full_grad[:, 1::2]
    )
    qgrad_all, ext_grad = attention_tiles(True, *kernel_args)
    ext_grad = ext_grad.reshape(-1, 2 * col_width)
    attn_mine = attn_all.reshape(node_count, col_width)
    low_part = ext_grad[:rim_rows]
    high_part = ext_grad[rim_rows + node_count :]
    own_grad = ext_grad[rim_rows : rim_rows + node_count]
    from_next = from_behind(low_part.astype(jnp.bfloat16), "dom", -1).astype(low_part.dtype)
    from_prev = from_behind(high_part.astype(jnp.bfloat16), "dom", 1).astype(high_part.dtype)
    own_grad = own_grad.at[:rim_rows].add(from_prev).at[node_count - rim_rows :].add(from_next)
    n_dom, cap = received.shape[0], received.shape[1]
    n_pairs = DEG * node_count
    w_per = (far_grad.shape[0] - n_pairs) // n_dom
    pair_hi = lax.reduce_precision(far_grad, exponent_bits=8, mantissa_bits=7)
    pair_lo = (far_grad - pair_hi).astype(jnp.bfloat16)
    rho = jnp.arange(n_dom * (cap + w_per), dtype=jnp.int32)
    dest, sub = rho // (cap + w_per), rho % (cap + w_per)
    slot_target = jnp.where(sub < cap, dest * cap + sub, -1)
    row_target = jnp.where(sub >= cap, n_pairs + dest * w_per + sub - cap, -1)
    col = jnp.arange(far_grad.shape[0], dtype=jnp.int32)
    col_slot = jnp.concatenate(
        [edge_slots, jnp.full((far_grad.shape[0] - n_pairs,), -2, jnp.int32)]
    )
    payload_hit = (
        (col_slot[None, :] == slot_target[:, None]) | (col[None, :] == row_target[:, None])
    ).astype(jnp.bfloat16)
    both = (
        jnp.dot(payload_hit, pair_hi.astype(jnp.bfloat16), preferred_element_type=jnp.float32)
        + jnp.dot(payload_hit, pair_lo, preferred_element_type=jnp.float32)
    ).astype(jnp.bfloat16).reshape(n_dom, cap + w_per, -1)
    both_back = lax.all_to_all(both, "dom", split_axis=0, concat_axis=0, tiled=True)
    returned = both_back[:, :cap].reshape(-1, 2 * col_width)
    weight_sum = jnp.sum(both_back[:, cap:].astype(jnp.float32), axis=0)
    row_hit = (
        send_rows[0].reshape(1, -1) == jnp.arange(node_count, dtype=jnp.int32)[:, None]
    ).astype(jnp.bfloat16)
    own_grad = own_grad + jnp.dot(row_hit, returned, preferred_element_type=jnp.float32)
    key_grad = own_grad[:, :col_width].astype(jnp.bfloat16)
    value_grad = own_grad[:, col_width:].astype(jnp.bfloat16)
    partial_out = jnp.dot(attn_mine, out_weight, preferred_element_type=jnp.float32)
    head_index = lax.axis_index("head")
    other_cols = lax.dynamic_slice_in_dim(partial_out, (1 - head_index) * col_width, col_width, 1)
    own_cols = lax.dynamic_slice_in_dim(partial_out, head_index * col_width, col_width, 1)
    swapped = lax.ppermute(other_cols, "head", [(0, 1), (1, 0)])
    layer_out = (own_cols + swapped).astype(jnp.bfloat16)
    out_weight_grad = weight_sum.reshape(-1, col_width)
    return (
        layer_out,
        qgrad_all.reshape(node_count, col_width),
        key_grad,
        value_grad,
        out_weight_grad,
    )


def solution(mesh):
    in_specs = (
        P("dom", "head"),
        P("dom", "head"),
        P("dom", "head"),
        P("head", None),
        P("dom", "head"),
        P("head"),
        P("dom", None),
        P("dom"),
        P("dom", None, None),
        P("dom", None),
    )
    out_specs = (
        P("dom", "head"),
        P("dom", "head"),
        P("dom", "head"),
        P("dom", "head"),
        P("dom", "head"),
    )
    return jax.shard_map(shards, mesh=mesh, in_specs=in_specs, out_specs=out_specs, check_vma=False)
```

```python
import functools
import math

import jax
import jax.numpy as jnp
from jax import lax
from jax.experimental import pallas as pl
from jax.experimental.pallas import tpu as pltpu
from jax.sharding import PartitionSpec as P

TILE = 128
HALO = 2
DEG = 3


def extended_2(value, sides, width):
    for axis, dim in sides:
        peers, length = (lax.axis_size(axis), value.shape[dim])
        up = [(i, (i + 1) % peers) for i in range(peers - 1)]
        down = [(j, i) for i, j in up]
        last = lax.slice_in_dim(value, length - width, length, axis=dim)
        leading = lax.slice_in_dim(value, 0, width, axis=dim)
        before = lax.ppermute(last, axis, up)
        after = lax.ppermute(leading, axis, down)
        value = jnp.concatenate([before, value, after], axis=dim)
    return value


def from_behind(value, axis, steps):
    count = lax.axis_size(axis)
    leading, last = (max(0, -steps), min(count, count - steps))
    return lax.ppermute(value, axis, [(source, source + steps) for source in range(leading, last)])


def rounded(values):
    return lax.optimization_barrier(values.astype(jnp.bfloat16)).astype(jnp.float32)


def tile_work(query_tile, grad_tile, tile_ids, live_count, far_tile, ext_tiles, bias, base_tile):
    col_width = query_tile.shape[1]
    heads_here = bias.shape[0]
    head_size = col_width // heads_here
    score_scale = head_size ** (-0.5)
    key_block = ext_tiles[tile_ids - base_tile].reshape(-1, 2 * col_width)
    near_keys = key_block[:, :col_width].reshape(-1, heads_here, head_size)
    near_values = key_block[:, col_width:].reshape(-1, heads_here, head_size)
    far_keys = far_tile[:, :, :col_width].reshape(TILE, -1, heads_here, head_size)
    far_values = far_tile[:, :, col_width:].reshape(TILE, -1, heads_here, head_size)
    queries = query_tile.reshape(TILE, heads_here, head_size)
    upstream = grad_tile.reshape(TILE, heads_here, head_size)
    live_keys = jnp.repeat(jnp.arange(tile_ids.shape[0]) < live_count, TILE)
    near_score = (
        jnp.einsum("qhd,khd->hqk", queries, near_keys, preferred_element_type=jnp.float32)
        * score_scale
    )
    far_score = (
        jnp.einsum("qhd,qehd->hqe", queries, far_keys, preferred_element_type=jnp.float32)
        * score_scale
        + bias[:, None, None]
    )
    row_max = jnp.maximum(
        jnp.max(jnp.where(live_keys, near_score, -jnp.inf), axis=2), jnp.max(far_score, axis=2)
    )
    near_exp = jnp.where(live_keys, jnp.exp(near_score - row_max[:, :, None]), 0.0)
    far_exp = jnp.exp(far_score - row_max[:, :, None])
    row_sum = jnp.sum(near_exp, axis=2) + jnp.sum(far_exp, axis=2)
    mixed = jnp.einsum(
        "hqk,khd->qhd",
        near_exp.astype(jnp.bfloat16),
        near_values,
        preferred_element_type=jnp.float32,
    )
    mixed = mixed + jnp.einsum(
        "hqe,qehd->qhd",
        far_exp.astype(jnp.bfloat16),
        far_values,
        preferred_element_type=jnp.float32,
    )
    attention = (mixed / row_sum.T[:, :, None]).astype(jnp.bfloat16)
    delta_term = jnp.sum(
        upstream.astype(jnp.float32) * rounded(mixed / row_sum.T[:, :, None]), axis=2
    ).T
    near_dprob = jnp.einsum(
        "qhd,khd->hqk", upstream, near_values, preferred_element_type=jnp.float32
    )
    far_dprob = jnp.einsum(
        "qhd,qehd->hqe", upstream, far_values, preferred_element_type=jnp.float32
    )
    near_prob = near_exp / row_sum[:, :, None]
    far_prob = far_exp / row_sum[:, :, None]
    near_dscore = (near_prob * (near_dprob - delta_term[:, :, None])).astype(jnp.bfloat16)
    far_dscore = (far_prob * (far_dprob - delta_term[:, :, None])).astype(jnp.bfloat16)
    query_grad = jnp.einsum(
        "hqk,khd->qhd", near_dscore, near_keys, preferred_element_type=jnp.float32
    )
    query_grad = (
        query_grad
        + jnp.einsum("hqe,qehd->qhd", far_dscore, far_keys, preferred_element_type=jnp.float32)
    ) * score_scale
    near_kgrad = (
        jnp.einsum("hqk,qhd->khd", near_dscore, queries, preferred_element_type=jnp.float32)
        * score_scale
    )
    near_vgrad = jnp.einsum(
        "hqk,qhd->khd", near_prob.astype(jnp.bfloat16), upstream, preferred_element_type=jnp.float32
    )
    far_kgrad = (
        jnp.einsum("hqe,qhd->qehd", far_dscore, queries, preferred_element_type=jnp.float32)
        * score_scale
    )
    far_vgrad = jnp.einsum(
        "hqe,qhd->qehd", far_prob.astype(jnp.bfloat16), upstream, preferred_element_type=jnp.float32
    )
    near_grad = jnp.concatenate(
        [near_kgrad.reshape(-1, col_width), near_vgrad.reshape(-1, col_width)], axis=1
    )
    far_grad = jnp.concatenate(
        [far_kgrad.reshape(TILE, -1, col_width), far_vgrad.reshape(TILE, -1, col_width)], axis=2
    )
    return (
        attention.reshape(TILE, col_width),
        query_grad.astype(jnp.bfloat16).reshape(TILE, col_width),
        near_grad,
        far_grad,
    )


def _attn_kernel(heads, kt, near_out, pos_ref, cnt_ref, bias_ref, q_ref, do_ref, ext_ref, far_ref, *refs):
    if near_out:
        qg_ref, eg_ref, acc = refs
    else:
        mx_ref, st_ref, attn_ref, fg_ref, acc = refs
    cols = q_ref.shape[1]
    hs = cols // heads
    scale = hs ** (-0.5)
    n_tiles = q_ref.shape[0] // TILE
    f32, bf16 = jnp.float32, jnp.bfloat16
    if near_out:
        eg_ref[...] = jnp.zeros(eg_ref.shape, f32)
    else:
        fg_ref[...] = jnp.zeros(fg_ref.shape, f32)
    acc[...] = jnp.zeros(acc.shape, f32)
    lane = lax.broadcasted_iota(jnp.int32, (TILE, cols), 1)
    nt = (((1,), (1,)), ((), ()))
    tn = (((0,), (0,)), ((), ()))
    for t in range(n_tiles):
        rows = pl.ds(t * TILE, TILE)
        count = cnt_ref[t]
        pos = [pos_ref[t * kt + j] for j in range(kt)]

        def head_body(h, carry):
            mask = (lane >= h * hs) & (lane < (h + 1) * hs)
            q = q_ref[rows, :]
            do = do_ref[rows, :]
            qf = q.astype(f32)
            dof = do.astype(f32)
            qh = jnp.where(mask, q, jnp.zeros_like(q))
            doh = jnp.where(mask, do, jnp.zeros_like(do))
            fk = [far_ref[e, rows, :cols].astype(f32) for e in range(DEG)]
            fv = [far_ref[e, rows, cols:].astype(f32) for e in range(DEG)]
            bias = bias_ref[h]
            fs = [jnp.sum(jnp.where(mask, qf * fk[e], 0.0), axis=1, keepdims=True) * scale + bias
                  for e in range(DEG)]
            if near_out:
                keys = [ext_ref[pos[j], :, :cols] for j in range(kt)]
                vals = [ext_ref[pos[j], :, cols:] for j in range(kt)]
                live = [j < count for j in range(kt)]
                s = [lax.dot_general(qh, keys[j], nt, preferred_element_type=f32) * scale for j in range(kt)]
                m = fs[0]
                for e in range(1, DEG):
                    m = jnp.maximum(m, fs[e])
                for j in range(kt):
                    m = jnp.maximum(m, jnp.where(live[j], jnp.max(s[j], axis=1, keepdims=True), -jnp.inf))
                ne = [jnp.where(live[j], jnp.exp(s[j] - m), 0.0) for j in range(kt)]
                fe = [jnp.exp(fs[e] - m) for e in range(DEG)]
                row_sum = fe[0] + fe[1] + fe[2]
                row_sum = jnp.sum(ne[0], axis=1, keepdims=True) + row_sum
                for j in range(1, kt):
                    row_sum = row_sum + jnp.sum(ne[j], axis=1, keepdims=True)
                mixed = jnp.dot(ne[0].astype(bf16), vals[0], preferred_element_type=f32)
                for j in range(1, kt):
                    mixed = mixed + jnp.dot(ne[j].astype(bf16), vals[j], preferred_element_type=f32)
            else:
                colh = lax.broadcasted_iota(jnp.int32, (TILE, TILE), 1) == h
                near_max = jnp.sum(jnp.where(colh, st_ref[0, rows, :], 0.0), axis=1, keepdims=True)
                near_total = jnp.sum(jnp.where(colh, st_ref[1, rows, :], 0.0), axis=1, keepdims=True)
                m = jnp.maximum(near_max, fs[0])
                for e in range(1, DEG):
                    m = jnp.maximum(m, fs[e])
                rescale = jnp.exp(near_max - m)
                fe = [jnp.exp(fs[e] - m) for e in range(DEG)]
                row_sum = near_total * rescale + (fe[0] + fe[1] + fe[2])
                mixed = mx_ref[rows, :] * rescale
            for e in range(DEG):
                mixed = mixed + fe[e].astype(bf16).astype(f32) * fv[e]
            attn = (mixed / row_sum).astype(bf16).astype(f32)
            delta = jnp.sum(jnp.where(mask, dof * attn, 0.0), axis=1, keepdims=True)
            if not near_out:
                acc[rows, :] += jnp.where(mask, attn, 0.0)
                for e in range(DEG):
                    fdp = jnp.sum(jnp.where(mask, dof * fv[e], 0.0), axis=1, keepdims=True)
                    fpr = fe[e] / row_sum
                    fds = (fpr * (fdp - delta)).astype(bf16).astype(f32)
                    fg_ref[e, rows, :cols] += jnp.where(mask, fds * qf * scale, 0.0)
                    fg_ref[e, rows, cols:] += jnp.where(mask, fpr.astype(bf16).astype(f32) * dof, 0.0)
                return carry
            qg = None
            for j in range(kt):
                ndp = lax.dot_general(doh, vals[j], nt, preferred_element_type=f32)
                npr = ne[j] / row_sum
                nds = (npr * (ndp - delta)).astype(bf16)
                part = jnp.dot(nds, keys[j], preferred_element_type=f32)
                qg = part if qg is None else qg + part
                kg = lax.dot_general(nds, qh, tn, preferred_element_type=f32) * scale
                vg = lax.dot_general(npr.astype(bf16), doh, tn, preferred_element_type=f32)
                eg_ref[pos[j], :, :cols] += kg
                eg_ref[pos[j], :, cols:] += vg
            for e in range(DEG):
                fdp = jnp.sum(jnp.where(mask, dof * fv[e], 0.0), axis=1, keepdims=True)
                fpr = fe[e] / row_sum
                fds = (fpr * (fdp - delta)).astype(bf16).astype(f32)
                qg = qg + fds * fk[e]
            acc[rows, :] += jnp.where(mask, qg * scale, 0.0)
            return carry

        lax.fori_loop(0, heads, head_body, 0)
        out_ref = qg_ref if near_out else attn_ref
        out_ref[rows, :] = acc[rows, :].astype(out_ref.dtype)


def _near_kernel(heads, kt, pos_ref, cnt_ref, q_ref, ext_ref, mx_ref, st_ref):
    cols = q_ref.shape[1]
    hs = cols // heads
    scale = hs ** (-0.5)
    n_tiles = q_ref.shape[0] // TILE
    f32, bf16 = jnp.float32, jnp.bfloat16
    mx_ref[...] = jnp.zeros(mx_ref.shape, f32)
    st_ref[...] = jnp.zeros(st_ref.shape, f32)
    lane = lax.broadcasted_iota(jnp.int32, (TILE, cols), 1)
    col = lax.broadcasted_iota(jnp.int32, (TILE, TILE), 1)
    nt = (((1,), (1,)), ((), ()))
    for t in range(n_tiles):
        rows = pl.ds(t * TILE, TILE)
        count = cnt_ref[t]
        pos = [pos_ref[t * kt + j] for j in range(kt)]

        def head_body(h, carry):
            mask = (lane >= h * hs) & (lane < (h + 1) * hs)
            q = q_ref[rows, :]
            qh = jnp.where(mask, q, jnp.zeros_like(q))
            keys = [ext_ref[pos[j], :, :cols] for j in range(kt)]
            vals = [ext_ref[pos[j], :, cols:] for j in range(kt)]
            live = [j < count for j in range(kt)]
            s = [lax.dot_general(qh, keys[j], nt, preferred_element_type=f32) * scale for j in range(kt)]
            m = jnp.max(s[0], axis=1, keepdims=True)
            for j in range(1, kt):
                m = jnp.maximum(m, jnp.where(live[j], jnp.max(s[j], axis=1, keepdims=True), -jnp.inf))
            ne = [jnp.where(live[j], jnp.exp(s[j] - m), 0.0) for j in range(kt)]
            total = jnp.sum(ne[0], axis=1, keepdims=True)
            for j in range(1, kt):
                total = total + jnp.sum(ne[j], axis=1, keepdims=True)
            mixed = jnp.dot(ne[0].astype(bf16), vals[0], preferred_element_type=f32)
            for j in range(1, kt):
                mixed = mixed + jnp.dot(ne[j].astype(bf16), vals[j], preferred_element_type=f32)
            mx_ref[rows, :] += jnp.where(mask, mixed, 0.0)
            st_ref[0, rows, :] = jnp.where(col == h, m, st_ref[0, rows, :])
            st_ref[1, rows, :] = jnp.where(col == h, total, st_ref[1, rows, :])
            return carry

        lax.fori_loop(0, heads, head_body, 0)


def near_tiles(pos, cnt, q, ext, heads):
    kt = pos.shape[0] // cnt.shape[0]
    n, cols = q.shape
    smem = pl.BlockSpec(memory_space=pltpu.SMEM)
    vmem = pl.BlockSpec(memory_space=pltpu.VMEM)
    return pl.pallas_call(
        functools.partial(_near_kernel, heads, kt),
        out_shape=(
            jax.ShapeDtypeStruct((n, cols), jnp.float32),
            jax.ShapeDtypeStruct((2, n, TILE), jnp.float32),
        ),
        in_specs=[smem, smem, vmem, vmem],
        out_specs=(vmem, vmem),
        cost_estimate=pl.CostEstimate(
            flops=int(2 * n * kt * TILE * cols * 2 * heads),
            bytes_accessed=int(2 * 1024 * 1024),
            transcendentals=int(n * heads * kt * TILE),
        ),
    )(pos, cnt, q, ext)


def attention_tiles(near_out, pos, cnt, bias, q, do, ext, far, *near_stats):
    heads = bias.shape[0]
    kt = pos.shape[0] // cnt.shape[0]
    n, cols = q.shape
    smem = pl.BlockSpec(memory_space=pltpu.SMEM)
    vmem = pl.BlockSpec(memory_space=pltpu.VMEM)
    grads = jax.ShapeDtypeStruct(ext.shape if near_out else far.shape, jnp.float32)
    return pl.pallas_call(
        functools.partial(_attn_kernel, heads, kt, near_out),
        out_shape=(jax.ShapeDtypeStruct((n, cols), jnp.bfloat16), grads),
        in_specs=[smem, smem, smem] + [vmem] * (4 + len(near_stats)),
        out_specs=(vmem, vmem),
        scratch_shapes=[pltpu.VMEM((n, cols), jnp.float32)],
        cost_estimate=pl.CostEstimate(
            flops=int(2 * n * kt * TILE * cols * (6 if near_out else 3) * heads),
            bytes_accessed=int(4 * 1024 * 1024),
            transcendentals=int(n * heads * (kt * TILE + DEG)),
        ),
    )(pos, cnt, bias, q, do, ext, far, *near_stats)


def shards(
    query_rows,
    key_rows,
    value_rows,
    out_weight,
    out_grad,
    far_bias,
    tile_list,
    tile_count,
    send_rows,
    expander_slot,
):
    col_width = query_rows.shape[1]
    node_count = query_rows.shape[0]
    per_part = node_count // TILE
    dom_index = lax.axis_index("dom")
    full_grad = lax.all_gather(out_grad, "head", axis=1, tiled=True)
    attn_grad = lax.dot_general(
        full_grad, out_weight, (((1,), (1,)), ((), ())), preferred_element_type=jnp.float32
    ).astype(jnp.bfloat16)
    stacked = jnp.concatenate([key_rows, value_rows], axis=1)
    rim_rows = HALO * TILE
    extended = extended_2(stacked, (("dom", 0),), rim_rows)
    ext_tiles = extended.reshape(-1, TILE, 2 * col_width)
    send_hit = (
        send_rows[0].reshape(-1, 1) == jnp.arange(node_count, dtype=jnp.int32)[None, :]
    ).astype(jnp.bfloat16)
    outgoing = (
        jnp.dot(send_hit, stacked, preferred_element_type=jnp.float32)
        .astype(jnp.bfloat16)
        .reshape(send_rows.shape[1], send_rows.shape[2], -1)
    )
    received = lax.all_to_all(outgoing, "dom", split_axis=0, concat_axis=0, tiled=True)
    edge_slots = expander_slot.T.reshape(-1)
    n_recv = received.shape[0] * received.shape[1]
    far_hit = (
        edge_slots[:, None] == jnp.arange(n_recv, dtype=jnp.int32)[None, :]
    ).astype(jnp.bfloat16)
    far_all = (
        jnp.dot(far_hit, received.reshape(n_recv, -1), preferred_element_type=jnp.float32)
        .astype(jnp.bfloat16)
        .reshape(DEG, node_count, -1)
    )
    base_tile = dom_index * per_part - HALO
    kernel_args = (
        (tile_list - base_tile).reshape(-1),
        tile_count,
        far_bias,
        query_rows,
        attn_grad,
        ext_tiles,
        far_all,
    )
    near_mixed, near_stats = near_tiles(
        kernel_args[0], tile_count, query_rows, ext_tiles, far_bias.shape[0]
    )
    attn_all, far_grad = attention_tiles(False, *kernel_args, near_mixed, near_stats)
    qgrad_all, ext_grad = attention_tiles(True, *kernel_args)
    ext_grad = ext_grad.reshape(-1, 2 * col_width)
    attn_mine = attn_all.reshape(node_count, col_width)
    low_part = ext_grad[:rim_rows]
    high_part = ext_grad[rim_rows + node_count :]
    own_grad = ext_grad[rim_rows : rim_rows + node_count]
    from_next = from_behind(low_part.astype(jnp.bfloat16), "dom", -1).astype(low_part.dtype)
    from_prev = from_behind(high_part.astype(jnp.bfloat16), "dom", 1).astype(high_part.dtype)
    own_grad = own_grad.at[:rim_rows].add(from_prev).at[node_count - rim_rows :].add(from_next)
    n_dom, cap = received.shape[0], received.shape[1]
    pair_grad = far_grad.reshape(-1, 2 * col_width)
    pair_hi = lax.reduce_precision(pair_grad, exponent_bits=8, mantissa_bits=7)
    pair_lo = (pair_grad - pair_hi).astype(jnp.bfloat16)
    slot_hit = (
        edge_slots.reshape(1, -1) == jnp.arange(n_dom * cap, dtype=jnp.int32)[:, None]
    ).astype(jnp.bfloat16)
    slot_grad = jnp.dot(
        slot_hit, pair_hi.astype(jnp.bfloat16), preferred_element_type=jnp.float32
    ) + jnp.dot(slot_hit, pair_lo, preferred_element_type=jnp.float32)
    weight_part = lax.dot_general(
        full_grad, attn_mine, (((0,), (0,)), ((), ())), preferred_element_type=jnp.float32
    ).reshape(n_dom, -1, 2 * col_width)
    both = jnp.concatenate(
        [slot_grad.reshape(n_dom, cap, -1), weight_part], axis=1
    ).astype(jnp.bfloat16)
    both_back = lax.all_to_all(both, "dom", split_axis=0, concat_axis=0, tiled=True)
    returned = both_back[:, :cap].reshape(-1, 2 * col_width)
    weight_sum = jnp.sum(both_back[:, cap:].astype(jnp.float32), axis=0)
    row_hit = (
        send_rows[0].reshape(1, -1) == jnp.arange(node_count, dtype=jnp.int32)[:, None]
    ).astype(jnp.bfloat16)
    own_grad = own_grad + jnp.dot(row_hit, returned, preferred_element_type=jnp.float32)
    key_grad = own_grad[:, :col_width].astype(jnp.bfloat16)
    value_grad = own_grad[:, col_width:].astype(jnp.bfloat16)
    partial_out = jnp.dot(attn_mine, out_weight, preferred_element_type=jnp.float32)
    head_index = lax.axis_index("head")
    other_cols = lax.dynamic_slice_in_dim(partial_out, (1 - head_index) * col_width, col_width, 1)
    own_cols = lax.dynamic_slice_in_dim(partial_out, head_index * col_width, col_width, 1)
    swapped = lax.ppermute(other_cols, "head", [(0, 1), (1, 0)])
    layer_out = (own_cols + swapped).astype(jnp.bfloat16)
    out_weight_grad = weight_sum.reshape(-1, col_width)
    return (
        layer_out,
        qgrad_all.reshape(node_count, col_width),
        key_grad,
        value_grad,
        out_weight_grad,
    )


def solution(mesh):
    in_specs = (
        P("dom", "head"),
        P("dom", "head"),
        P("dom", "head"),
        P("head", None),
        P("dom", "head"),
        P("head"),
        P("dom", None),
        P("dom"),
        P("dom", None, None),
        P("dom", None),
    )
    out_specs = (
        P("dom", "head"),
        P("dom", "head"),
        P("dom", "head"),
        P("dom", "head"),
        P("dom", "head"),
    )
    return jax.shard_map(shards, mesh=mesh, in_specs=in_specs, out_specs=out_specs, check_vma=False)
```

```python
import functools

import jax
import jax.numpy as jnp
from jax import lax
from jax.experimental import pallas as pl
from jax.experimental.pallas import tpu as pltpu
from jax.sharding import PartitionSpec as P


TILE = 128
HALO = 2
DEG = 3


def extended_2(value, sides, width):
    for axis, dim in sides:
        peers, length = (lax.axis_size(axis), value.shape[dim])
        up = [(i, (i + 1) % peers) for i in range(peers - 1)]
        down = [(j, i) for i, j in up]
        last = lax.slice_in_dim(value, length - width, length, axis=dim)
        leading = lax.slice_in_dim(value, 0, width, axis=dim)
        before = lax.ppermute(last, axis, up)
        after = lax.ppermute(leading, axis, down)
        value = jnp.concatenate([before, value, after], axis=dim)
    return value


def from_behind(value, axis, steps):
    count = lax.axis_size(axis)
    leading, last = (max(0, -steps), min(count, count - steps))
    return lax.ppermute(value, axis, [(source, source + steps) for source in range(leading, last)])


def _attn_kernel(heads, kt, near_out, pos_ref, cnt_ref, bias_ref, q_ref, do_ref, ext_ref, far_ref, *refs):
    if near_out:
        qg_ref, eg_ref, acc = refs
    else:
        mx_ref, st_ref, attn_ref, fg_ref, acc = refs
    cols = q_ref.shape[1]
    hs = cols // heads
    scale = hs ** (-0.5)
    n_tiles = q_ref.shape[0] // TILE
    f32, bf16 = jnp.float32, jnp.bfloat16
    if near_out:
        eg_ref[...] = jnp.zeros(eg_ref.shape, f32)
    else:
        fg_ref[...] = jnp.zeros(fg_ref.shape, f32)
    acc[...] = jnp.zeros(acc.shape, f32)
    lane = lax.broadcasted_iota(jnp.int32, (TILE, cols), 1)
    nt = (((1,), (1,)), ((), ()))
    tn = (((0,), (0,)), ((), ()))
    for t in range(n_tiles):
        rows = pl.ds(t * TILE, TILE)
        count = cnt_ref[t]
        pos = [pos_ref[t * kt + j] for j in range(kt)]

        def head_body(h, carry):
            mask = (lane >= h * hs) & (lane < (h + 1) * hs)
            q = q_ref[rows, :]
            do = do_ref[rows, :]
            qf = q.astype(f32)
            dof = do.astype(f32)
            qh = jnp.where(mask, q, jnp.zeros_like(q))
            doh = jnp.where(mask, do, jnp.zeros_like(do))
            fk = [far_ref[e, rows, :cols].astype(f32) for e in range(DEG)]
            fv = [far_ref[e, rows, cols:].astype(f32) for e in range(DEG)]
            bias = bias_ref[h]
            fs = [jnp.sum(jnp.where(mask, qf * fk[e], 0.0), axis=1, keepdims=True) * scale + bias
                  for e in range(DEG)]
            if near_out:
                keys = [ext_ref[pos[j], :, :cols] for j in range(kt)]
                vals = [ext_ref[pos[j], :, cols:] for j in range(kt)]
                live = [j < count for j in range(kt)]
                s = [lax.dot_general(qh, keys[j], nt, preferred_element_type=f32) * scale for j in range(kt)]
                m = fs[0]
                for e in range(1, DEG):
                    m = jnp.maximum(m, fs[e])
                for j in range(kt):
                    m = jnp.maximum(m, jnp.where(live[j], jnp.max(s[j], axis=1, keepdims=True), -jnp.inf))
                ne = [jnp.where(live[j], jnp.exp(s[j] - m), 0.0) for j in range(kt)]
                fe = [jnp.exp(fs[e] - m) for e in range(DEG)]
                row_sum = fe[0] + fe[1] + fe[2]
                row_sum = jnp.sum(ne[0], axis=1, keepdims=True) + row_sum
                for j in range(1, kt):
                    row_sum = row_sum + jnp.sum(ne[j], axis=1, keepdims=True)
                mixed = jnp.dot(ne[0].astype(bf16), vals[0], preferred_element_type=f32)
                for j in range(1, kt):
                    mixed = mixed + jnp.dot(ne[j].astype(bf16), vals[j], preferred_element_type=f32)
            else:
                colh = lax.broadcasted_iota(jnp.int32, (TILE, TILE), 1) == h
                near_max = jnp.sum(jnp.where(colh, st_ref[0, rows, :], 0.0), axis=1, keepdims=True)
                near_total = jnp.sum(jnp.where(colh, st_ref[1, rows, :], 0.0), axis=1, keepdims=True)
                m = jnp.maximum(near_max, fs[0])
                for e in range(1, DEG):
                    m = jnp.maximum(m, fs[e])
                rescale = jnp.exp(near_max - m)
                fe = [jnp.exp(fs[e] - m) for e in range(DEG)]
                row_sum = near_total * rescale + (fe[0] + fe[1] + fe[2])
                mixed = mx_ref[rows, :] * rescale
            for e in range(DEG):
                mixed = mixed + fe[e].astype(bf16).astype(f32) * fv[e]
            attn = (mixed / row_sum).astype(bf16).astype(f32)
            delta = jnp.sum(jnp.where(mask, dof * attn, 0.0), axis=1, keepdims=True)
            if not near_out:
                acc[rows, :] += jnp.where(mask, attn, 0.0)
                for e in range(DEG):
                    fdp = jnp.sum(jnp.where(mask, dof * fv[e], 0.0), axis=1, keepdims=True)
                    fpr = fe[e] / row_sum
                    fds = (fpr * (fdp - delta)).astype(bf16).astype(f32)
                    fg_ref[e, rows, :cols] += jnp.where(mask, fds * qf * scale, 0.0)
                    fg_ref[e, rows, cols:] += jnp.where(mask, fpr.astype(bf16).astype(f32) * dof, 0.0)
                return carry
            qg = None
            for j in range(kt):
                ndp = lax.dot_general(doh, vals[j], nt, preferred_element_type=f32)
                npr = ne[j] / row_sum
                nds = (npr * (ndp - delta)).astype(bf16)
                part = jnp.dot(nds, keys[j], preferred_element_type=f32)
                qg = part if qg is None else qg + part
                kg = lax.dot_general(nds, qh, tn, preferred_element_type=f32) * scale
                vg = lax.dot_general(npr.astype(bf16), doh, tn, preferred_element_type=f32)
                eg_ref[pos[j], :, :cols] += kg
                eg_ref[pos[j], :, cols:] += vg
            for e in range(DEG):
                fdp = jnp.sum(jnp.where(mask, dof * fv[e], 0.0), axis=1, keepdims=True)
                fpr = fe[e] / row_sum
                fds = (fpr * (fdp - delta)).astype(bf16).astype(f32)
                qg = qg + fds * fk[e]
            acc[rows, :] += jnp.where(mask, qg * scale, 0.0)
            return carry

        lax.fori_loop(0, heads, head_body, 0)
        out_ref = qg_ref if near_out else attn_ref
        out_ref[rows, :] = acc[rows, :].astype(out_ref.dtype)


def _near_kernel(heads, kt, pos_ref, cnt_ref, q_ref, ext_ref, mx_ref, st_ref):
    cols = q_ref.shape[1]
    hs = cols // heads
    scale = hs ** (-0.5)
    n_tiles = q_ref.shape[0] // TILE
    f32, bf16 = jnp.float32, jnp.bfloat16
    mx_ref[...] = jnp.zeros(mx_ref.shape, f32)
    st_ref[...] = jnp.zeros(st_ref.shape, f32)
    lane = lax.broadcasted_iota(jnp.int32, (TILE, cols), 1)
    col = lax.broadcasted_iota(jnp.int32, (TILE, TILE), 1)
    nt = (((1,), (1,)), ((), ()))
    for t in range(n_tiles):
        rows = pl.ds(t * TILE, TILE)
        count = cnt_ref[t]
        pos = [pos_ref[t * kt + j] for j in range(kt)]

        def head_body(h, carry):
            mask = (lane >= h * hs) & (lane < (h + 1) * hs)
            q = q_ref[rows, :]
            qh = jnp.where(mask, q, jnp.zeros_like(q))
            keys = [ext_ref[pos[j], :, :cols] for j in range(kt)]
            vals = [ext_ref[pos[j], :, cols:] for j in range(kt)]
            live = [j < count for j in range(kt)]
            s = [lax.dot_general(qh, keys[j], nt, preferred_element_type=f32) * scale for j in range(kt)]
            m = jnp.max(s[0], axis=1, keepdims=True)
            for j in range(1, kt):
                m = jnp.maximum(m, jnp.where(live[j], jnp.max(s[j], axis=1, keepdims=True), -jnp.inf))
            ne = [jnp.where(live[j], jnp.exp(s[j] - m), 0.0) for j in range(kt)]
            total = jnp.sum(ne[0], axis=1, keepdims=True)
            for j in range(1, kt):
                total = total + jnp.sum(ne[j], axis=1, keepdims=True)
            mixed = jnp.dot(ne[0].astype(bf16), vals[0], preferred_element_type=f32)
            for j in range(1, kt):
                mixed = mixed + jnp.dot(ne[j].astype(bf16), vals[j], preferred_element_type=f32)
            mx_ref[rows, :] += jnp.where(mask, mixed, 0.0)
            st_ref[0, rows, :] = jnp.where(col == h, m, st_ref[0, rows, :])
            st_ref[1, rows, :] = jnp.where(col == h, total, st_ref[1, rows, :])
            return carry

        lax.fori_loop(0, heads, head_body, 0)


def near_tiles(pos, cnt, q, ext, heads):
    kt = pos.shape[0] // cnt.shape[0]
    n, cols = q.shape
    smem = pl.BlockSpec(memory_space=pltpu.SMEM)
    vmem = pl.BlockSpec(memory_space=pltpu.VMEM)
    return pl.pallas_call(
        functools.partial(_near_kernel, heads, kt),
        out_shape=(
            jax.ShapeDtypeStruct((n, cols), jnp.float32),
            jax.ShapeDtypeStruct((2, n, TILE), jnp.float32),
        ),
        in_specs=[smem, smem, vmem, vmem],
        out_specs=(vmem, vmem),
        cost_estimate=pl.CostEstimate(
            flops=int(2 * n * kt * TILE * cols * 2 * heads),
            bytes_accessed=int(2 * 1024 * 1024),
            transcendentals=int(n * heads * kt * TILE),
        ),
    )(pos, cnt, q, ext)


def attention_tiles(near_out, pos, cnt, bias, q, do, ext, far, *near_stats):
    heads = bias.shape[0]
    kt = pos.shape[0] // cnt.shape[0]
    n, cols = q.shape
    smem = pl.BlockSpec(memory_space=pltpu.SMEM)
    vmem = pl.BlockSpec(memory_space=pltpu.VMEM)
    grads = jax.ShapeDtypeStruct(ext.shape if near_out else far.shape, jnp.float32)
    return pl.pallas_call(
        functools.partial(_attn_kernel, heads, kt, near_out),
        out_shape=(jax.ShapeDtypeStruct((n, cols), jnp.bfloat16), grads),
        in_specs=[smem, smem, smem] + [vmem] * (4 + len(near_stats)),
        out_specs=(vmem, vmem),
        scratch_shapes=[pltpu.VMEM((n, cols), jnp.float32)],
        cost_estimate=pl.CostEstimate(
            flops=int(2 * n * kt * TILE * cols * (6 if near_out else 3) * heads),
            bytes_accessed=int(4 * 1024 * 1024),
            transcendentals=int(n * heads * (kt * TILE + DEG)),
        ),
    )(pos, cnt, bias, q, do, ext, far, *near_stats)


def shards(
    query_rows,
    key_rows,
    value_rows,
    out_weight,
    out_grad,
    far_bias,
    tile_list,
    tile_count,
    send_rows,
    expander_slot,
):
    col_width = query_rows.shape[1]
    node_count = query_rows.shape[0]
    per_part = node_count // TILE
    dom_index = lax.axis_index("dom")
    full_grad = lax.all_gather(out_grad, "head", axis=1, tiled=True)
    attn_grad = lax.dot_general(
        full_grad, out_weight, (((1,), (1,)), ((), ())), preferred_element_type=jnp.float32
    ).astype(jnp.bfloat16)
    stacked = jnp.concatenate([key_rows, value_rows], axis=1)
    rim_rows = HALO * TILE
    extended = extended_2(stacked, (("dom", 0),), rim_rows)
    ext_tiles = extended.reshape(-1, TILE, 2 * col_width)
    send_hit = (
        send_rows[0].reshape(-1, 1) == jnp.arange(node_count, dtype=jnp.int32)[None, :]
    ).astype(jnp.bfloat16)
    outgoing = (
        jnp.dot(send_hit, stacked, preferred_element_type=jnp.float32)
        .astype(jnp.bfloat16)
        .reshape(send_rows.shape[1], send_rows.shape[2], -1)
    )
    received = lax.all_to_all(outgoing, "dom", split_axis=0, concat_axis=0, tiled=True)
    edge_slots = expander_slot.T.reshape(-1)
    n_recv = received.shape[0] * received.shape[1]
    far_hit = (
        edge_slots[:, None] == jnp.arange(n_recv, dtype=jnp.int32)[None, :]
    ).astype(jnp.bfloat16)
    far_all = (
        jnp.dot(far_hit, received.reshape(n_recv, -1), preferred_element_type=jnp.float32)
        .astype(jnp.bfloat16)
        .reshape(DEG, node_count, -1)
    )
    base_tile = dom_index * per_part - HALO
    kernel_args = (
        (tile_list - base_tile).reshape(-1),
        tile_count,
        far_bias,
        query_rows,
        attn_grad,
        ext_tiles,
        far_all,
    )
    near_mixed, near_stats = near_tiles(
        kernel_args[0], tile_count, query_rows, ext_tiles, far_bias.shape[0]
    )
    attn_all, far_grad = attention_tiles(False, *kernel_args, near_mixed, near_stats)
    qgrad_all, ext_grad = attention_tiles(True, *kernel_args)
    ext_grad = ext_grad.reshape(-1, 2 * col_width)
    attn_mine = attn_all.reshape(node_count, col_width)
    low_part = ext_grad[:rim_rows]
    high_part = ext_grad[rim_rows + node_count :]
    own_grad = ext_grad[rim_rows : rim_rows + node_count]
    from_next = from_behind(low_part.astype(jnp.bfloat16), "dom", -1).astype(low_part.dtype)
    from_prev = from_behind(high_part.astype(jnp.bfloat16), "dom", 1).astype(high_part.dtype)
    own_grad = own_grad.at[:rim_rows].add(from_prev).at[node_count - rim_rows :].add(from_next)
    n_dom, cap = received.shape[0], received.shape[1]
    pair_grad = far_grad.reshape(-1, 2 * col_width)
    pair_hi = lax.reduce_precision(pair_grad, exponent_bits=8, mantissa_bits=7)
    pair_lo = (pair_grad - pair_hi).astype(jnp.bfloat16)
    slot_hit = (
        edge_slots.reshape(1, -1) == jnp.arange(n_dom * cap, dtype=jnp.int32)[:, None]
    ).astype(jnp.bfloat16)
    slot_grad = jnp.dot(
        slot_hit, pair_hi.astype(jnp.bfloat16), preferred_element_type=jnp.float32
    ) + jnp.dot(slot_hit, pair_lo, preferred_element_type=jnp.float32)
    weight_part = lax.dot_general(
        full_grad, attn_mine, (((0,), (0,)), ((), ())), preferred_element_type=jnp.float32
    ).reshape(n_dom, -1, 2 * col_width)
    both = jnp.concatenate(
        [slot_grad.reshape(n_dom, cap, -1), weight_part], axis=1
    ).astype(jnp.bfloat16)
    both_back = lax.all_to_all(both, "dom", split_axis=0, concat_axis=0, tiled=True)
    returned = both_back[:, :cap].reshape(-1, 2 * col_width)
    weight_sum = jnp.sum(both_back[:, cap:].astype(jnp.float32), axis=0)
    row_hit = (
        send_rows[0].reshape(1, -1) == jnp.arange(node_count, dtype=jnp.int32)[:, None]
    ).astype(jnp.bfloat16)
    own_grad = own_grad + jnp.dot(row_hit, returned, preferred_element_type=jnp.float32)
    key_grad = own_grad[:, :col_width].astype(jnp.bfloat16)
    value_grad = own_grad[:, col_width:].astype(jnp.bfloat16)
    partial_out = jnp.dot(attn_mine, out_weight, preferred_element_type=jnp.float32)
    head_index = lax.axis_index("head")
    other_cols = lax.dynamic_slice_in_dim(partial_out, (1 - head_index) * col_width, col_width, 1)
    own_cols = lax.dynamic_slice_in_dim(partial_out, head_index * col_width, col_width, 1)
    swapped = lax.ppermute(other_cols, "head", [(0, 1), (1, 0)])
    layer_out = (own_cols + swapped).astype(jnp.bfloat16)
    out_weight_grad = weight_sum.reshape(-1, col_width)
    return (
        layer_out,
        qgrad_all.reshape(node_count, col_width),
        key_grad,
        value_grad,
        out_weight_grad,
    )


def solution(mesh):
    in_specs = (
        P("dom", "head"),
        P("dom", "head"),
        P("dom", "head"),
        P("head", None),
        P("dom", "head"),
        P("head"),
        P("dom", None),
        P("dom"),
        P("dom", None, None),
        P("dom", None),
    )
    out_specs = (
        P("dom", "head"),
        P("dom", "head"),
        P("dom", "head"),
        P("dom", "head"),
        P("dom", "head"),
    )

    return jax.shard_map(shards, mesh=mesh, in_specs=in_specs, out_specs=out_specs, check_vma=False)
```

```python
import functools

import jax
import jax.numpy as jnp
from jax import lax
from jax.experimental import pallas as pl
from jax.experimental.pallas import tpu as pltpu
from jax.sharding import PartitionSpec as P


TILE = 128
HALO = 2
DEG = 3


def extended_2(value, sides, width):
    for axis, dim in sides:
        peers, length = (lax.axis_size(axis), value.shape[dim])
        up = [(i, (i + 1) % peers) for i in range(peers - 1)]
        down = [(j, i) for i, j in up]
        last = lax.slice_in_dim(value, length - width, length, axis=dim)
        leading = lax.slice_in_dim(value, 0, width, axis=dim)
        before = lax.ppermute(last, axis, up)
        after = lax.ppermute(leading, axis, down)
        value = jnp.concatenate([before, value, after], axis=dim)
    return value


def from_behind(value, axis, steps):
    count = lax.axis_size(axis)
    leading, last = (max(0, -steps), min(count, count - steps))
    return lax.ppermute(value, axis, [(source, source + steps) for source in range(leading, last)])


def _attn_kernel(heads, kt, near_out, pos_ref, cnt_ref, bias_ref, q_ref, do_ref, ext_ref, far_ref, *refs):
    if near_out:
        qg_ref, eg_ref, acc = refs
    else:
        mx_ref, st_ref, attn_ref, fg_ref, acc = refs
    cols = q_ref.shape[1]
    hs = cols // heads
    scale = hs ** (-0.5)
    n_tiles = q_ref.shape[0] // TILE
    f32, bf16 = jnp.float32, jnp.bfloat16
    if near_out:
        eg_ref[...] = jnp.zeros(eg_ref.shape, f32)
    else:
        fg_ref[...] = jnp.zeros(fg_ref.shape, f32)
    acc[...] = jnp.zeros(acc.shape, f32)
    lane = lax.broadcasted_iota(jnp.int32, (TILE, cols), 1)
    nt = (((1,), (1,)), ((), ()))
    tn = (((0,), (0,)), ((), ()))
    for t in range(n_tiles):
        rows = pl.ds(t * TILE, TILE)
        count = cnt_ref[t]
        pos = [pos_ref[t * kt + j] for j in range(kt)]

        def head_body(h, carry):
            mask = (lane >= h * hs) & (lane < (h + 1) * hs)
            q = q_ref[rows, :]
            do = do_ref[rows, :]
            qf = q.astype(f32)
            dof = do.astype(f32)
            qh = jnp.where(mask, q, jnp.zeros_like(q))
            doh = jnp.where(mask, do, jnp.zeros_like(do))
            fk = [far_ref[e, rows, :cols].astype(f32) for e in range(DEG)]
            fv = [far_ref[e, rows, cols:].astype(f32) for e in range(DEG)]
            bias = bias_ref[h]
            fs = [jnp.sum(jnp.where(mask, qf * fk[e], 0.0), axis=1, keepdims=True) * scale + bias
                  for e in range(DEG)]
            if near_out:
                keys = [ext_ref[pos[j], :, :cols] for j in range(kt)]
                vals = [ext_ref[pos[j], :, cols:] for j in range(kt)]
                live = [j < count for j in range(kt)]
                s = [lax.dot_general(qh, keys[j], nt, preferred_element_type=f32) * scale for j in range(kt)]
                m = fs[0]
                for e in range(1, DEG):
                    m = jnp.maximum(m, fs[e])
                for j in range(kt):
                    m = jnp.maximum(m, jnp.where(live[j], jnp.max(s[j], axis=1, keepdims=True), -jnp.inf))
                ne = [jnp.where(live[j], jnp.exp(s[j] - m), 0.0) for j in range(kt)]
                fe = [jnp.exp(fs[e] - m) for e in range(DEG)]
                row_sum = fe[0] + fe[1] + fe[2]
                row_sum = jnp.sum(ne[0], axis=1, keepdims=True) + row_sum
                for j in range(1, kt):
                    row_sum = row_sum + jnp.sum(ne[j], axis=1, keepdims=True)
                mixed = jnp.dot(ne[0].astype(bf16), vals[0], preferred_element_type=f32)
                for j in range(1, kt):
                    mixed = mixed + jnp.dot(ne[j].astype(bf16), vals[j], preferred_element_type=f32)
            else:
                colh = lax.broadcasted_iota(jnp.int32, (TILE, TILE), 1) == h
                near_max = jnp.sum(jnp.where(colh, st_ref[0, rows, :], 0.0), axis=1, keepdims=True)
                near_total = jnp.sum(jnp.where(colh, st_ref[1, rows, :], 0.0), axis=1, keepdims=True)
                m = jnp.maximum(near_max, fs[0])
                for e in range(1, DEG):
                    m = jnp.maximum(m, fs[e])
                rescale = jnp.exp(near_max - m)
                fe = [jnp.exp(fs[e] - m) for e in range(DEG)]
                row_sum = near_total * rescale + (fe[0] + fe[1] + fe[2])
                mixed = mx_ref[rows, :] * rescale
            for e in range(DEG):
                mixed = mixed + fe[e].astype(bf16).astype(f32) * fv[e]
            attn = (mixed / row_sum).astype(bf16).astype(f32)
            delta = jnp.sum(jnp.where(mask, dof * attn, 0.0), axis=1, keepdims=True)
            if not near_out:
                acc[rows, :] += jnp.where(mask, attn, 0.0)
                for e in range(DEG):
                    fdp = jnp.sum(jnp.where(mask, dof * fv[e], 0.0), axis=1, keepdims=True)
                    fpr = fe[e] / row_sum
                    fds = (fpr * (fdp - delta)).astype(bf16).astype(f32)
                    fg_ref[e, rows, :cols] += jnp.where(mask, fds * qf * scale, 0.0)
                    fg_ref[e, rows, cols:] += jnp.where(mask, fpr.astype(bf16).astype(f32) * dof, 0.0)
                return carry
            qg = None
            for j in range(kt):
                ndp = lax.dot_general(doh, vals[j], nt, preferred_element_type=f32)
                npr = ne[j] / row_sum
                nds = (npr * (ndp - delta)).astype(bf16)
                part = jnp.dot(nds, keys[j], preferred_element_type=f32)
                qg = part if qg is None else qg + part
                kg = lax.dot_general(nds, qh, tn, preferred_element_type=f32) * scale
                vg = lax.dot_general(npr.astype(bf16), doh, tn, preferred_element_type=f32)
                eg_ref[pos[j], :, :cols] += kg
                eg_ref[pos[j], :, cols:] += vg
            for e in range(DEG):
                fdp = jnp.sum(jnp.where(mask, dof * fv[e], 0.0), axis=1, keepdims=True)
                fpr = fe[e] / row_sum
                fds = (fpr * (fdp - delta)).astype(bf16).astype(f32)
                qg = qg + fds * fk[e]
            acc[rows, :] += jnp.where(mask, qg * scale, 0.0)
            return carry

        lax.fori_loop(0, heads, head_body, 0)
        out_ref = qg_ref if near_out else attn_ref
        out_ref[rows, :] = acc[rows, :].astype(out_ref.dtype)


def _near_kernel(heads, kt, pos_ref, cnt_ref, q_ref, ext_ref, mx_ref, st_ref):
    cols = q_ref.shape[1]
    hs = cols // heads
    scale = hs ** (-0.5)
    n_tiles = q_ref.shape[0] // TILE
    f32, bf16 = jnp.float32, jnp.bfloat16
    mx_ref[...] = jnp.zeros(mx_ref.shape, f32)
    st_ref[...] = jnp.zeros(st_ref.shape, f32)
    lane = lax.broadcasted_iota(jnp.int32, (TILE, cols), 1)
    col = lax.broadcasted_iota(jnp.int32, (TILE, TILE), 1)
    nt = (((1,), (1,)), ((), ()))
    for t in range(n_tiles):
        rows = pl.ds(t * TILE, TILE)
        count = cnt_ref[t]
        pos = [pos_ref[t * kt + j] for j in range(kt)]

        def head_body(h, carry):
            mask = (lane >= h * hs) & (lane < (h + 1) * hs)
            q = q_ref[rows, :]
            qh = jnp.where(mask, q, jnp.zeros_like(q))
            keys = [ext_ref[pos[j], :, :cols] for j in range(kt)]
            vals = [ext_ref[pos[j], :, cols:] for j in range(kt)]
            live = [j < count for j in range(kt)]
            s = [lax.dot_general(qh, keys[j], nt, preferred_element_type=f32) * scale for j in range(kt)]
            m = jnp.max(s[0], axis=1, keepdims=True)
            for j in range(1, kt):
                m = jnp.maximum(m, jnp.where(live[j], jnp.max(s[j], axis=1, keepdims=True), -jnp.inf))
            ne = [jnp.where(live[j], jnp.exp(s[j] - m), 0.0) for j in range(kt)]
            total = jnp.sum(ne[0], axis=1, keepdims=True)
            for j in range(1, kt):
                total = total + jnp.sum(ne[j], axis=1, keepdims=True)
            mixed = jnp.dot(ne[0].astype(bf16), vals[0], preferred_element_type=f32)
            for j in range(1, kt):
                mixed = mixed + jnp.dot(ne[j].astype(bf16), vals[j], preferred_element_type=f32)
            mx_ref[rows, :] += jnp.where(mask, mixed, 0.0)
            st_ref[0, rows, :] = jnp.where(col == h, m, st_ref[0, rows, :])
            st_ref[1, rows, :] = jnp.where(col == h, total, st_ref[1, rows, :])
            return carry

        lax.fori_loop(0, heads, head_body, 0)


def near_tiles(pos, cnt, q, ext, heads):
    kt = pos.shape[0] // cnt.shape[0]
    n, cols = q.shape
    smem = pl.BlockSpec(memory_space=pltpu.SMEM)
    vmem = pl.BlockSpec(memory_space=pltpu.VMEM)
    return pl.pallas_call(
        functools.partial(_near_kernel, heads, kt),
        out_shape=(
            jax.ShapeDtypeStruct((n, cols), jnp.float32),
            jax.ShapeDtypeStruct((2, n, TILE), jnp.float32),
        ),
        in_specs=[smem, smem, vmem, vmem],
        out_specs=(vmem, vmem),
        cost_estimate=pl.CostEstimate(
            flops=int(2 * n * kt * TILE * cols * 2 * heads),
            bytes_accessed=int(2 * 1024 * 1024),
            transcendentals=int(n * heads * kt * TILE),
        ),
    )(pos, cnt, q, ext)


def attention_tiles(near_out, pos, cnt, bias, q, do, ext, far, *near_stats):
    heads = bias.shape[0]
    kt = pos.shape[0] // cnt.shape[0]
    n, cols = q.shape
    smem = pl.BlockSpec(memory_space=pltpu.SMEM)
    vmem = pl.BlockSpec(memory_space=pltpu.VMEM)
    grads = jax.ShapeDtypeStruct(ext.shape if near_out else far.shape, jnp.float32)
    return pl.pallas_call(
        functools.partial(_attn_kernel, heads, kt, near_out),
        out_shape=(jax.ShapeDtypeStruct((n, cols), jnp.bfloat16), grads),
        in_specs=[smem, smem, smem] + [vmem] * (4 + len(near_stats)),
        out_specs=(vmem, vmem),
        scratch_shapes=[pltpu.VMEM((n, cols), jnp.float32)],
        cost_estimate=pl.CostEstimate(
            flops=int(2 * n * kt * TILE * cols * (6 if near_out else 3) * heads),
            bytes_accessed=int(4 * 1024 * 1024),
            transcendentals=int(n * heads * (kt * TILE + DEG)),
        ),
    )(pos, cnt, bias, q, do, ext, far, *near_stats)


def shards(
    query_rows,
    key_rows,
    value_rows,
    out_weight,
    out_grad,
    far_bias,
    tile_list,
    tile_count,
    send_rows,
    expander_slot,
):
    col_width = query_rows.shape[1]
    node_count = query_rows.shape[0]
    per_part = node_count // TILE
    dom_index = lax.axis_index("dom")
    full_grad = lax.all_gather(out_grad, "head", axis=1, tiled=True)
    attn_grad = lax.dot_general(
        full_grad, out_weight, (((1,), (1,)), ((), ())), preferred_element_type=jnp.float32
    ).astype(jnp.bfloat16)
    stacked = jnp.concatenate([key_rows, value_rows], axis=1)
    rim_rows = HALO * TILE
    extended = extended_2(stacked, (("dom", 0),), rim_rows)
    ext_tiles = extended.reshape(-1, TILE, 2 * col_width)
    send_hit = (
        send_rows[0].reshape(-1, 1) == jnp.arange(node_count, dtype=jnp.int32)[None, :]
    ).astype(jnp.bfloat16)
    outgoing = (
        jnp.dot(send_hit, stacked, preferred_element_type=jnp.float32)
        .astype(jnp.bfloat16)
        .reshape(send_rows.shape[1], send_rows.shape[2], -1)
    )
    received = lax.all_to_all(outgoing, "dom", split_axis=0, concat_axis=0, tiled=True)
    edge_slots = expander_slot.T.reshape(-1)
    n_recv = received.shape[0] * received.shape[1]
    far_hit = (
        edge_slots[:, None] == jnp.arange(n_recv, dtype=jnp.int32)[None, :]
    ).astype(jnp.bfloat16)
    far_all = (
        jnp.dot(far_hit, received.reshape(n_recv, -1), preferred_element_type=jnp.float32)
        .astype(jnp.bfloat16)
        .reshape(DEG, node_count, -1)
    )
    base_tile = dom_index * per_part - HALO
    kernel_args = (
        (tile_list - base_tile).reshape(-1),
        tile_count,
        far_bias,
        query_rows,
        attn_grad,
        ext_tiles,
        far_all,
    )
    near_mixed, near_stats = near_tiles(
        kernel_args[0], tile_count, query_rows, ext_tiles, far_bias.shape[0]
    )
    attn_all, far_grad = attention_tiles(False, *kernel_args, near_mixed, near_stats)
    qgrad_all, ext_grad = attention_tiles(True, *kernel_args)
    ext_grad = ext_grad.reshape(-1, 2 * col_width)
    attn_mine = attn_all.reshape(node_count, col_width)
    low_part = ext_grad[:rim_rows]
    high_part = ext_grad[rim_rows + node_count :]
    own_grad = ext_grad[rim_rows : rim_rows + node_count]
    from_next = from_behind(low_part.astype(jnp.bfloat16), "dom", -1).astype(low_part.dtype)
    from_prev = from_behind(high_part.astype(jnp.bfloat16), "dom", 1).astype(high_part.dtype)
    own_grad = own_grad.at[:rim_rows].add(from_prev).at[node_count - rim_rows :].add(from_next)
    n_dom, cap = received.shape[0], received.shape[1]
    pair_grad = far_grad.reshape(-1, 2 * col_width)
    slot_hit = (
        edge_slots.reshape(1, -1) == jnp.arange(n_dom * cap, dtype=jnp.int32)[:, None]
    ).astype(jnp.bfloat16)
    slot_grad = jnp.dot(
        slot_hit, pair_grad.astype(jnp.bfloat16), preferred_element_type=jnp.float32
    )
    weight_part = lax.dot_general(
        full_grad, attn_mine, (((0,), (0,)), ((), ())), preferred_element_type=jnp.float32
    ).reshape(n_dom, -1, 2 * col_width)
    both = jnp.concatenate(
        [slot_grad.reshape(n_dom, cap, -1), weight_part], axis=1
    ).astype(jnp.bfloat16)
    both_back = lax.all_to_all(both, "dom", split_axis=0, concat_axis=0, tiled=True)
    returned = both_back[:, :cap].reshape(-1, 2 * col_width)
    weight_sum = jnp.sum(both_back[:, cap:].astype(jnp.float32), axis=0)
    row_hit = (
        send_rows[0].reshape(1, -1) == jnp.arange(node_count, dtype=jnp.int32)[:, None]
    ).astype(jnp.bfloat16)
    own_grad = own_grad + jnp.dot(row_hit, returned, preferred_element_type=jnp.float32)
    key_grad = own_grad[:, :col_width].astype(jnp.bfloat16)
    value_grad = own_grad[:, col_width:].astype(jnp.bfloat16)
    partial_out = jnp.dot(attn_mine, out_weight, preferred_element_type=jnp.float32)
    head_index = lax.axis_index("head")
    other_cols = lax.dynamic_slice_in_dim(partial_out, (1 - head_index) * col_width, col_width, 1)
    own_cols = lax.dynamic_slice_in_dim(partial_out, head_index * col_width, col_width, 1)
    swapped = lax.ppermute(other_cols, "head", [(0, 1), (1, 0)])
    layer_out = (own_cols + swapped).astype(jnp.bfloat16)
    out_weight_grad = weight_sum.reshape(-1, col_width)
    return (
        layer_out,
        qgrad_all.reshape(node_count, col_width),
        key_grad,
        value_grad,
        out_weight_grad,
    )


def solution(mesh):
    in_specs = (
        P("dom", "head"),
        P("dom", "head"),
        P("dom", "head"),
        P("head", None),
        P("dom", "head"),
        P("head"),
        P("dom", None),
        P("dom"),
        P("dom", None, None),
        P("dom", None),
    )
    out_specs = (
        P("dom", "head"),
        P("dom", "head"),
        P("dom", "head"),
        P("dom", "head"),
        P("dom", "head"),
    )

    return jax.shard_map(shards, mesh=mesh, in_specs=in_specs, out_specs=out_specs, check_vma=False)
```

```python
import functools

import jax
import jax.numpy as jnp
from jax import lax
from jax.experimental import pallas as pl
from jax.experimental.pallas import tpu as pltpu
from jax.sharding import PartitionSpec as P


TILE = 128
HALO = 2
DEG = 3


def extended_2(value, sides, width):
    for axis, dim in sides:
        peers, length = (lax.axis_size(axis), value.shape[dim])
        up = [(i, (i + 1) % peers) for i in range(peers - 1)]
        down = [(j, i) for i, j in up]
        last = lax.slice_in_dim(value, length - width, length, axis=dim)
        leading = lax.slice_in_dim(value, 0, width, axis=dim)
        before = lax.ppermute(last, axis, up)
        after = lax.ppermute(leading, axis, down)
        value = jnp.concatenate([before, value, after], axis=dim)
    return value


def from_behind(value, axis, steps):
    count = lax.axis_size(axis)
    leading, last = (max(0, -steps), min(count, count - steps))
    return lax.ppermute(value, axis, [(source, source + steps) for source in range(leading, last)])


def _attn_kernel(heads, kt, near_out, pos_ref, cnt_ref, bias_ref, q_ref, do_ref, ext_ref, far_ref, *refs):
    if near_out:
        qg_ref, eg_ref, acc = refs
    else:
        mx_ref, st_ref, attn_ref, fg_ref, acc = refs
    cols = q_ref.shape[1]
    hs = cols // heads
    scale = hs ** (-0.5)
    n_tiles = q_ref.shape[0] // TILE
    f32, bf16 = jnp.float32, jnp.bfloat16
    if near_out:
        eg_ref[...] = jnp.zeros(eg_ref.shape, f32)
    else:
        fg_ref[...] = jnp.zeros(fg_ref.shape, f32)
    acc[...] = jnp.zeros(acc.shape, f32)
    lane = lax.broadcasted_iota(jnp.int32, (TILE, cols), 1)
    nt = (((1,), (1,)), ((), ()))
    tn = (((0,), (0,)), ((), ()))
    for t in range(n_tiles):
        rows = pl.ds(t * TILE, TILE)
        count = cnt_ref[t]
        pos = [pos_ref[t * kt + j] for j in range(kt)]

        def head_body(h, carry):
            mask = (lane >= h * hs) & (lane < (h + 1) * hs)
            q = q_ref[rows, :]
            do = do_ref[rows, :]
            qf = q.astype(f32)
            dof = do.astype(f32)
            qh = jnp.where(mask, q, jnp.zeros_like(q))
            doh = jnp.where(mask, do, jnp.zeros_like(do))
            fk = [far_ref[e, rows, :cols].astype(f32) for e in range(DEG)]
            fv = [far_ref[e, rows, cols:].astype(f32) for e in range(DEG)]
            bias = bias_ref[h]
            fs = [jnp.sum(jnp.where(mask, qf * fk[e], 0.0), axis=1, keepdims=True) * scale + bias
                  for e in range(DEG)]
            if near_out:
                keys = [ext_ref[pos[j], :, :cols] for j in range(kt)]
                vals = [ext_ref[pos[j], :, cols:] for j in range(kt)]
                live = [j < count for j in range(kt)]
                s = [lax.dot_general(qh, keys[j], nt, preferred_element_type=f32) * scale for j in range(kt)]
                m = fs[0]
                for e in range(1, DEG):
                    m = jnp.maximum(m, fs[e])
                for j in range(kt):
                    m = jnp.maximum(m, jnp.where(live[j], jnp.max(s[j], axis=1, keepdims=True), -jnp.inf))
                ne = [jnp.where(live[j], jnp.exp(s[j] - m), 0.0) for j in range(kt)]
                fe = [jnp.exp(fs[e] - m) for e in range(DEG)]
                row_sum = fe[0] + fe[1] + fe[2]
                row_sum = jnp.sum(ne[0], axis=1, keepdims=True) + row_sum
                for j in range(1, kt):
                    row_sum = row_sum + jnp.sum(ne[j], axis=1, keepdims=True)
                mixed = jnp.dot(ne[0].astype(bf16), vals[0], preferred_element_type=f32)
                for j in range(1, kt):
                    mixed = mixed + jnp.dot(ne[j].astype(bf16), vals[j], preferred_element_type=f32)
            else:
                colh = lax.broadcasted_iota(jnp.int32, (TILE, TILE), 1) == h
                near_max = jnp.sum(jnp.where(colh, st_ref[0, rows, :], 0.0), axis=1, keepdims=True)
                near_total = jnp.sum(jnp.where(colh, st_ref[1, rows, :], 0.0), axis=1, keepdims=True)
                m = jnp.maximum(near_max, fs[0])
                for e in range(1, DEG):
                    m = jnp.maximum(m, fs[e])
                rescale = jnp.exp(near_max - m)
                fe = [jnp.exp(fs[e] - m) for e in range(DEG)]
                row_sum = near_total * rescale + (fe[0] + fe[1] + fe[2])
                mixed = mx_ref[rows, :] * rescale
            for e in range(DEG):
                mixed = mixed + fe[e].astype(bf16).astype(f32) * fv[e]
            attn = (mixed / row_sum).astype(bf16).astype(f32)
            delta = jnp.sum(jnp.where(mask, dof * attn, 0.0), axis=1, keepdims=True)
            if not near_out:
                acc[rows, :] += jnp.where(mask, attn, 0.0)
                for e in range(DEG):
                    fdp = jnp.sum(jnp.where(mask, dof * fv[e], 0.0), axis=1, keepdims=True)
                    fpr = fe[e] / row_sum
                    fds = (fpr * (fdp - delta)).astype(bf16).astype(f32)
                    fg_ref[e, rows, :cols] += jnp.where(mask, fds * qf * scale, 0.0)
                    fg_ref[e, rows, cols:] += jnp.where(mask, fpr.astype(bf16).astype(f32) * dof, 0.0)
                return carry
            qg = None
            for j in range(kt):
                ndp = lax.dot_general(doh, vals[j], nt, preferred_element_type=f32)
                npr = ne[j] / row_sum
                nds = (npr * (ndp - delta)).astype(bf16)
                part = jnp.dot(nds, keys[j], preferred_element_type=f32)
                qg = part if qg is None else qg + part
                kg = lax.dot_general(nds, qh, tn, preferred_element_type=f32) * scale
                vg = lax.dot_general(npr.astype(bf16), doh, tn, preferred_element_type=f32)
                eg_ref[pos[j], :, :cols] += kg
                eg_ref[pos[j], :, cols:] += vg
            for e in range(DEG):
                fdp = jnp.sum(jnp.where(mask, dof * fv[e], 0.0), axis=1, keepdims=True)
                fpr = fe[e] / row_sum
                fds = (fpr * (fdp - delta)).astype(bf16).astype(f32)
                qg = qg + fds * fk[e]
            acc[rows, :] += jnp.where(mask, qg * scale, 0.0)
            return carry

        lax.fori_loop(0, heads, head_body, 0)
        out_ref = qg_ref if near_out else attn_ref
        out_ref[rows, :] = acc[rows, :].astype(out_ref.dtype)


def _near_kernel(heads, kt, pos_ref, cnt_ref, q_ref, ext_ref, mx_ref, st_ref):
    cols = q_ref.shape[1]
    hs = cols // heads
    scale = hs ** (-0.5)
    n_tiles = q_ref.shape[0] // TILE
    f32, bf16 = jnp.float32, jnp.bfloat16
    mx_ref[...] = jnp.zeros(mx_ref.shape, f32)
    st_ref[...] = jnp.zeros(st_ref.shape, f32)
    lane = lax.broadcasted_iota(jnp.int32, (TILE, cols), 1)
    col = lax.broadcasted_iota(jnp.int32, (TILE, TILE), 1)
    nt = (((1,), (1,)), ((), ()))
    for t in range(n_tiles):
        rows = pl.ds(t * TILE, TILE)
        count = cnt_ref[t]
        pos = [pos_ref[t * kt + j] for j in range(kt)]

        def head_body(h, carry):
            mask = (lane >= h * hs) & (lane < (h + 1) * hs)
            q = q_ref[rows, :]
            qh = jnp.where(mask, q, jnp.zeros_like(q))
            keys = [ext_ref[pos[j], :, :cols] for j in range(kt)]
            vals = [ext_ref[pos[j], :, cols:] for j in range(kt)]
            live = [j < count for j in range(kt)]
            s = [lax.dot_general(qh, keys[j], nt, preferred_element_type=f32) * scale for j in range(kt)]
            m = jnp.max(s[0], axis=1, keepdims=True)
            for j in range(1, kt):
                m = jnp.maximum(m, jnp.where(live[j], jnp.max(s[j], axis=1, keepdims=True), -jnp.inf))
            ne = [jnp.where(live[j], jnp.exp(s[j] - m), 0.0) for j in range(kt)]
            total = jnp.sum(ne[0], axis=1, keepdims=True)
            for j in range(1, kt):
                total = total + jnp.sum(ne[j], axis=1, keepdims=True)
            mixed = jnp.dot(ne[0].astype(bf16), vals[0], preferred_element_type=f32)
            for j in range(1, kt):
                mixed = mixed + jnp.dot(ne[j].astype(bf16), vals[j], preferred_element_type=f32)
            mx_ref[rows, :] += jnp.where(mask, mixed, 0.0)
            st_ref[0, rows, :] = jnp.where(col == h, m, st_ref[0, rows, :])
            st_ref[1, rows, :] = jnp.where(col == h, total, st_ref[1, rows, :])
            return carry

        lax.fori_loop(0, heads, head_body, 0)


def near_tiles(pos, cnt, q, ext, heads):
    kt = pos.shape[0] // cnt.shape[0]
    n, cols = q.shape
    smem = pl.BlockSpec(memory_space=pltpu.SMEM)
    vmem = pl.BlockSpec(memory_space=pltpu.VMEM)
    return pl.pallas_call(
        functools.partial(_near_kernel, heads, kt),
        out_shape=(
            jax.ShapeDtypeStruct((n, cols), jnp.float32),
            jax.ShapeDtypeStruct((2, n, TILE), jnp.float32),
        ),
        in_specs=[smem, smem, vmem, vmem],
        out_specs=(vmem, vmem),
        cost_estimate=pl.CostEstimate(
            flops=int(2 * n * kt * TILE * cols * 2 * heads),
            bytes_accessed=int(2 * 1024 * 1024),
            transcendentals=int(n * heads * kt * TILE),
        ),
    )(pos, cnt, q, ext)


def attention_tiles(near_out, pos, cnt, bias, q, do, ext, far, *near_stats):
    heads = bias.shape[0]
    kt = pos.shape[0] // cnt.shape[0]
    n, cols = q.shape
    smem = pl.BlockSpec(memory_space=pltpu.SMEM)
    vmem = pl.BlockSpec(memory_space=pltpu.VMEM)
    grads = jax.ShapeDtypeStruct(ext.shape if near_out else far.shape, jnp.float32)
    return pl.pallas_call(
        functools.partial(_attn_kernel, heads, kt, near_out),
        out_shape=(jax.ShapeDtypeStruct((n, cols), jnp.bfloat16), grads),
        in_specs=[smem, smem, smem] + [vmem] * (4 + len(near_stats)),
        out_specs=(vmem, vmem),
        scratch_shapes=[pltpu.VMEM((n, cols), jnp.float32)],
        cost_estimate=pl.CostEstimate(
            flops=int(2 * n * kt * TILE * cols * (6 if near_out else 3) * heads),
            bytes_accessed=int(4 * 1024 * 1024),
            transcendentals=int(n * heads * (kt * TILE + DEG)),
        ),
    )(pos, cnt, bias, q, do, ext, far, *near_stats)


def shards(
    query_rows,
    key_rows,
    value_rows,
    out_weight,
    out_grad,
    far_bias,
    tile_list,
    tile_count,
    send_rows,
    expander_slot,
):
    col_width = query_rows.shape[1]
    node_count = query_rows.shape[0]
    per_part = node_count // TILE
    dom_index = lax.axis_index("dom")
    full_grad = lax.all_gather(out_grad, "head", axis=1, tiled=True)
    attn_grad = lax.dot_general(
        full_grad, out_weight, (((1,), (1,)), ((), ())), preferred_element_type=jnp.float32
    ).astype(jnp.bfloat16)
    stacked = jnp.concatenate([key_rows, value_rows], axis=1)
    rim_rows = HALO * TILE
    extended = extended_2(stacked, (("dom", 0),), rim_rows)
    ext_tiles = extended.reshape(-1, TILE, 2 * col_width)
    send_hit = (
        send_rows[0].reshape(-1, 1) == jnp.arange(node_count, dtype=jnp.int32)[None, :]
    ).astype(jnp.bfloat16)
    outgoing = (
        jnp.dot(send_hit, stacked, preferred_element_type=jnp.float32)
        .astype(jnp.bfloat16)
        .reshape(send_rows.shape[1], send_rows.shape[2], -1)
    )
    received = lax.all_to_all(outgoing, "dom", split_axis=0, concat_axis=0, tiled=True)
    edge_slots = expander_slot.T.reshape(-1)
    n_recv = received.shape[0] * received.shape[1]
    far_hit = (
        edge_slots[:, None] == jnp.arange(n_recv, dtype=jnp.int32)[None, :]
    ).astype(jnp.bfloat16)
    far_all = (
        jnp.dot(far_hit, received.reshape(n_recv, -1), preferred_element_type=jnp.float32)
        .astype(jnp.bfloat16)
        .reshape(DEG, node_count, -1)
    )
    base_tile = dom_index * per_part - HALO
    kernel_args = (
        (tile_list - base_tile).reshape(-1),
        tile_count,
        far_bias,
        query_rows,
        attn_grad,
        ext_tiles,
        far_all,
    )
    near_mixed, near_stats = near_tiles(
        kernel_args[0], tile_count, query_rows, ext_tiles, far_bias.shape[0]
    )
    attn_all, far_grad = attention_tiles(False, *kernel_args, near_mixed, near_stats)
    qgrad_all, ext_grad = attention_tiles(True, *kernel_args)
    ext_grad = ext_grad.reshape(-1, 2 * col_width)
    attn_mine = attn_all.reshape(node_count, col_width)
    low_part = ext_grad[:rim_rows]
    high_part = ext_grad[rim_rows + node_count :]
    own_grad = ext_grad[rim_rows : rim_rows + node_count]
    from_next = from_behind(low_part.astype(jnp.bfloat16), "dom", -1).astype(low_part.dtype)
    from_prev = from_behind(high_part.astype(jnp.bfloat16), "dom", 1).astype(high_part.dtype)
    own_grad = own_grad.at[:rim_rows].add(from_prev).at[node_count - rim_rows :].add(from_next)
    n_dom, cap = received.shape[0], received.shape[1]
    pair_grad = far_grad.reshape(-1, 2 * col_width)
    pair_hi = lax.reduce_precision(pair_grad, exponent_bits=8, mantissa_bits=7)
    pair_lo = (pair_grad - pair_hi).astype(jnp.bfloat16)
    slot_hit = (
        edge_slots.reshape(1, -1) == jnp.arange(n_dom * cap, dtype=jnp.int32)[:, None]
    ).astype(jnp.bfloat16)
    slot_grad = jnp.dot(
        slot_hit, pair_hi.astype(jnp.bfloat16), preferred_element_type=jnp.float32
    ) + jnp.dot(slot_hit, pair_lo, preferred_element_type=jnp.float32)
    weight_part = lax.dot_general(
        full_grad, attn_mine, (((0,), (0,)), ((), ())), preferred_element_type=jnp.float32
    ).reshape(n_dom, -1, 2 * col_width)
    both = jnp.concatenate(
        [slot_grad.reshape(n_dom, cap, -1), weight_part], axis=1
    ).astype(jnp.bfloat16)
    both_back = lax.all_to_all(both, "dom", split_axis=0, concat_axis=0, tiled=True)
    weight_sum = jnp.sum(both_back[:, cap:].astype(jnp.float32), axis=0)
    row_hit = (
        jnp.pad(send_rows[0], ((0, 0), (0, both_back.shape[1] - cap)), constant_values=-1)[None]
        == jnp.arange(node_count, dtype=jnp.int32)[:, None, None]
    ).astype(jnp.bfloat16)
    own_grad = own_grad + lax.dot_general(
        row_hit, both_back, (((1, 2), (0, 1)), ((), ())), preferred_element_type=jnp.float32
    )
    key_grad = own_grad[:, :col_width].astype(jnp.bfloat16)
    value_grad = own_grad[:, col_width:].astype(jnp.bfloat16)
    partial_out = jnp.dot(attn_mine, out_weight, preferred_element_type=jnp.float32)
    head_index = lax.axis_index("head")
    other_cols = lax.dynamic_slice_in_dim(partial_out, (1 - head_index) * col_width, col_width, 1)
    own_cols = lax.dynamic_slice_in_dim(partial_out, head_index * col_width, col_width, 1)
    swapped = lax.ppermute(other_cols, "head", [(0, 1), (1, 0)])
    layer_out = (own_cols + swapped).astype(jnp.bfloat16)
    out_weight_grad = weight_sum.reshape(-1, col_width)
    return (
        layer_out,
        qgrad_all.reshape(node_count, col_width),
        key_grad,
        value_grad,
        out_weight_grad,
    )


def solution(mesh):
    in_specs = (
        P("dom", "head"),
        P("dom", "head"),
        P("dom", "head"),
        P("head", None),
        P("dom", "head"),
        P("head"),
        P("dom", None),
        P("dom"),
        P("dom", None, None),
        P("dom", None),
    )
    out_specs = (
        P("dom", "head"),
        P("dom", "head"),
        P("dom", "head"),
        P("dom", "head"),
        P("dom", "head"),
    )

    return jax.shard_map(shards, mesh=mesh, in_specs=in_specs, out_specs=out_specs, check_vma=False)
```

```python
import functools

import jax
import jax.numpy as jnp
from jax import lax
from jax.experimental import pallas as pl
from jax.experimental.pallas import tpu as pltpu
from jax.sharding import PartitionSpec as P


TILE = 128
HALO = 2
DEG = 3


def extended_2(value, sides, width):
    for axis, dim in sides:
        peers, length = (lax.axis_size(axis), value.shape[dim])
        up = [(i, (i + 1) % peers) for i in range(peers - 1)]
        down = [(j, i) for i, j in up]
        last = lax.slice_in_dim(value, length - width, length, axis=dim)
        leading = lax.slice_in_dim(value, 0, width, axis=dim)
        before = lax.ppermute(last, axis, up)
        after = lax.ppermute(leading, axis, down)
        value = jnp.concatenate([before, value, after], axis=dim)
    return value


def from_behind(value, axis, steps):
    count = lax.axis_size(axis)
    leading, last = (max(0, -steps), min(count, count - steps))
    return lax.ppermute(value, axis, [(source, source + steps) for source in range(leading, last)])


def _attn_kernel(heads, kt, near_out, pos_ref, cnt_ref, bias_ref, q_ref, do_ref, ext_ref, far_ref, *refs):
    if near_out:
        qg_ref, eg_ref, acc = refs
    else:
        mx_ref, st_ref, attn_ref, fg_ref, acc = refs
    cols = q_ref.shape[1]
    hs = cols // heads
    scale = hs ** (-0.5)
    n_tiles = q_ref.shape[0] // TILE
    f32, bf16 = jnp.float32, jnp.bfloat16
    if near_out:
        eg_ref[...] = jnp.zeros(eg_ref.shape, f32)
    else:
        fg_ref[...] = jnp.zeros(fg_ref.shape, f32)
    acc[...] = jnp.zeros(acc.shape, f32)
    lane = lax.broadcasted_iota(jnp.int32, (TILE, cols), 1)
    nt = (((1,), (1,)), ((), ()))
    tn = (((0,), (0,)), ((), ()))
    for t in range(n_tiles):
        rows = pl.ds(t * TILE, TILE)
        count = cnt_ref[t]
        pos = [pos_ref[t * kt + j] for j in range(kt)]

        q = q_ref[rows, :]
        do = do_ref[rows, :]
        qf = q.astype(f32)
        dof = do.astype(f32)
        fk = [far_ref[e, rows, :cols].astype(f32) for e in range(DEG)]
        fv = [far_ref[e, rows, cols:].astype(f32) for e in range(DEG)]
        pk = [qf * fk[e] for e in range(DEG)]
        pv = [dof * fv[e] for e in range(DEG)]

        def head_body(h, carry):
            mask = (lane >= h * hs) & (lane < (h + 1) * hs)
            qh = jnp.where(mask, q, jnp.zeros_like(q))
            doh = jnp.where(mask, do, jnp.zeros_like(do))
            bias = bias_ref[h]
            fs = [jnp.sum(jnp.where(mask, pk[e], 0.0), axis=1, keepdims=True) * scale + bias
                  for e in range(DEG)]
            if near_out:
                keys = [ext_ref[pos[j], :, :cols] for j in range(kt)]
                vals = [ext_ref[pos[j], :, cols:] for j in range(kt)]
                live = [j < count for j in range(kt)]
                s = [lax.dot_general(qh, keys[j], nt, preferred_element_type=f32) * scale for j in range(kt)]
                m = fs[0]
                for e in range(1, DEG):
                    m = jnp.maximum(m, fs[e])
                for j in range(kt):
                    m = jnp.maximum(m, jnp.where(live[j], jnp.max(s[j], axis=1, keepdims=True), -jnp.inf))
                ne = [jnp.where(live[j], jnp.exp(s[j] - m), 0.0) for j in range(kt)]
                fe = [jnp.exp(fs[e] - m) for e in range(DEG)]
                row_sum = fe[0] + fe[1] + fe[2]
                row_sum = jnp.sum(ne[0], axis=1, keepdims=True) + row_sum
                for j in range(1, kt):
                    row_sum = row_sum + jnp.sum(ne[j], axis=1, keepdims=True)
                mixed = jnp.dot(ne[0].astype(bf16), vals[0], preferred_element_type=f32)
                for j in range(1, kt):
                    mixed = mixed + jnp.dot(ne[j].astype(bf16), vals[j], preferred_element_type=f32)
            else:
                colh = lax.broadcasted_iota(jnp.int32, (TILE, TILE), 1) == h
                near_max = jnp.sum(jnp.where(colh, st_ref[0, rows, :], 0.0), axis=1, keepdims=True)
                near_total = jnp.sum(jnp.where(colh, st_ref[1, rows, :], 0.0), axis=1, keepdims=True)
                m = jnp.maximum(near_max, fs[0])
                for e in range(1, DEG):
                    m = jnp.maximum(m, fs[e])
                rescale = jnp.exp(near_max - m)
                fe = [jnp.exp(fs[e] - m) for e in range(DEG)]
                row_sum = near_total * rescale + (fe[0] + fe[1] + fe[2])
                mixed = mx_ref[rows, :] * rescale
            for e in range(DEG):
                mixed = mixed + fe[e].astype(bf16).astype(f32) * fv[e]
            attn = (mixed / row_sum).astype(bf16).astype(f32)
            delta = jnp.sum(jnp.where(mask, dof * attn, 0.0), axis=1, keepdims=True)
            if not near_out:
                acc[rows, :] += jnp.where(mask, attn, 0.0)
                for e in range(DEG):
                    fdp = jnp.sum(jnp.where(mask, pv[e], 0.0), axis=1, keepdims=True)
                    fpr = fe[e] / row_sum
                    fds = (fpr * (fdp - delta)).astype(bf16).astype(f32)
                    fg_ref[e, rows, :cols] += jnp.where(mask, fds * qf * scale, 0.0)
                    fg_ref[e, rows, cols:] += jnp.where(mask, fpr.astype(bf16).astype(f32) * dof, 0.0)
                return carry
            qg = None
            for j in range(kt):
                ndp = lax.dot_general(doh, vals[j], nt, preferred_element_type=f32)
                npr = ne[j] / row_sum
                nds = (npr * (ndp - delta)).astype(bf16)
                part = jnp.dot(nds, keys[j], preferred_element_type=f32)
                qg = part if qg is None else qg + part
                kg = lax.dot_general(nds, qh, tn, preferred_element_type=f32) * scale
                vg = lax.dot_general(npr.astype(bf16), doh, tn, preferred_element_type=f32)
                eg_ref[pos[j], :, :cols] += kg
                eg_ref[pos[j], :, cols:] += vg
            for e in range(DEG):
                fdp = jnp.sum(jnp.where(mask, pv[e], 0.0), axis=1, keepdims=True)
                fpr = fe[e] / row_sum
                fds = (fpr * (fdp - delta)).astype(bf16).astype(f32)
                qg = qg + fds * fk[e]
            acc[rows, :] += jnp.where(mask, qg * scale, 0.0)
            return carry

        lax.fori_loop(0, heads, head_body, 0)
        out_ref = qg_ref if near_out else attn_ref
        out_ref[rows, :] = acc[rows, :].astype(out_ref.dtype)


def _near_kernel(heads, kt, pos_ref, cnt_ref, q_ref, ext_ref, mx_ref, st_ref):
    cols = q_ref.shape[1]
    hs = cols // heads
    scale = hs ** (-0.5)
    n_tiles = q_ref.shape[0] // TILE
    f32, bf16 = jnp.float32, jnp.bfloat16
    mx_ref[...] = jnp.zeros(mx_ref.shape, f32)
    st_ref[...] = jnp.zeros(st_ref.shape, f32)
    lane = lax.broadcasted_iota(jnp.int32, (TILE, cols), 1)
    col = lax.broadcasted_iota(jnp.int32, (TILE, TILE), 1)
    nt = (((1,), (1,)), ((), ()))
    for t in range(n_tiles):
        rows = pl.ds(t * TILE, TILE)
        count = cnt_ref[t]
        pos = [pos_ref[t * kt + j] for j in range(kt)]

        def head_body(h, carry):
            mask = (lane >= h * hs) & (lane < (h + 1) * hs)
            q = q_ref[rows, :]
            qh = jnp.where(mask, q, jnp.zeros_like(q))
            keys = [ext_ref[pos[j], :, :cols] for j in range(kt)]
            vals = [ext_ref[pos[j], :, cols:] for j in range(kt)]
            live = [j < count for j in range(kt)]
            s = [lax.dot_general(qh, keys[j], nt, preferred_element_type=f32) * scale for j in range(kt)]
            m = jnp.max(s[0], axis=1, keepdims=True)
            for j in range(1, kt):
                m = jnp.maximum(m, jnp.where(live[j], jnp.max(s[j], axis=1, keepdims=True), -jnp.inf))
            ne = [jnp.where(live[j], jnp.exp(s[j] - m), 0.0) for j in range(kt)]
            total = jnp.sum(ne[0], axis=1, keepdims=True)
            for j in range(1, kt):
                total = total + jnp.sum(ne[j], axis=1, keepdims=True)
            mixed = jnp.dot(ne[0].astype(bf16), vals[0], preferred_element_type=f32)
            for j in range(1, kt):
                mixed = mixed + jnp.dot(ne[j].astype(bf16), vals[j], preferred_element_type=f32)
            mx_ref[rows, :] += jnp.where(mask, mixed, 0.0)
            st_ref[0, rows, :] = jnp.where(col == h, m, st_ref[0, rows, :])
            st_ref[1, rows, :] = jnp.where(col == h, total, st_ref[1, rows, :])
            return carry

        lax.fori_loop(0, heads, head_body, 0)


def near_tiles(pos, cnt, q, ext, heads):
    kt = pos.shape[0] // cnt.shape[0]
    n, cols = q.shape
    smem = pl.BlockSpec(memory_space=pltpu.SMEM)
    vmem = pl.BlockSpec(memory_space=pltpu.VMEM)
    return pl.pallas_call(
        functools.partial(_near_kernel, heads, kt),
        out_shape=(
            jax.ShapeDtypeStruct((n, cols), jnp.float32),
            jax.ShapeDtypeStruct((2, n, TILE), jnp.float32),
        ),
        in_specs=[smem, smem, vmem, vmem],
        out_specs=(vmem, vmem),
        cost_estimate=pl.CostEstimate(
            flops=int(2 * n * kt * TILE * cols * 2 * heads),
            bytes_accessed=int(2 * 1024 * 1024),
            transcendentals=int(n * heads * kt * TILE),
        ),
    )(pos, cnt, q, ext)


def attention_tiles(near_out, pos, cnt, bias, q, do, ext, far, *near_stats):
    heads = bias.shape[0]
    kt = pos.shape[0] // cnt.shape[0]
    n, cols = q.shape
    smem = pl.BlockSpec(memory_space=pltpu.SMEM)
    vmem = pl.BlockSpec(memory_space=pltpu.VMEM)
    grads = jax.ShapeDtypeStruct(ext.shape if near_out else far.shape, jnp.float32)
    return pl.pallas_call(
        functools.partial(_attn_kernel, heads, kt, near_out),
        out_shape=(jax.ShapeDtypeStruct((n, cols), jnp.bfloat16), grads),
        in_specs=[smem, smem, smem] + [vmem] * (4 + len(near_stats)),
        out_specs=(vmem, vmem),
        scratch_shapes=[pltpu.VMEM((n, cols), jnp.float32)],
        cost_estimate=pl.CostEstimate(
            flops=int(2 * n * kt * TILE * cols * (6 if near_out else 3) * heads),
            bytes_accessed=int(4 * 1024 * 1024),
            transcendentals=int(n * heads * (kt * TILE + DEG)),
        ),
    )(pos, cnt, bias, q, do, ext, far, *near_stats)


def shards(
    query_rows,
    key_rows,
    value_rows,
    out_weight,
    out_grad,
    far_bias,
    tile_list,
    tile_count,
    send_rows,
    expander_slot,
):
    col_width = query_rows.shape[1]
    node_count = query_rows.shape[0]
    per_part = node_count // TILE
    dom_index = lax.axis_index("dom")
    full_grad = lax.all_gather(out_grad, "head", axis=1, tiled=True)
    attn_grad = lax.dot_general(
        full_grad, out_weight, (((1,), (1,)), ((), ())), preferred_element_type=jnp.float32
    ).astype(jnp.bfloat16)
    stacked = jnp.concatenate([key_rows, value_rows], axis=1)
    rim_rows = HALO * TILE
    extended = extended_2(stacked, (("dom", 0),), rim_rows)
    ext_tiles = extended.reshape(-1, TILE, 2 * col_width)
    send_hit = (
        send_rows[0].reshape(-1, 1) == jnp.arange(node_count, dtype=jnp.int32)[None, :]
    ).astype(jnp.bfloat16)
    outgoing = (
        jnp.dot(send_hit, stacked, preferred_element_type=jnp.float32)
        .astype(jnp.bfloat16)
        .reshape(send_rows.shape[1], send_rows.shape[2], -1)
    )
    received = lax.all_to_all(outgoing, "dom", split_axis=0, concat_axis=0, tiled=True)
    edge_slots = expander_slot.T.reshape(-1)
    n_recv = received.shape[0] * received.shape[1]
    far_hit = (
        edge_slots[:, None] == jnp.arange(n_recv, dtype=jnp.int32)[None, :]
    ).astype(jnp.bfloat16)
    far_all = (
        jnp.dot(far_hit, received.reshape(n_recv, -1), preferred_element_type=jnp.float32)
        .astype(jnp.bfloat16)
        .reshape(DEG, node_count, -1)
    )
    base_tile = dom_index * per_part - HALO
    kernel_args = (
        (tile_list - base_tile).reshape(-1),
        tile_count,
        far_bias,
        query_rows,
        attn_grad,
        ext_tiles,
        far_all,
    )
    near_mixed, near_stats = near_tiles(
        kernel_args[0], tile_count, query_rows, ext_tiles, far_bias.shape[0]
    )
    attn_all, far_grad = attention_tiles(False, *kernel_args, near_mixed, near_stats)
    qgrad_all, ext_grad = attention_tiles(True, *kernel_args)
    ext_grad = ext_grad.reshape(-1, 2 * col_width)
    attn_mine = attn_all.reshape(node_count, col_width)
    low_part = ext_grad[:rim_rows]
    high_part = ext_grad[rim_rows + node_count :]
    own_grad = ext_grad[rim_rows : rim_rows + node_count]
    from_next = from_behind(low_part.astype(jnp.bfloat16), "dom", -1).astype(low_part.dtype)
    from_prev = from_behind(high_part.astype(jnp.bfloat16), "dom", 1).astype(high_part.dtype)
    own_grad = own_grad.at[:rim_rows].add(from_prev).at[node_count - rim_rows :].add(from_next)
    n_dom, cap = received.shape[0], received.shape[1]
    pair_grad = far_grad.reshape(-1, 2 * col_width)
    pair_hi = lax.reduce_precision(pair_grad, exponent_bits=8, mantissa_bits=7)
    pair_lo = (pair_grad - pair_hi).astype(jnp.bfloat16)
    slot_hit = (
        edge_slots.reshape(1, -1) == jnp.arange(n_dom * cap, dtype=jnp.int32)[:, None]
    ).astype(jnp.bfloat16)
    slot_grad = jnp.dot(
        slot_hit, pair_hi.astype(jnp.bfloat16), preferred_element_type=jnp.float32
    ) + jnp.dot(slot_hit, pair_lo, preferred_element_type=jnp.float32)
    weight_part = lax.dot_general(
        full_grad, attn_mine, (((0,), (0,)), ((), ())), preferred_element_type=jnp.float32
    ).reshape(n_dom, -1, 2 * col_width)
    both = jnp.concatenate(
        [slot_grad.reshape(n_dom, cap, -1), weight_part], axis=1
    ).astype(jnp.bfloat16)
    both_back = lax.all_to_all(both, "dom", split_axis=0, concat_axis=0, tiled=True)
    returned = both_back[:, :cap].reshape(-1, 2 * col_width)
    weight_sum = jnp.sum(both_back[:, cap:].astype(jnp.float32), axis=0)
    row_hit = (
        send_rows[0].reshape(1, -1) == jnp.arange(node_count, dtype=jnp.int32)[:, None]
    ).astype(jnp.bfloat16)
    own_grad = own_grad + jnp.dot(row_hit, returned, preferred_element_type=jnp.float32)
    key_grad = own_grad[:, :col_width].astype(jnp.bfloat16)
    value_grad = own_grad[:, col_width:].astype(jnp.bfloat16)
    partial_out = jnp.dot(attn_mine, out_weight, preferred_element_type=jnp.float32)
    head_index = lax.axis_index("head")
    other_cols = lax.dynamic_slice_in_dim(partial_out, (1 - head_index) * col_width, col_width, 1)
    own_cols = lax.dynamic_slice_in_dim(partial_out, head_index * col_width, col_width, 1)
    swapped = lax.ppermute(other_cols, "head", [(0, 1), (1, 0)])
    layer_out = (own_cols + swapped).astype(jnp.bfloat16)
    out_weight_grad = weight_sum.reshape(-1, col_width)
    return (
        layer_out,
        qgrad_all.reshape(node_count, col_width),
        key_grad,
        value_grad,
        out_weight_grad,
    )


def solution(mesh):
    in_specs = (
        P("dom", "head"),
        P("dom", "head"),
        P("dom", "head"),
        P("head", None),
        P("dom", "head"),
        P("head"),
        P("dom", None),
        P("dom"),
        P("dom", None, None),
        P("dom", None),
    )
    out_specs = (
        P("dom", "head"),
        P("dom", "head"),
        P("dom", "head"),
        P("dom", "head"),
        P("dom", "head"),
    )

    return jax.shard_map(shards, mesh=mesh, in_specs=in_specs, out_specs=out_specs, check_vma=False)
```
